32 devices in a mesh: gx: 8 (over z, x), gy: 4 (over y, core).
Axes of the slice: x: 2, y: 2, z: 4, core: 2. Of those that a mesh axis runs over, the one named last changes fastest.
Arguments:
- patches: bfloat16 [128, 64, 256], P('gx', 'gy'), may hold values from -9 to 9
- w_query: bfloat16 [256, 256], replicated, may hold values from -2 to 2
- w_key: bfloat16 [256, 256], replicated, may hold values from -2 to 2
- w_value: bfloat16 [256, 256], replicated, may hold values from -0.375 to 0.375
- w_out: bfloat16 [256, 256], replicated, may hold values from -0.375 to 0.375
- region_memory: bfloat16 [8, 4, 4, 64, 512], P('gx', 'gy'), may hold values from -6 to 6
- region_owner: int32 [8, 4, 4, 2], P('gx', 'gy'), may hold values from 0 to 7, all different within a row; in each aligned block of 4 rows (0 to 3, 4 to 7, ..., all dimensions but the last counted through in order) at most 2 rows name the same one
- region_local: int32 [8, 4, 4, 2], P('gx', 'gy'), may hold values from 0 to 3
- grad_out: bfloat16 [128, 64, 256], P('gx', 'gy'), may hold values from -6 to 6
Outputs:
- layer_out: bfloat16 [128, 64, 256], P('gx', 'gy')
- grad_patches: bfloat16 [128, 64, 256], P('gx', 'gy')
- grad_w_query: float32 [256, 256], replicated
- grad_w_key: float32 [256, 256], replicated
- grad_w_value: float32 [256, 256], replicated
- grad_w_out: float32 [256, 256], replicated
The draws below stay inside these ranges and needn't reach their ends.
Inputs may be any that keep to these rules, and one draw needn't show every extreme that they name: `region_owner`: each block names two different owner tiles. The blocks of one tile name one owner at most 2 times, a bound that some tile reaches.
All inputs are finite; a program needn't handle non-finite values.
Results may differ from the reference program's by a relative error of at most 0.02.
Values may be sent and summed in bfloat16 or wider, within the bound.
No kernel may reach another device: no remote copies, remote signals or barrier semaphores. Data moves between devices by JAX's collectives and lax.ppermute only.
A program may use at most 64 MiB of HBM per device.

```python
import math
import jax
import jax.numpy as jnp
import numpy as np
from jax import lax

D = 256
HEADS = 2
HEAD_DIM = 128
BSIDE = 8
BT = 64
REG_DEV = 4
BLK = 2
NB = 4
CAP = 2
PATCH_ROWS = 128
PATCH_COLS = 64
N_GX = 8
N_GY = 4


def draw_patches(key, part):
    normal_part = jax.random.normal(jax.random.fold_in(key, 11), (PATCH_ROWS, PATCH_COLS, D), jnp.float32)
    return jnp.clip(normal_part, -6.0, 6.0).astype(jnp.bfloat16)


def weight_parts(key):
    query_part = jnp.clip(jax.random.normal(jax.random.fold_in(key, 22), (D, D), jnp.float32), -6.0, 6.0)
    key_part = jnp.clip(jax.random.normal(jax.random.fold_in(key, 23), (D, D), jnp.float32), -6.0, 6.0)
    return (query_part, key_part)


def draw_w_query(key, part):
    query_part, key_part = weight_parts(key)
    return (query_part / math.sqrt(D)).astype(jnp.bfloat16)


def draw_w_key(key, part):
    query_part, key_part = weight_parts(key)
    return (key_part / math.sqrt(D)).astype(jnp.bfloat16)


def plant(entries, key, smallest, top_value):
    longest = entries.shape.index(max(entries.shape))
    spots = []
    for shift in (0, 1):
        where = [jax.random.randint(jax.random.fold_in(key, axis), (), 0, length) for axis, length in enumerate(entries.shape)]
        where[longest] = (where[longest] + shift) % entries.shape[longest]
        spots.append(tuple(where))
    return entries.at[spots[0]].set(smallest).at[spots[1]].set(top_value)


def block_levels(stream_key, extent, cuts, least, high):
    level = 1.0
    for position, parts in cuts:
        heights = jax.random.uniform(jax.random.fold_in(jax.random.fold_in(stream_key, 6), position), (parts,), jnp.float32, least / len(cuts), high / len(cuts))
        level = level * jnp.repeat(jnp.exp(heights), extent[position] // parts).reshape((-1,) + (1,) * (len(extent) - 1 - position))
    return level


def routed_block(rng, own, number, rows, amount, top, bound, lean):
    ranking = jax.random.permutation(rng, amount)
    heavy_load, ordinary = shares(amount, rows * top, bound, lean, True), shares(amount, rows * top, bound, lean, False)
    places = jnp.arange(amount)

    def named(tallies, offset_by):
        used = int((tallies > 0).sum())
        fixed = max(1, used // 4)
        passed = fixed + (places - fixed + offset_by * (used - fixed)) % max(1, amount - fixed)
        return jnp.zeros((amount,), jnp.int32).at[ranking[jnp.where(places < fixed, places, passed)]].set(jnp.asarray(tallies, jnp.int32))

    tallies = jnp.where(number % 4 == 0, named(heavy_load, number // 4), named(ordinary, number - number // 4 - 1))
    mixed = jax.random.permutation(jax.random.fold_in(own, 3), amount)
    giver, receiver = mixed[0:amount // 2 * 2:2], mixed[1:amount // 2 * 2:2]
    slack = jnp.minimum(tallies[giver] - 1, bound - tallies[receiver]) // 2
    slack = jnp.where((giver == ranking[0]) | (receiver == ranking[0]) | (tallies[receiver] == 0), 0, jnp.maximum(slack, 0))
    passed = jax.random.randint(jax.random.fold_in(own, 4), (amount // 2,), 0, 1 << 20) % (slack + 1)
    tallies = tallies.at[giver].add(-passed).at[receiver].add(passed)
    items = jnp.searchsorted(jnp.cumsum(tallies), jnp.arange(rows * top), side="right").astype(jnp.int32)
    grid = items.reshape(top, rows).T
    grid = grid[jax.random.permutation(jax.random.fold_in(own, 1), rows)]
    offset_by = jax.random.randint(jax.random.fold_in(own, 2), (rows, 1), 0, top)
    return jnp.take_along_axis(grid, (jnp.arange(top)[None, :] + offset_by) % top, axis=1)


def shares(amount, total, limit, lean, full):
    weights = [(1 << 20) // math.isqrt(rank ** lean) + 1 for rank in range(1, amount + 1)]
    largest = limit if full else min(limit, max(-(-total // amount), total * weights[0] // sum(weights)))
    least = 1 if total - largest >= amount - 1 else 0
    counts, rest = [largest] + [least] * (amount - 1), total - largest - least * (amount - 1)
    while rest > 0:
        free = [i for i in range(1, amount) if counts[i] < largest] or [i for i in range(1, amount) if counts[i] < limit]
        pool, remaining = sum([weights[i] for i in free]), rest
        for i in free:
            extra = min(limit - counts[i], max(1, remaining * weights[i] // pool), rest)
            counts[i] = counts[i] + extra
            rest = rest - extra
    return np.array(counts)


def centred(key, dims, scale, most, cuts=(), kind=jnp.bfloat16):
    loudness = block_levels(key, dims, cuts, -0.22, 0.18) if cuts else 1.0
    entries = jax.random.normal(key, dims, jnp.float32) * scale * loudness
    return jnp.minimum(jnp.maximum(entries, -most), most).astype(kind)


def setup_inputs(seed: int = 0) -> dict:
    key_of = jax.random.split(jax.random.key(seed), 10)
    patches = draw_patches(jax.random.fold_in(key_of[9], 71), 0)
    w_query = draw_w_query(jax.random.fold_in(key_of[9], 71), 0)
    w_key = draw_w_key(jax.random.fold_in(key_of[9], 71), 0)
    w_value = centred(key_of[3], (D, D), D ** -0.5, 0.375)
    w_out = centred(key_of[4], (D, D), D ** -0.5, 0.375)
    region_memory = centred(key_of[5], (N_GX, N_GY, REG_DEV, BT, 2 * D), 1.0, 6.0, ((0, 8), (1, 4)))
    region_owner_keys = jax.random.split(jax.random.fold_in(key_of[6], 1), N_GX * N_GY * NB // NB)
    region_owner_turns = jax.random.permutation(jax.random.fold_in(key_of[6], 3), N_GX * N_GY * NB // NB)
    region_owner = jax.vmap(lambda own, number: routed_block(jax.random.fold_in(key_of[6], 2), own, number, NB, N_GX, 2, CAP, 2))(region_owner_keys, region_owner_turns).reshape((N_GX, N_GY, NB, 2))
    region_local = plant(jax.random.randint(key_of[7], (N_GX, N_GY, NB, 2), 0, REG_DEV), jax.random.fold_in(key_of[7], 1), 0, REG_DEV - 1).astype(jnp.int32)
    grad_out = centred(key_of[8], (PATCH_ROWS, PATCH_COLS, D), 1.0, 6.0, ((0, 8), (1, 4)))
    return dict(patches=patches, w_query=w_query, w_key=w_key, w_value=w_value, w_out=w_out, region_memory=region_memory, region_owner=region_owner, region_local=region_local, grad_out=grad_out)


masked_score = -1000000000.0

def to_blocks(grid_array):
    grid_rows, grid_cols, feature_width = grid_array.shape
    shaped = grid_array.reshape(grid_rows // BSIDE, BSIDE, grid_cols // BSIDE, BSIDE, feature_width)
    return shaped.transpose(0, 2, 1, 3, 4).reshape(grid_rows // BSIDE, grid_cols // BSIDE, BSIDE * BSIDE, feature_width)

def from_blocks(block_array):
    block_rows, block_cols, block_tokens, feature_width = block_array.shape
    shaped = block_array.reshape(block_rows, block_cols, BSIDE, BSIDE, feature_width)
    return shaped.transpose(0, 2, 1, 3, 4).reshape(block_rows * BSIDE, block_cols * BSIDE, feature_width)

def split_heads(source):
    return source.reshape(source.shape[:-1] + (HEADS, source.shape[-1] // HEADS)).astype(jnp.float32)

def key_pieces(keyval_pad, key_valid, region_keyval):
    block_rows, block_cols = (region_keyval.shape[0], region_keyval.shape[1])
    pieces = []
    for row_off in range(3):
        for col_off in range(3):
            key_block = keyval_pad[row_off:row_off + block_rows, col_off:col_off + block_cols]
            valid_mask = key_valid[row_off:row_off + block_rows, col_off:col_off + block_cols]
            pieces.append((key_block[..., :D], key_block[..., D:], valid_mask))
    merged = region_keyval.reshape(block_rows, block_cols, 2 * BT, 2 * D)
    pieces.append((merged[..., :D], merged[..., D:], jnp.ones((block_rows, block_cols), dtype=jnp.bool_)))
    return pieces

def piece_scores(query_heads, key_part, valid_mask):
    scores = jnp.einsum('abqhe,abkhe->abhqk', query_heads, split_heads(key_part)) * (1.0 / math.sqrt(HEAD_DIM))
    return jnp.where(valid_mask[:, :, None, None, None], scores, masked_score)

def attend_forward(query_blocks, keyval_pad, key_valid, region_keyval):
    query_heads = split_heads(query_blocks)
    pieces = key_pieces(keyval_pad, key_valid, region_keyval)
    scores = [piece_scores(query_heads, key_part, valid_mask) for key_part, value_part, valid_mask in pieces]
    row_top = lax.optimization_barrier(jnp.max(jnp.concatenate(scores, -1), -1, keepdims=True))
    row_total = sum((lax.optimization_barrier(jnp.sum(jnp.exp(part_scores - row_top), -1, keepdims=True)) for part_scores in scores))
    log_total = row_top + jnp.log(row_total)
    mixed_sum = jnp.zeros(query_heads.shape, jnp.float32)
    for part_scores, (key_part, value_part, valid_mask) in zip(scores, pieces):
        weights = jnp.exp(part_scores - log_total).astype(jnp.bfloat16)
        mixed_sum = mixed_sum + jnp.einsum('abhqk,abkhe->abqhe', weights.astype(jnp.float32), split_heads(value_part))
    output = mixed_sum.reshape(query_blocks.shape).astype(jnp.bfloat16)
    return (output, log_total[..., 0])

def query_grads(query_blocks, keyval_pad, key_valid, region_keyval, log_total, dout_blocks, delta_rows):
    query_heads = split_heads(query_blocks)
    dout_heads = split_heads(dout_blocks)
    accum_sum = jnp.zeros(query_heads.shape, jnp.float32)
    for key_part, value_part, valid_mask in key_pieces(keyval_pad, key_valid, region_keyval):
        part_scores = piece_scores(query_heads, key_part, valid_mask)
        prob_part = jnp.exp(part_scores - log_total[..., None])
        grad_prob = jnp.einsum('abqhe,abkhe->abhqk', dout_heads, split_heads(value_part))
        grad_score = (prob_part * (grad_prob - delta_rows[..., None])).astype(jnp.bfloat16)
        accum_sum = accum_sum + jnp.einsum('abhqk,abkhe->abqhe', grad_score.astype(jnp.float32), split_heads(key_part))
    return (accum_sum * (1.0 / math.sqrt(HEAD_DIM))).reshape(query_blocks.shape).astype(jnp.bfloat16)

def key_grads(keyval_center, query_pad, dout_pad, log_pad, delta_pad, query_valid):
    block_rows, block_cols = (keyval_center.shape[0], keyval_center.shape[1])
    key_heads = split_heads(keyval_center[..., :D])
    value_heads = split_heads(keyval_center[..., D:])
    grad_key = jnp.zeros(key_heads.shape, jnp.float32)
    grad_value = jnp.zeros(key_heads.shape, jnp.float32)
    for row_off in range(3):
        for col_off in range(3):
            query_heads = split_heads(query_pad[row_off:row_off + block_rows, col_off:col_off + block_cols])
            dout_heads = split_heads(dout_pad[row_off:row_off + block_rows, col_off:col_off + block_cols])
            log_part = log_pad[row_off:row_off + block_rows, col_off:col_off + block_cols]
            delta_part = delta_pad[row_off:row_off + block_rows, col_off:col_off + block_cols]
            valid_mask = query_valid[row_off:row_off + block_rows, col_off:col_off + block_cols]
            part_scores = jnp.einsum('abqhe,abkhe->abhqk', query_heads, key_heads) * (1.0 / math.sqrt(HEAD_DIM))
            prob_part = jnp.where(valid_mask[:, :, None, None, None], jnp.exp(part_scores - log_part[..., None]), 0.0)
            grad_prob = jnp.einsum('abqhe,abkhe->abhqk', dout_heads, value_heads)
            grad_score = (prob_part * (grad_prob - delta_part[..., None])).astype(jnp.bfloat16)
            grad_key = grad_key + jnp.einsum('abhqk,abqhe->abkhe', grad_score.astype(jnp.float32), query_heads)
            rounded_prob = prob_part.astype(jnp.bfloat16).astype(jnp.float32)
            grad_value = grad_value + jnp.einsum('abhqk,abqhe->abkhe', rounded_prob, dout_heads)
    out_shape = (block_rows, block_cols, BT, D)
    grad_key = (grad_key * (1.0 / math.sqrt(HEAD_DIM))).reshape(out_shape).astype(jnp.bfloat16)
    return (grad_key, grad_value.reshape(out_shape).astype(jnp.bfloat16))

def reference(patches, w_query, w_key, w_value, w_out, region_memory, region_owner, region_local, grad_out):
    flat_in = patches.reshape(-1, D)
    queries = jnp.dot(flat_in, w_query, preferred_element_type=jnp.float32).astype(jnp.bfloat16)
    keys = jnp.dot(flat_in, w_key, preferred_element_type=jnp.float32).astype(jnp.bfloat16)
    values = jnp.dot(flat_in, w_value, preferred_element_type=jnp.float32).astype(jnp.bfloat16)
    keyvals = jnp.concatenate([keys, values], 1)
    query_blocks = to_blocks(queries.reshape(PATCH_ROWS, PATCH_COLS, D))
    keyval_blocks = to_blocks(keyvals.reshape(PATCH_ROWS, PATCH_COLS, 2 * D))
    grid_rows, grid_cols = (query_blocks.shape[0], query_blocks.shape[1])
    block_pad = ((1, 1), (1, 1), (0, 0), (0, 0))
    keyval_pad = jnp.pad(keyval_blocks, block_pad)
    key_valid = jnp.pad(jnp.ones((grid_rows, grid_cols), dtype=jnp.bool_), 1)
    owner_grid = region_owner.reshape(N_GX, N_GY, BLK, BLK, 2).transpose(0, 2, 1, 3, 4).reshape(grid_rows, grid_cols, 2)
    local_grid = region_local.reshape(N_GX, N_GY, BLK, BLK, 2).transpose(0, 2, 1, 3, 4).reshape(grid_rows, grid_cols, 2)
    column_dev = (jnp.arange(grid_cols, dtype=jnp.int32) // BLK).astype(jnp.int32)

    def region_row(row_index):
        return region_memory[owner_grid[row_index], column_dev[:, None], local_grid[row_index]][None]

    def forward_row(row_index):
        center = lax.dynamic_slice_in_dim(keyval_pad, row_index, 3, 0)
        valid_mask = lax.dynamic_slice_in_dim(key_valid, row_index, 3, 0)
        query_row = lax.dynamic_slice_in_dim(query_blocks, row_index, 1, 0)
        out_row, log_row = attend_forward(query_row, center, valid_mask, region_row(row_index))
        return (out_row[0], log_row[0])
    row_ids = jnp.arange(grid_rows, dtype=jnp.int32)
    outputs, log_totals = lax.map(forward_row, row_ids)
    attended = from_blocks(outputs).reshape(-1, D)
    layer_out = jnp.dot(attended, w_out, preferred_element_type=jnp.float32).astype(jnp.bfloat16)
    grad_flat = grad_out.reshape(-1, D)
    d_attended = jnp.dot(grad_flat, w_out.T, preferred_element_type=jnp.float32).astype(jnp.bfloat16)
    grad_w_out = jnp.dot(attended.T, grad_flat, preferred_element_type=jnp.float32)
    dout_blocks = to_blocks(d_attended.reshape(PATCH_ROWS, PATCH_COLS, D))
    delta_rows = lax.optimization_barrier(jnp.sum(split_heads(dout_blocks) * split_heads(outputs), -1)).transpose(0, 1, 3, 2)

    def query_row_grads(row_index):
        center = lax.dynamic_slice_in_dim(keyval_pad, row_index, 3, 0)
        valid_mask = lax.dynamic_slice_in_dim(key_valid, row_index, 3, 0)
        query_row = lax.dynamic_slice_in_dim(query_blocks, row_index, 1, 0)
        log_row = lax.dynamic_slice_in_dim(log_totals, row_index, 1, 0)
        dout_row = lax.dynamic_slice_in_dim(dout_blocks, row_index, 1, 0)
        delta_row = lax.dynamic_slice_in_dim(delta_rows, row_index, 1, 0)
        return query_grads(query_row, center, valid_mask, region_row(row_index), log_row, dout_row, delta_row)[0]
    d_queries = lax.map(query_row_grads, row_ids)
    query_pad = jnp.pad(query_blocks, block_pad)
    dout_pad = jnp.pad(dout_blocks, block_pad)
    log_pad = jnp.pad(log_totals, block_pad)
    delta_pad = jnp.pad(delta_rows, block_pad)

    def key_row_grads(row_index):
        center = lax.dynamic_slice_in_dim(keyval_pad, row_index + 1, 1, 0)[:, 1:-1]
        return key_grads(center, lax.dynamic_slice_in_dim(query_pad, row_index, 3, 0), lax.dynamic_slice_in_dim(dout_pad, row_index, 3, 0), lax.dynamic_slice_in_dim(log_pad, row_index, 3, 0), lax.dynamic_slice_in_dim(delta_pad, row_index, 3, 0), lax.dynamic_slice_in_dim(key_valid, row_index, 3, 0))

    def key_row_first(row_index):
        grad_key, grad_value = key_row_grads(row_index)
        return (grad_key[0], grad_value[0])
    d_keys, d_values = lax.map(key_row_first, row_ids)
    dq_flat = from_blocks(d_queries).reshape(-1, D)
    dk_flat = from_blocks(d_keys).reshape(-1, D)
    dv_flat = from_blocks(d_values).reshape(-1, D)
    grad_sum = jnp.dot(dq_flat, w_query.T, preferred_element_type=jnp.float32)
    grad_sum = grad_sum + jnp.dot(dk_flat, w_key.T, preferred_element_type=jnp.float32)
    grad_sum = grad_sum + jnp.dot(dv_flat, w_value.T, preferred_element_type=jnp.float32)
    grad_patches = grad_sum.astype(jnp.bfloat16).reshape(PATCH_ROWS, PATCH_COLS, D)
    grad_w_query = jnp.dot(flat_in.T, dq_flat, preferred_element_type=jnp.float32)
    grad_w_key = jnp.dot(flat_in.T, dk_flat, preferred_element_type=jnp.float32)
    grad_w_value = jnp.dot(flat_in.T, dv_flat, preferred_element_type=jnp.float32)
    return (layer_out.reshape(PATCH_ROWS, PATCH_COLS, D), grad_patches, grad_w_query, grad_w_key, grad_w_value, grad_w_out)
```

```python
import math

import jax
import jax.numpy as jnp
from jax import lax
from jax.sharding import PartitionSpec as P

D = 256
HEADS = 2
HEAD_DIM = 128
BSIDE = 8
BT = 64


masked_score = -1000000000.0


def padded(block, sides, width):
    for axis, dim in sides:
        count = lax.axis_size(axis)
        forward = [(i, i + 1) for i in range(count - 1)]
        backward = [(target, source) for source, target in forward]
        low = lax.ppermute(
            lax.slice_in_dim(block, block.shape[dim] - width, None, axis=dim), axis, forward
        )
        high = lax.ppermute(lax.slice_in_dim(block, 0, width, axis=dim), axis, backward)
        block = jnp.concatenate([low, block, high], axis=dim)
    return block


def to_blocks(grid_array):
    grid_rows, grid_cols, feature_width = grid_array.shape
    shaped = grid_array.reshape(grid_rows // BSIDE, BSIDE, grid_cols // BSIDE, BSIDE, feature_width)
    return shaped.transpose(0, 2, 1, 3, 4).reshape(
        grid_rows // BSIDE, grid_cols // BSIDE, BSIDE * BSIDE, feature_width
    )


def from_blocks(block_array):
    block_rows, block_cols, block_tokens, feature_width = block_array.shape
    shaped = block_array.reshape(block_rows, block_cols, BSIDE, BSIDE, feature_width)
    return shaped.transpose(0, 2, 1, 3, 4).reshape(
        block_rows * BSIDE, block_cols * BSIDE, feature_width
    )


def split_heads(source):
    return source.reshape(source.shape[:-1] + (HEADS, source.shape[-1] // HEADS))


def key_pieces(keyval_pad, key_valid, region_keyval):
    block_rows, block_cols = (region_keyval.shape[0], region_keyval.shape[1])
    pieces = []
    for row_off in range(3):
        for col_off in range(3):
            key_block = keyval_pad[row_off : row_off + block_rows, col_off : col_off + block_cols]
            valid_mask = key_valid[row_off : row_off + block_rows, col_off : col_off + block_cols]
            pieces.append((key_block[..., :D], key_block[..., D:], valid_mask))
    merged = region_keyval.reshape(block_rows, block_cols, 2 * BT, 2 * D)
    pieces.append(
        (merged[..., :D], merged[..., D:], jnp.ones((block_rows, block_cols), dtype=jnp.bool_))
    )
    return pieces


def piece_scores(query_heads, key_part, valid_mask):
    scores = jnp.einsum(
        "abqhe,abkhe->abhqk", query_heads, split_heads(key_part), preferred_element_type=jnp.float32
    )
    scores = scores * (1.0 / math.sqrt(HEAD_DIM))
    return jnp.where(valid_mask[:, :, None, None, None], scores, masked_score)


def attend_forward(query_blocks, keyval_pad, key_valid, region_keyval):
    query_heads = split_heads(query_blocks)
    pieces = key_pieces(keyval_pad, key_valid, region_keyval)
    scores = [
        piece_scores(query_heads, key_part, valid_mask)
        for key_part, value_part, valid_mask in pieces
    ]
    row_top = jnp.max(jnp.concatenate(scores, -1), -1, keepdims=True)
    row_total = sum(
        (jnp.sum(jnp.exp(part_scores - row_top), -1, keepdims=True) for part_scores in scores)
    )
    log_total = row_top + jnp.log(row_total)
    mixed_sum = jnp.zeros(query_heads.shape, jnp.float32)
    for part_scores, (key_part, value_part, valid_mask) in zip(scores, pieces):
        weights = jnp.exp(part_scores - log_total).astype(jnp.bfloat16)
        mixed_sum = mixed_sum + jnp.einsum(
            "abhqk,abkhe->abqhe",
            weights,
            split_heads(value_part),
            preferred_element_type=jnp.float32,
        )
    output = mixed_sum.reshape(query_blocks.shape).astype(jnp.bfloat16)
    return (output, log_total[..., 0])


def query_grads(
    query_blocks, keyval_pad, key_valid, region_keyval, log_total, dout_blocks, delta_rows
):
    query_heads = split_heads(query_blocks)
    dout_heads = split_heads(dout_blocks)
    accum_sum = jnp.zeros(query_heads.shape, jnp.float32)
    for key_part, value_part, valid_mask in key_pieces(keyval_pad, key_valid, region_keyval):
        part_scores = piece_scores(query_heads, key_part, valid_mask)
        prob_part = jnp.exp(part_scores - log_total[..., None])
        grad_prob = jnp.einsum(
            "abqhe,abkhe->abhqk",
            dout_heads,
            split_heads(value_part),
            preferred_element_type=jnp.float32,
        )
        grad_score = (prob_part * (grad_prob - delta_rows[..., None])).astype(jnp.bfloat16)
        accum_sum = accum_sum + jnp.einsum(
            "abhqk,abkhe->abqhe",
            grad_score,
            split_heads(key_part),
            preferred_element_type=jnp.float32,
        )
    return (
        (accum_sum * (1.0 / math.sqrt(HEAD_DIM))).reshape(query_blocks.shape).astype(jnp.bfloat16)
    )


def key_grads(keyval_center, query_pad, dout_pad, log_pad, delta_pad, query_valid):
    block_rows, block_cols = (keyval_center.shape[0], keyval_center.shape[1])
    key_heads = split_heads(keyval_center[..., :D])
    value_heads = split_heads(keyval_center[..., D:])
    grad_key = jnp.zeros(key_heads.shape, jnp.float32)
    grad_value = jnp.zeros(key_heads.shape, jnp.float32)
    for row_off in range(3):
        for col_off in range(3):
            query_heads = split_heads(
                query_pad[row_off : row_off + block_rows, col_off : col_off + block_cols]
            )
            dout_heads = split_heads(
                dout_pad[row_off : row_off + block_rows, col_off : col_off + block_cols]
            )
            log_part = log_pad[row_off : row_off + block_rows, col_off : col_off + block_cols]
            delta_part = delta_pad[row_off : row_off + block_rows, col_off : col_off + block_cols]
            valid_mask = query_valid[row_off : row_off + block_rows, col_off : col_off + block_cols]
            part_scores = jnp.einsum(
                "abqhe,abkhe->abhqk", query_heads, key_heads, preferred_element_type=jnp.float32
            )
            part_scores = part_scores * (1.0 / math.sqrt(HEAD_DIM))
            prob_part = jnp.where(
                valid_mask[:, :, None, None, None], jnp.exp(part_scores - log_part[..., None]), 0.0
            )
            grad_prob = jnp.einsum(
                "abqhe,abkhe->abhqk", dout_heads, value_heads, preferred_element_type=jnp.float32
            )
            grad_score = (prob_part * (grad_prob - delta_part[..., None])).astype(jnp.bfloat16)
            grad_key = grad_key + jnp.einsum(
                "abhqk,abqhe->abkhe", grad_score, query_heads, preferred_element_type=jnp.float32
            )
            rounded_prob = prob_part.astype(jnp.bfloat16)
            grad_value = grad_value + jnp.einsum(
                "abhqk,abqhe->abkhe", rounded_prob, dout_heads, preferred_element_type=jnp.float32
            )
    out_shape = (block_rows, block_cols, BT, D)
    grad_key = (grad_key * (1.0 / math.sqrt(HEAD_DIM))).reshape(out_shape).astype(jnp.bfloat16)
    return (grad_key, grad_value.reshape(out_shape).astype(jnp.bfloat16))


def inner_rows(left_rows, right_rows):
    return lax.dot_general(
        left_rows, right_rows, (((0,), (0,)), ((), ())), preferred_element_type=jnp.float32
    )


def halving_steps(axes):
    steps = []
    for axis in axes:
        count = lax.axis_size(axis)
        stride = 1
        while stride < count:
            steps.append((axis, stride))
            stride *= 2
    return steps


def tree_sum(parts, axes):
    sizes = [lax.axis_size(axis) for axis in axes]
    rows = sum(part.shape[0] for part in parts)
    total = math.prod(sizes)
    if any(size & (size - 1) for size in sizes) or rows % total:
        return lax.psum(parts, axes)
    steps = halving_steps(axes)
    joined = jnp.concatenate(parts, 0)
    for axis, stride in steps:
        pairs = [(i, i ^ stride) for i in range(lax.axis_size(axis))]
        bit = (lax.axis_index(axis) // stride) % 2
        half = joined.shape[0] // 2
        keep = lax.dynamic_slice_in_dim(joined, bit * half, half, 0)
        send = lax.dynamic_slice_in_dim(joined, (1 - bit) * half, half, 0)
        joined = keep + lax.ppermute(send, axis, pairs)
    for axis, stride in reversed(steps):
        pairs = [(i, i ^ stride) for i in range(lax.axis_size(axis))]
        bit = (lax.axis_index(axis) // stride) % 2
        got = lax.ppermute(joined, axis, pairs)
        low = jnp.where(bit == 0, joined, got)
        high = jnp.where(bit == 0, got, joined)
        joined = jnp.concatenate([low, high], 0)
    out = []
    start = 0
    for part in parts:
        out.append(joined[start : start + part.shape[0]])
        start += part.shape[0]
    return tuple(out)


def on_device(
    patches, w_query, w_key, w_value, w_out, region_memory, region_owner, region_local, grad_out
):
    tile_rows, tile_cols, model_width = patches.shape
    block_rows, block_cols = (tile_rows // BSIDE, tile_cols // BSIDE)
    block_count = block_rows * block_cols
    flat_in = patches.reshape(-1, model_width)
    w_pair = jnp.concatenate([w_key, w_value], 1)
    queries = jnp.dot(flat_in, w_query, preferred_element_type=jnp.float32).astype(jnp.bfloat16)
    keyvals = jnp.dot(flat_in, w_pair, preferred_element_type=jnp.float32).astype(jnp.bfloat16)
    keyvals = keyvals.reshape(tile_rows, tile_cols, 2 * model_width)
    keyval_grid = padded(keyvals, (("gx", 0), ("gy", 1)), BSIDE)
    keyval_pad = to_blocks(keyval_grid)
    gx_count = lax.axis_size("gx")
    gy_count = lax.axis_size("gy")
    row_ids = lax.axis_index("gx") * block_rows - 1 + jnp.arange(block_rows + 2, dtype=jnp.int32)
    col_ids = lax.axis_index("gy") * block_cols - 1 + jnp.arange(block_cols + 2, dtype=jnp.int32)
    row_valid = (row_ids >= 0) & (row_ids < block_rows * gx_count)
    col_valid = (col_ids >= 0) & (col_ids < block_cols * gy_count)
    key_valid = row_valid[:, None] & col_valid[None, :]
    owners = region_owner.reshape(2 * block_count)
    local_ids = region_local.reshape(2 * block_count)
    memory_local = region_memory.reshape(
        region_memory.shape[2], region_memory.shape[3], region_memory.shape[4]
    )
    region_count = memory_local.shape[0]
    row_tables = lax.all_gather(memory_local, "gx", axis=0, tiled=True)
    fetched = jnp.take(row_tables, owners * region_count + local_ids, axis=0)
    region_keyval = fetched.reshape(
        block_rows, block_cols, 2, memory_local.shape[1], memory_local.shape[2]
    )
    query_blocks = to_blocks(queries.reshape(tile_rows, tile_cols, model_width))
    outputs, log_totals = attend_forward(query_blocks, keyval_pad, key_valid, region_keyval)
    attended = from_blocks(outputs).reshape(-1, model_width)
    layer_out = jnp.dot(attended, w_out, preferred_element_type=jnp.float32).astype(jnp.bfloat16)
    grad_flat = grad_out.reshape(-1, model_width)
    d_attended = jnp.dot(grad_flat, w_out.T, preferred_element_type=jnp.float32).astype(
        jnp.bfloat16
    )
    grad_out_local = inner_rows(attended, grad_flat)
    dout_blocks = to_blocks(d_attended.reshape(tile_rows, tile_cols, model_width))
    delta_rows = jnp.sum(
        split_heads(dout_blocks).astype(jnp.float32) * split_heads(outputs).astype(jnp.float32), -1
    )
    delta_rows = delta_rows.transpose(0, 1, 3, 2)
    d_queries = query_grads(
        query_blocks, keyval_pad, key_valid, region_keyval, log_totals, dout_blocks, delta_rows
    )
    query_grid = jnp.concatenate(
        [
            queries.reshape(tile_rows, tile_cols, model_width),
            d_attended.reshape(tile_rows, tile_cols, model_width),
        ],
        -1,
    )
    query_halo = padded(query_grid, (("gx", 0), ("gy", 1)), BSIDE)
    stat_grid = from_blocks(jnp.concatenate([log_totals, delta_rows], 2).transpose(0, 1, 3, 2))
    stat_halo = padded(stat_grid, (("gx", 0), ("gy", 1)), BSIDE)
    query_all = to_blocks(query_halo)
    stat_pad = to_blocks(stat_halo).transpose(0, 1, 3, 2)
    d_keys, d_values = key_grads(
        keyval_pad[1:-1, 1:-1],
        query_all[..., :model_width],
        query_all[..., model_width:],
        stat_pad[:, :, :HEADS],
        stat_pad[:, :, HEADS:],
        key_valid,
    )
    dq_flat = from_blocks(d_queries).reshape(-1, model_width)
    dk_flat = from_blocks(d_keys).reshape(-1, model_width)
    dv_flat = from_blocks(d_values).reshape(-1, model_width)
    grads_joined = jnp.concatenate([dq_flat, dk_flat, dv_flat], 1)
    w_stacked = jnp.concatenate([w_query.T, w_key.T, w_value.T], 0)
    grad_patches = jnp.dot(grads_joined, w_stacked, preferred_element_type=jnp.float32).astype(
        jnp.bfloat16
    )
    partials = (
        inner_rows(flat_in, dq_flat),
        inner_rows(flat_in, dk_flat),
        inner_rows(flat_in, dv_flat),
        grad_out_local,
    )
    summed = tree_sum(partials, ("gy", "gx"))
    return (
        layer_out.reshape(tile_rows, tile_cols, model_width),
        grad_patches.reshape(tile_rows, tile_cols, model_width),
        summed[0],
        summed[1],
        summed[2],
        summed[3],
    )


def solution(mesh):
    return jax.shard_map(
        on_device,
        mesh=mesh,
        in_specs=(
            P("gx", "gy", None),
            P(),
            P(),
            P(),
            P(),
            P("gx", "gy", None, None, None),
            P("gx", "gy", None, None),
            P("gx", "gy", None, None),
            P("gx", "gy", None),
        ),
        out_specs=(P("gx", "gy", None), P("gx", "gy", None), P(), P(), P(), P()),
        check_vma=False,
    )
```

```python
import math

import jax
import jax.numpy as jnp
from jax import lax
from jax.sharding import PartitionSpec as P

D = 256
HEADS = 2
HEAD_DIM = 128
BSIDE = 8
BT = 64


masked_score = -1000000000.0


def padded(block, sides, width):
    for axis, dim in sides:
        count = lax.axis_size(axis)
        forward = [(i, i + 1) for i in range(count - 1)]
        backward = [(target, source) for source, target in forward]
        low = lax.ppermute(
            lax.slice_in_dim(block, block.shape[dim] - width, None, axis=dim), axis, forward
        )
        high = lax.ppermute(lax.slice_in_dim(block, 0, width, axis=dim), axis, backward)
        block = jnp.concatenate([low, block, high], axis=dim)
    return block


def to_blocks(grid_array):
    grid_rows, grid_cols, feature_width = grid_array.shape
    shaped = grid_array.reshape(grid_rows // BSIDE, BSIDE, grid_cols // BSIDE, BSIDE, feature_width)
    return shaped.transpose(0, 2, 1, 3, 4).reshape(
        grid_rows // BSIDE, grid_cols // BSIDE, BSIDE * BSIDE, feature_width
    )


def from_blocks(block_array):
    block_rows, block_cols, block_tokens, feature_width = block_array.shape
    shaped = block_array.reshape(block_rows, block_cols, BSIDE, BSIDE, feature_width)
    return shaped.transpose(0, 2, 1, 3, 4).reshape(
        block_rows * BSIDE, block_cols * BSIDE, feature_width
    )


def split_heads(source):
    return source.reshape(source.shape[:-1] + (HEADS, source.shape[-1] // HEADS))


def key_pieces(keyval_pad, key_valid, region_keyval):
    block_rows, block_cols = (region_keyval.shape[0], region_keyval.shape[1])
    pieces = []
    for row_off in range(3):
        for col_off in range(3):
            key_block = keyval_pad[row_off : row_off + block_rows, col_off : col_off + block_cols]
            valid_mask = key_valid[row_off : row_off + block_rows, col_off : col_off + block_cols]
            pieces.append((key_block[..., :D], key_block[..., D:], valid_mask))
    merged = region_keyval.reshape(block_rows, block_cols, 2 * BT, 2 * D)
    pieces.append(
        (merged[..., :D], merged[..., D:], jnp.ones((block_rows, block_cols), dtype=jnp.bool_))
    )
    return pieces


def piece_scores(query_heads, key_part, valid_mask):
    scores = jnp.einsum(
        "abqhe,abkhe->abhqk", query_heads, split_heads(key_part), preferred_element_type=jnp.float32
    )
    scores = scores * (1.0 / math.sqrt(HEAD_DIM))
    return jnp.where(valid_mask[:, :, None, None, None], scores, masked_score)


def attend_forward(query_blocks, keyval_pad, key_valid, region_keyval):
    query_heads = split_heads(query_blocks)
    pieces = key_pieces(keyval_pad, key_valid, region_keyval)
    scores = [
        piece_scores(query_heads, key_part, valid_mask)
        for key_part, value_part, valid_mask in pieces
    ]
    row_top = jnp.max(jnp.concatenate(scores, -1), -1, keepdims=True)
    row_total = sum(
        (jnp.sum(jnp.exp(part_scores - row_top), -1, keepdims=True) for part_scores in scores)
    )
    log_total = row_top + jnp.log(row_total)
    mixed_sum = jnp.zeros(query_heads.shape, jnp.float32)
    for part_scores, (key_part, value_part, valid_mask) in zip(scores, pieces):
        weights = jnp.exp(part_scores - log_total).astype(jnp.bfloat16)
        mixed_sum = mixed_sum + jnp.einsum(
            "abhqk,abkhe->abqhe",
            weights,
            split_heads(value_part),
            preferred_element_type=jnp.float32,
        )
    output = mixed_sum.reshape(query_blocks.shape).astype(jnp.bfloat16)
    return (output, log_total[..., 0])


def query_grads(
    query_blocks, keyval_pad, key_valid, region_keyval, log_total, dout_blocks, delta_rows
):
    query_heads = split_heads(query_blocks)
    dout_heads = split_heads(dout_blocks)
    accum_sum = jnp.zeros(query_heads.shape, jnp.float32)
    for key_part, value_part, valid_mask in key_pieces(keyval_pad, key_valid, region_keyval):
        part_scores = piece_scores(query_heads, key_part, valid_mask)
        prob_part = jnp.exp(part_scores - log_total[..., None])
        grad_prob = jnp.einsum(
            "abqhe,abkhe->abhqk",
            dout_heads,
            split_heads(value_part),
            preferred_element_type=jnp.float32,
        )
        grad_score = (prob_part * (grad_prob - delta_rows[..., None])).astype(jnp.bfloat16)
        accum_sum = accum_sum + jnp.einsum(
            "abhqk,abkhe->abqhe",
            grad_score,
            split_heads(key_part),
            preferred_element_type=jnp.float32,
        )
    return (
        (accum_sum * (1.0 / math.sqrt(HEAD_DIM))).reshape(query_blocks.shape).astype(jnp.bfloat16)
    )


def key_grads(keyval_center, query_pad, dout_pad, log_pad, delta_pad, query_valid):
    block_rows, block_cols = (keyval_center.shape[0], keyval_center.shape[1])
    key_heads = split_heads(keyval_center[..., :D])
    value_heads = split_heads(keyval_center[..., D:])
    grad_key = jnp.zeros(key_heads.shape, jnp.float32)
    grad_value = jnp.zeros(key_heads.shape, jnp.float32)
    for row_off in range(3):
        for col_off in range(3):
            query_heads = split_heads(
                query_pad[row_off : row_off + block_rows, col_off : col_off + block_cols]
            )
            dout_heads = split_heads(
                dout_pad[row_off : row_off + block_rows, col_off : col_off + block_cols]
            )
            log_part = log_pad[row_off : row_off + block_rows, col_off : col_off + block_cols]
            delta_part = delta_pad[row_off : row_off + block_rows, col_off : col_off + block_cols]
            valid_mask = query_valid[row_off : row_off + block_rows, col_off : col_off + block_cols]
            part_scores = jnp.einsum(
                "abqhe,abkhe->abhqk", query_heads, key_heads, preferred_element_type=jnp.float32
            )
            part_scores = part_scores * (1.0 / math.sqrt(HEAD_DIM))
            prob_part = jnp.where(
                valid_mask[:, :, None, None, None], jnp.exp(part_scores - log_part[..., None]), 0.0
            )
            grad_prob = jnp.einsum(
                "abqhe,abkhe->abhqk", dout_heads, value_heads, preferred_element_type=jnp.float32
            )
            grad_score = (prob_part * (grad_prob - delta_part[..., None])).astype(jnp.bfloat16)
            grad_key = grad_key + jnp.einsum(
                "abhqk,abqhe->abkhe", grad_score, query_heads, preferred_element_type=jnp.float32
            )
            rounded_prob = prob_part.astype(jnp.bfloat16)
            grad_value = grad_value + jnp.einsum(
                "abhqk,abqhe->abkhe", rounded_prob, dout_heads, preferred_element_type=jnp.float32
            )
    out_shape = (block_rows, block_cols, BT, D)
    grad_key = (grad_key * (1.0 / math.sqrt(HEAD_DIM))).reshape(out_shape).astype(jnp.bfloat16)
    return (grad_key, grad_value.reshape(out_shape).astype(jnp.bfloat16))


def inner_rows(left_rows, right_rows):
    return lax.dot_general(
        left_rows, right_rows, (((0,), (0,)), ((), ())), preferred_element_type=jnp.float32
    )


def halving_steps(axes):
    steps = []
    for axis in axes:
        count = lax.axis_size(axis)
        stride = 1
        while stride < count:
            steps.append((axis, stride))
            stride *= 2
    return steps


def doubling_gather(joined, steps):
    for axis, stride in reversed(steps):
        pairs = [(i, i ^ stride) for i in range(lax.axis_size(axis))]
        bit = (lax.axis_index(axis) // stride) % 2
        got = lax.ppermute(joined, axis, pairs)
        low = jnp.where(bit == 0, joined, got)
        high = jnp.where(bit == 0, got, joined)
        joined = jnp.concatenate([low, high], 0)
    return joined


def tree_gather(block, axis):
    count = lax.axis_size(axis)
    if count & (count - 1):
        return lax.all_gather(block, axis, axis=0, tiled=True), lambda index: index
    width = count.bit_length() - 1

    def slot_of(index):
        return sum(((index >> bit) & 1) << (width - 1 - bit) for bit in range(width))

    return doubling_gather(block, halving_steps((axis,))), slot_of


def tree_sum(parts, axes):
    sizes = [lax.axis_size(axis) for axis in axes]
    rows = sum(part.shape[0] for part in parts)
    total = math.prod(sizes)
    if any(size & (size - 1) for size in sizes) or rows % total:
        return lax.psum(parts, axes)
    steps = halving_steps(axes)
    joined = jnp.concatenate(parts, 0)
    for axis, stride in steps:
        pairs = [(i, i ^ stride) for i in range(lax.axis_size(axis))]
        bit = (lax.axis_index(axis) // stride) % 2
        half = joined.shape[0] // 2
        keep = lax.dynamic_slice_in_dim(joined, bit * half, half, 0)
        send = lax.dynamic_slice_in_dim(joined, (1 - bit) * half, half, 0)
        joined = keep + lax.ppermute(send, axis, pairs)
    joined = doubling_gather(joined, steps)
    out = []
    start = 0
    for part in parts:
        out.append(joined[start : start + part.shape[0]])
        start += part.shape[0]
    return tuple(out)


def on_device(
    patches, w_query, w_key, w_value, w_out, region_memory, region_owner, region_local, grad_out
):
    tile_rows, tile_cols, model_width = patches.shape
    block_rows, block_cols = (tile_rows // BSIDE, tile_cols // BSIDE)
    block_count = block_rows * block_cols
    flat_in = patches.reshape(-1, model_width)
    w_pair = jnp.concatenate([w_key, w_value], 1)
    queries = jnp.dot(flat_in, w_query, preferred_element_type=jnp.float32).astype(jnp.bfloat16)
    keyvals = jnp.dot(flat_in, w_pair, preferred_element_type=jnp.float32).astype(jnp.bfloat16)
    keyvals = keyvals.reshape(tile_rows, tile_cols, 2 * model_width)
    keyval_grid = padded(keyvals, (("gx", 0), ("gy", 1)), BSIDE)
    keyval_pad = to_blocks(keyval_grid)
    gx_count = lax.axis_size("gx")
    gy_count = lax.axis_size("gy")
    row_ids = lax.axis_index("gx") * block_rows - 1 + jnp.arange(block_rows + 2, dtype=jnp.int32)
    col_ids = lax.axis_index("gy") * block_cols - 1 + jnp.arange(block_cols + 2, dtype=jnp.int32)
    row_valid = (row_ids >= 0) & (row_ids < block_rows * gx_count)
    col_valid = (col_ids >= 0) & (col_ids < block_cols * gy_count)
    key_valid = row_valid[:, None] & col_valid[None, :]
    owners = region_owner.reshape(2 * block_count)
    local_ids = region_local.reshape(2 * block_count)
    memory_local = region_memory.reshape(
        region_memory.shape[2], region_memory.shape[3], region_memory.shape[4]
    )
    region_count = memory_local.shape[0]
    row_tables, slot_of = tree_gather(memory_local, "gx")
    fetched = jnp.take(row_tables, slot_of(owners) * region_count + local_ids, axis=0)
    region_keyval = fetched.reshape(
        block_rows, block_cols, 2, memory_local.shape[1], memory_local.shape[2]
    )
    query_blocks = to_blocks(queries.reshape(tile_rows, tile_cols, model_width))
    outputs, log_totals = attend_forward(query_blocks, keyval_pad, key_valid, region_keyval)
    attended = from_blocks(outputs).reshape(-1, model_width)
    layer_out = jnp.dot(attended, w_out, preferred_element_type=jnp.float32).astype(jnp.bfloat16)
    grad_flat = grad_out.reshape(-1, model_width)
    d_attended = jnp.dot(grad_flat, w_out.T, preferred_element_type=jnp.float32).astype(
        jnp.bfloat16
    )
    grad_out_local = inner_rows(attended, grad_flat)
    dout_blocks = to_blocks(d_attended.reshape(tile_rows, tile_cols, model_width))
    delta_rows = jnp.sum(
        split_heads(dout_blocks).astype(jnp.float32) * split_heads(outputs).astype(jnp.float32), -1
    )
    delta_rows = delta_rows.transpose(0, 1, 3, 2)
    d_queries = query_grads(
        query_blocks, keyval_pad, key_valid, region_keyval, log_totals, dout_blocks, delta_rows
    )
    query_grid = jnp.concatenate(
        [
            queries.reshape(tile_rows, tile_cols, model_width),
            d_attended.reshape(tile_rows, tile_cols, model_width),
        ],
        -1,
    )
    query_halo = padded(query_grid, (("gx", 0), ("gy", 1)), BSIDE)
    stat_grid = from_blocks(jnp.concatenate([log_totals, delta_rows], 2).transpose(0, 1, 3, 2))
    stat_halo = padded(stat_grid, (("gx", 0), ("gy", 1)), BSIDE)
    query_all = to_blocks(query_halo)
    stat_pad = to_blocks(stat_halo).transpose(0, 1, 3, 2)
    d_keys, d_values = key_grads(
        keyval_pad[1:-1, 1:-1],
        query_all[..., :model_width],
        query_all[..., model_width:],
        stat_pad[:, :, :HEADS],
        stat_pad[:, :, HEADS:],
        key_valid,
    )
    dq_flat = from_blocks(d_queries).reshape(-1, model_width)
    dk_flat = from_blocks(d_keys).reshape(-1, model_width)
    dv_flat = from_blocks(d_values).reshape(-1, model_width)
    grads_joined = jnp.concatenate([dq_flat, dk_flat, dv_flat], 1)
    w_stacked = jnp.concatenate([w_query.T, w_key.T, w_value.T], 0)
    grad_patches = jnp.dot(grads_joined, w_stacked, preferred_element_type=jnp.float32).astype(
        jnp.bfloat16
    )
    partials = (
        inner_rows(flat_in, dq_flat),
        inner_rows(flat_in, dk_flat),
        inner_rows(flat_in, dv_flat),
        grad_out_local,
    )
    summed = tree_sum(partials, ("gy", "gx"))
    return (
        layer_out.reshape(tile_rows, tile_cols, model_width),
        grad_patches.reshape(tile_rows, tile_cols, model_width),
        summed[0],
        summed[1],
        summed[2],
        summed[3],
    )


def solution(mesh):
    return jax.shard_map(
        on_device,
        mesh=mesh,
        in_specs=(
            P("gx", "gy", None),
            P(),
            P(),
            P(),
            P(),
            P("gx", "gy", None, None, None),
            P("gx", "gy", None, None),
            P("gx", "gy", None, None),
            P("gx", "gy", None),
        ),
        out_specs=(P("gx", "gy", None), P("gx", "gy", None), P(), P(), P(), P()),
        check_vma=False,
    )
```

```python
import math

import jax
import jax.numpy as jnp
from jax import lax
from jax.sharding import PartitionSpec as P

D = 256
HEADS = 2
HEAD_DIM = 128
BSIDE = 8
BT = 64


masked_score = -1000000000.0


def padded(block, sides, width):
    for axis, dim in sides:
        count = lax.axis_size(axis)
        forward = [(i, i + 1) for i in range(count - 1)]
        backward = [(target, source) for source, target in forward]
        low = lax.ppermute(
            lax.slice_in_dim(block, block.shape[dim] - width, None, axis=dim), axis, forward
        )
        high = lax.ppermute(lax.slice_in_dim(block, 0, width, axis=dim), axis, backward)
        block = jnp.concatenate([low, block, high], axis=dim)
    return block


def to_blocks(grid_array):
    grid_rows, grid_cols, feature_width = grid_array.shape
    shaped = grid_array.reshape(grid_rows // BSIDE, BSIDE, grid_cols // BSIDE, BSIDE, feature_width)
    return shaped.transpose(0, 2, 1, 3, 4).reshape(
        grid_rows // BSIDE, grid_cols // BSIDE, BSIDE * BSIDE, feature_width
    )


def from_blocks(block_array):
    block_rows, block_cols, block_tokens, feature_width = block_array.shape
    shaped = block_array.reshape(block_rows, block_cols, BSIDE, BSIDE, feature_width)
    return shaped.transpose(0, 2, 1, 3, 4).reshape(
        block_rows * BSIDE, block_cols * BSIDE, feature_width
    )


def split_heads(source):
    return source.reshape(source.shape[:-1] + (HEADS, source.shape[-1] // HEADS))


def key_pieces(keyval_pad, key_valid, region_keyval):
    block_rows, block_cols = (region_keyval.shape[0], region_keyval.shape[1])
    pieces = []
    for row_off in range(3):
        for col_off in range(3):
            key_block = keyval_pad[row_off : row_off + block_rows, col_off : col_off + block_cols]
            valid_mask = key_valid[row_off : row_off + block_rows, col_off : col_off + block_cols]
            pieces.append((key_block[..., :D], key_block[..., D:], valid_mask))
    merged = region_keyval.reshape(block_rows, block_cols, 2 * BT, 2 * D)
    pieces.append(
        (merged[..., :D], merged[..., D:], jnp.ones((block_rows, block_cols), dtype=jnp.bool_))
    )
    return pieces


def piece_scores(query_heads, key_part, valid_mask):
    scores = jnp.einsum(
        "abqhe,abkhe->abhqk", query_heads, split_heads(key_part), preferred_element_type=jnp.float32
    )
    scores = scores * (1.0 / math.sqrt(HEAD_DIM))
    return jnp.where(valid_mask[:, :, None, None, None], scores, masked_score)


def attend_forward(query_blocks, keyval_pad, key_valid, region_keyval):
    query_heads = split_heads(query_blocks)
    pieces = key_pieces(keyval_pad, key_valid, region_keyval)
    scores = [
        piece_scores(query_heads, key_part, valid_mask)
        for key_part, value_part, valid_mask in pieces
    ]
    row_top = jnp.max(jnp.concatenate(scores, -1), -1, keepdims=True)
    row_total = sum(
        (jnp.sum(jnp.exp(part_scores - row_top), -1, keepdims=True) for part_scores in scores)
    )
    log_total = row_top + jnp.log(row_total)
    mixed_sum = jnp.zeros(query_heads.shape, jnp.float32)
    for part_scores, (key_part, value_part, valid_mask) in zip(scores, pieces):
        weights = jnp.exp(part_scores - log_total).astype(jnp.bfloat16)
        mixed_sum = mixed_sum + jnp.einsum(
            "abhqk,abkhe->abqhe",
            weights,
            split_heads(value_part),
            preferred_element_type=jnp.float32,
        )
    output = mixed_sum.reshape(query_blocks.shape).astype(jnp.bfloat16)
    return (output, log_total[..., 0])


def query_grads(
    query_blocks, keyval_pad, key_valid, region_keyval, log_total, dout_blocks, delta_rows
):
    query_heads = split_heads(query_blocks)
    dout_heads = split_heads(dout_blocks)
    accum_sum = jnp.zeros(query_heads.shape, jnp.float32)
    for key_part, value_part, valid_mask in key_pieces(keyval_pad, key_valid, region_keyval):
        part_scores = piece_scores(query_heads, key_part, valid_mask)
        prob_part = jnp.exp(part_scores - log_total[..., None])
        grad_prob = jnp.einsum(
            "abqhe,abkhe->abhqk",
            dout_heads,
            split_heads(value_part),
            preferred_element_type=jnp.float32,
        )
        grad_score = (prob_part * (grad_prob - delta_rows[..., None])).astype(jnp.bfloat16)
        accum_sum = accum_sum + jnp.einsum(
            "abhqk,abkhe->abqhe",
            grad_score,
            split_heads(key_part),
            preferred_element_type=jnp.float32,
        )
    return (
        (accum_sum * (1.0 / math.sqrt(HEAD_DIM))).reshape(query_blocks.shape).astype(jnp.bfloat16)
    )


def key_grads(keyval_center, query_pad, dout_pad, log_pad, delta_pad, query_valid):
    block_rows, block_cols = (keyval_center.shape[0], keyval_center.shape[1])
    key_heads = split_heads(keyval_center[..., :D])
    value_heads = split_heads(keyval_center[..., D:])
    grad_key = jnp.zeros(key_heads.shape, jnp.float32)
    grad_value = jnp.zeros(key_heads.shape, jnp.float32)
    for row_off in range(3):
        for col_off in range(3):
            query_heads = split_heads(
                query_pad[row_off : row_off + block_rows, col_off : col_off + block_cols]
            )
            dout_heads = split_heads(
                dout_pad[row_off : row_off + block_rows, col_off : col_off + block_cols]
            )
            log_part = log_pad[row_off : row_off + block_rows, col_off : col_off + block_cols]
            delta_part = delta_pad[row_off : row_off + block_rows, col_off : col_off + block_cols]
            valid_mask = query_valid[row_off : row_off + block_rows, col_off : col_off + block_cols]
            part_scores = jnp.einsum(
                "abqhe,abkhe->abhqk", query_heads, key_heads, preferred_element_type=jnp.float32
            )
            part_scores = part_scores * (1.0 / math.sqrt(HEAD_DIM))
            prob_part = jnp.where(
                valid_mask[:, :, None, None, None], jnp.exp(part_scores - log_part[..., None]), 0.0
            )
            grad_prob = jnp.einsum(
                "abqhe,abkhe->abhqk", dout_heads, value_heads, preferred_element_type=jnp.float32
            )
            grad_score = (prob_part * (grad_prob - delta_part[..., None])).astype(jnp.bfloat16)
            grad_key = grad_key + jnp.einsum(
                "abhqk,abqhe->abkhe", grad_score, query_heads, preferred_element_type=jnp.float32
            )
            rounded_prob = prob_part.astype(jnp.bfloat16)
            grad_value = grad_value + jnp.einsum(
                "abhqk,abqhe->abkhe", rounded_prob, dout_heads, preferred_element_type=jnp.float32
            )
    out_shape = (block_rows, block_cols, BT, D)
    grad_key = (grad_key * (1.0 / math.sqrt(HEAD_DIM))).reshape(out_shape).astype(jnp.bfloat16)
    return (grad_key, grad_value.reshape(out_shape).astype(jnp.bfloat16))


def inner_rows(left_rows, right_rows):
    return lax.dot_general(
        left_rows, right_rows, (((0,), (0,)), ((), ())), preferred_element_type=jnp.float32
    )


def halving_steps(axes):
    steps = []
    for axis in axes:
        count = lax.axis_size(axis)
        stride = 1
        while stride < count:
            steps.append((axis, stride))
            stride *= 2
    return steps


def doubling_gather(joined, steps):
    for axis, stride in reversed(steps):
        pairs = [(i, i ^ stride) for i in range(lax.axis_size(axis))]
        bit = (lax.axis_index(axis) // stride) % 2
        got = lax.ppermute(joined, axis, pairs)
        low = jnp.where(bit == 0, joined, got)
        high = jnp.where(bit == 0, got, joined)
        joined = jnp.concatenate([low, high], 0)
    return joined


def tree_gather(block, axis):
    count = lax.axis_size(axis)
    if count & (count - 1):
        return lax.all_gather(block, axis, axis=0, tiled=True), lambda index: index
    width = count.bit_length() - 1

    def slot_of(index):
        return sum(((index >> bit) & 1) << (width - 1 - bit) for bit in range(width))

    return doubling_gather(block, halving_steps((axis,))), slot_of


def tree_sum(parts, axes):
    sizes = [lax.axis_size(axis) for axis in axes]
    rows = sum(part.shape[0] for part in parts)
    if any(size & (size - 1) for size in sizes) or rows % math.prod(sizes):
        return lax.psum(parts, axes)
    steps = halving_steps(axes)
    last = [step for step in steps if step[0] == axes[-1]]
    halving = steps[: len(steps) - len(last) + 1]
    doubling = steps[len(halving) :]
    joined = jnp.concatenate(parts, 0)
    for axis, stride in halving:
        pairs = [(i, i ^ stride) for i in range(lax.axis_size(axis))]
        bit = (lax.axis_index(axis) // stride) % 2
        half = joined.shape[0] // 2
        keep = lax.dynamic_slice_in_dim(joined, bit * half, half, 0)
        send = lax.dynamic_slice_in_dim(joined, (1 - bit) * half, half, 0)
        joined = keep + lax.ppermute(send, axis, pairs)
    for axis, stride in doubling:
        pairs = [(i, i ^ stride) for i in range(lax.axis_size(axis))]
        joined = joined + lax.ppermute(joined, axis, pairs)
    joined = doubling_gather(joined, halving)
    out = []
    start = 0
    for part in parts:
        out.append(joined[start : start + part.shape[0]])
        start += part.shape[0]
    return tuple(out)


def on_device(
    patches, w_query, w_key, w_value, w_out, region_memory, region_owner, region_local, grad_out
):
    tile_rows, tile_cols, model_width = patches.shape
    block_rows, block_cols = (tile_rows // BSIDE, tile_cols // BSIDE)
    block_count = block_rows * block_cols
    flat_in = patches.reshape(-1, model_width)
    w_pair = jnp.concatenate([w_key, w_value], 1)
    queries = jnp.dot(flat_in, w_query, preferred_element_type=jnp.float32).astype(jnp.bfloat16)
    keyvals = jnp.dot(flat_in, w_pair, preferred_element_type=jnp.float32).astype(jnp.bfloat16)
    keyvals = keyvals.reshape(tile_rows, tile_cols, 2 * model_width)
    keyval_grid = padded(keyvals, (("gx", 0), ("gy", 1)), BSIDE)
    keyval_pad = to_blocks(keyval_grid)
    gx_count = lax.axis_size("gx")
    gy_count = lax.axis_size("gy")
    row_ids = lax.axis_index("gx") * block_rows - 1 + jnp.arange(block_rows + 2, dtype=jnp.int32)
    col_ids = lax.axis_index("gy") * block_cols - 1 + jnp.arange(block_cols + 2, dtype=jnp.int32)
    row_valid = (row_ids >= 0) & (row_ids < block_rows * gx_count)
    col_valid = (col_ids >= 0) & (col_ids < block_cols * gy_count)
    key_valid = row_valid[:, None] & col_valid[None, :]
    owners = region_owner.reshape(2 * block_count)
    local_ids = region_local.reshape(2 * block_count)
    memory_local = region_memory.reshape(
        region_memory.shape[2], region_memory.shape[3], region_memory.shape[4]
    )
    region_count = memory_local.shape[0]
    row_tables, slot_of = tree_gather(memory_local, "gx")
    fetched = jnp.take(row_tables, slot_of(owners) * region_count + local_ids, axis=0)
    region_keyval = fetched.reshape(
        block_rows, block_cols, 2, memory_local.shape[1], memory_local.shape[2]
    )
    query_blocks = to_blocks(queries.reshape(tile_rows, tile_cols, model_width))
    outputs, log_totals = attend_forward(query_blocks, keyval_pad, key_valid, region_keyval)
    attended = from_blocks(outputs).reshape(-1, model_width)
    layer_out = jnp.dot(attended, w_out, preferred_element_type=jnp.float32).astype(jnp.bfloat16)
    grad_flat = grad_out.reshape(-1, model_width)
    d_attended = jnp.dot(grad_flat, w_out.T, preferred_element_type=jnp.float32).astype(
        jnp.bfloat16
    )
    grad_out_local = inner_rows(attended, grad_flat)
    dout_blocks = to_blocks(d_attended.reshape(tile_rows, tile_cols, model_width))
    delta_rows = jnp.sum(
        split_heads(dout_blocks).astype(jnp.float32) * split_heads(outputs).astype(jnp.float32), -1
    )
    delta_rows = delta_rows.transpose(0, 1, 3, 2)
    d_queries = query_grads(
        query_blocks, keyval_pad, key_valid, region_keyval, log_totals, dout_blocks, delta_rows
    )
    query_grid = jnp.concatenate(
        [
            queries.reshape(tile_rows, tile_cols, model_width),
            d_attended.reshape(tile_rows, tile_cols, model_width),
        ],
        -1,
    )
    query_halo = padded(query_grid, (("gx", 0), ("gy", 1)), BSIDE)
    stat_grid = from_blocks(jnp.concatenate([log_totals, delta_rows], 2).transpose(0, 1, 3, 2))
    stat_halo = padded(stat_grid, (("gx", 0), ("gy", 1)), BSIDE)
    query_all = to_blocks(query_halo)
    stat_pad = to_blocks(stat_halo).transpose(0, 1, 3, 2)
    d_keys, d_values = key_grads(
        keyval_pad[1:-1, 1:-1],
        query_all[..., :model_width],
        query_all[..., model_width:],
        stat_pad[:, :, :HEADS],
        stat_pad[:, :, HEADS:],
        key_valid,
    )
    dq_flat = from_blocks(d_queries).reshape(-1, model_width)
    dk_flat = from_blocks(d_keys).reshape(-1, model_width)
    dv_flat = from_blocks(d_values).reshape(-1, model_width)
    grads_joined = jnp.concatenate([dq_flat, dk_flat, dv_flat], 1)
    w_stacked = jnp.concatenate([w_query.T, w_key.T, w_value.T], 0)
    grad_patches = jnp.dot(grads_joined, w_stacked, preferred_element_type=jnp.float32).astype(
        jnp.bfloat16
    )
    partials = (
        inner_rows(flat_in, dq_flat),
        inner_rows(flat_in, dk_flat),
        inner_rows(flat_in, dv_flat),
        grad_out_local,
    )
    summed = tree_sum(partials, ("gy", "gx"))
    return (
        layer_out.reshape(tile_rows, tile_cols, model_width),
        grad_patches.reshape(tile_rows, tile_cols, model_width),
        summed[0],
        summed[1],
        summed[2],
        summed[3],
    )


def solution(mesh):
    return jax.shard_map(
        on_device,
        mesh=mesh,
        in_specs=(
            P("gx", "gy", None),
            P(),
            P(),
            P(),
            P(),
            P("gx", "gy", None, None, None),
            P("gx", "gy", None, None),
            P("gx", "gy", None, None),
            P("gx", "gy", None),
        ),
        out_specs=(P("gx", "gy", None), P("gx", "gy", None), P(), P(), P(), P()),
        check_vma=False,
    )
```

```python
import math

import jax
import jax.numpy as jnp
from jax import lax
from jax.sharding import PartitionSpec as P

D = 256
HEADS = 2
HEAD_DIM = 128
BSIDE = 8
BT = 64


masked_score = -1000000000.0


def padded(block, sides, width):
    for axis, dim in sides:
        count = lax.axis_size(axis)
        forward = [(i, i + 1) for i in range(count - 1)]
        backward = [(target, source) for source, target in forward]
        low = lax.ppermute(
            lax.slice_in_dim(block, block.shape[dim] - width, None, axis=dim), axis, forward
        )
        high = lax.ppermute(lax.slice_in_dim(block, 0, width, axis=dim), axis, backward)
        block = jnp.concatenate([low, block, high], axis=dim)
    return block


def to_blocks(grid_array):
    grid_rows, grid_cols, feature_width = grid_array.shape
    shaped = grid_array.reshape(grid_rows // BSIDE, BSIDE, grid_cols // BSIDE, BSIDE, feature_width)
    return shaped.transpose(0, 2, 1, 3, 4).reshape(
        grid_rows // BSIDE, grid_cols // BSIDE, BSIDE * BSIDE, feature_width
    )


def from_blocks(block_array):
    block_rows, block_cols, block_tokens, feature_width = block_array.shape
    shaped = block_array.reshape(block_rows, block_cols, BSIDE, BSIDE, feature_width)
    return shaped.transpose(0, 2, 1, 3, 4).reshape(
        block_rows * BSIDE, block_cols * BSIDE, feature_width
    )


def split_heads(source):
    return source.reshape(source.shape[:-1] + (HEADS, source.shape[-1] // HEADS))


def key_pieces(keyval_pad, key_valid, region_keyval):
    block_rows, block_cols = (region_keyval.shape[0], region_keyval.shape[1])
    pieces = []
    for row_off in range(3):
        for col_off in range(3):
            key_block = keyval_pad[row_off : row_off + block_rows, col_off : col_off + block_cols]
            valid_mask = key_valid[row_off : row_off + block_rows, col_off : col_off + block_cols]
            pieces.append((key_block[..., :D], key_block[..., D:], valid_mask))
    merged = region_keyval.reshape(block_rows, block_cols, 2 * BT, 2 * D)
    pieces.append(
        (merged[..., :D], merged[..., D:], jnp.ones((block_rows, block_cols), dtype=jnp.bool_))
    )
    return pieces


def piece_scores(query_heads, key_part, valid_mask):
    scores = jnp.einsum(
        "abqhe,abkhe->abhqk", query_heads, split_heads(key_part), preferred_element_type=jnp.float32
    )
    scores = scores * (1.0 / math.sqrt(HEAD_DIM))
    return jnp.where(valid_mask[:, :, None, None, None], scores, masked_score)


def attend_forward(query_blocks, keyval_pad, key_valid, region_keyval):
    query_heads = split_heads(query_blocks)
    pieces = key_pieces(keyval_pad, key_valid, region_keyval)
    scores = [
        piece_scores(query_heads, key_part, valid_mask)
        for key_part, value_part, valid_mask in pieces
    ]
    row_top = jnp.max(jnp.concatenate(scores, -1), -1, keepdims=True)
    row_total = sum(
        (jnp.sum(jnp.exp(part_scores - row_top), -1, keepdims=True) for part_scores in scores)
    )
    log_total = row_top + jnp.log(row_total)
    mixed_sum = jnp.zeros(query_heads.shape, jnp.float32)
    for part_scores, (key_part, value_part, valid_mask) in zip(scores, pieces):
        weights = jnp.exp(part_scores - log_total).astype(jnp.bfloat16)
        mixed_sum = mixed_sum + jnp.einsum(
            "abhqk,abkhe->abqhe",
            weights,
            split_heads(value_part),
            preferred_element_type=jnp.float32,
        )
    output = mixed_sum.reshape(query_blocks.shape).astype(jnp.bfloat16)
    return (output, log_total[..., 0])


def query_grads(
    query_blocks, keyval_pad, key_valid, region_keyval, log_total, dout_blocks, delta_rows
):
    query_heads = split_heads(query_blocks)
    dout_heads = split_heads(dout_blocks)
    accum_sum = jnp.zeros(query_heads.shape, jnp.float32)
    for key_part, value_part, valid_mask in key_pieces(keyval_pad, key_valid, region_keyval):
        part_scores = piece_scores(query_heads, key_part, valid_mask)
        prob_part = jnp.exp(part_scores - log_total[..., None])
        grad_prob = jnp.einsum(
            "abqhe,abkhe->abhqk",
            dout_heads,
            split_heads(value_part),
            preferred_element_type=jnp.float32,
        )
        grad_score = (prob_part * (grad_prob - delta_rows[..., None])).astype(jnp.bfloat16)
        accum_sum = accum_sum + jnp.einsum(
            "abhqk,abkhe->abqhe",
            grad_score,
            split_heads(key_part),
            preferred_element_type=jnp.float32,
        )
    return (
        (accum_sum * (1.0 / math.sqrt(HEAD_DIM))).reshape(query_blocks.shape).astype(jnp.bfloat16)
    )


def key_grads(keyval_center, query_pad, dout_pad, log_pad, delta_pad, query_valid):
    block_rows, block_cols = (keyval_center.shape[0], keyval_center.shape[1])
    key_heads = split_heads(keyval_center[..., :D])
    value_heads = split_heads(keyval_center[..., D:])
    grad_key = jnp.zeros(key_heads.shape, jnp.float32)
    grad_value = jnp.zeros(key_heads.shape, jnp.float32)
    for row_off in range(3):
        for col_off in range(3):
            query_heads = split_heads(
                query_pad[row_off : row_off + block_rows, col_off : col_off + block_cols]
            )
            dout_heads = split_heads(
                dout_pad[row_off : row_off + block_rows, col_off : col_off + block_cols]
            )
            log_part = log_pad[row_off : row_off + block_rows, col_off : col_off + block_cols]
            delta_part = delta_pad[row_off : row_off + block_rows, col_off : col_off + block_cols]
            valid_mask = query_valid[row_off : row_off + block_rows, col_off : col_off + block_cols]
            part_scores = jnp.einsum(
                "abqhe,abkhe->abhqk", query_heads, key_heads, preferred_element_type=jnp.float32
            )
            part_scores = part_scores * (1.0 / math.sqrt(HEAD_DIM))
            prob_part = jnp.where(
                valid_mask[:, :, None, None, None], jnp.exp(part_scores - log_part[..., None]), 0.0
            )
            grad_prob = jnp.einsum(
                "abqhe,abkhe->abhqk", dout_heads, value_heads, preferred_element_type=jnp.float32
            )
            grad_score = (prob_part * (grad_prob - delta_part[..., None])).astype(jnp.bfloat16)
            grad_key = grad_key + jnp.einsum(
                "abhqk,abqhe->abkhe", grad_score, query_heads, preferred_element_type=jnp.float32
            )
            rounded_prob = prob_part.astype(jnp.bfloat16)
            grad_value = grad_value + jnp.einsum(
                "abhqk,abqhe->abkhe", rounded_prob, dout_heads, preferred_element_type=jnp.float32
            )
    out_shape = (block_rows, block_cols, BT, D)
    grad_key = (grad_key * (1.0 / math.sqrt(HEAD_DIM))).reshape(out_shape).astype(jnp.bfloat16)
    return (grad_key, grad_value.reshape(out_shape).astype(jnp.bfloat16))


def inner_rows(left_rows, right_rows):
    return lax.dot_general(
        left_rows, right_rows, (((0,), (0,)), ((), ())), preferred_element_type=jnp.float32
    )


def halving_steps(axes):
    steps = []
    for axis in axes:
        count = lax.axis_size(axis)
        stride = 1
        while stride < count:
            steps.append((axis, stride))
            stride *= 2
    return steps


def doubling_gather(joined, steps):
    for axis, stride in reversed(steps):
        pairs = [(i, i ^ stride) for i in range(lax.axis_size(axis))]
        bit = (lax.axis_index(axis) // stride) % 2
        got = lax.ppermute(joined, axis, pairs)
        low = jnp.where(bit == 0, joined, got)
        high = jnp.where(bit == 0, got, joined)
        joined = jnp.concatenate([low, high], 0)
    return joined


def tree_gather(block, axis):
    count = lax.axis_size(axis)
    if count & (count - 1):
        return lax.all_gather(block, axis, axis=0, tiled=True), lambda index: index
    width = count.bit_length() - 1

    def slot_of(index):
        return sum(((index >> bit) & 1) << (width - 1 - bit) for bit in range(width))

    return doubling_gather(block, halving_steps((axis,))), slot_of


def tree_sum(parts, axes):
    sizes = [lax.axis_size(axis) for axis in axes]
    rows = sum(part.shape[0] for part in parts)
    if any(size & (size - 1) for size in sizes) or rows % math.prod(sizes):
        return lax.psum(parts, axes)
    steps = halving_steps(axes)
    last = [step for step in steps if step[0] == axes[-1]]
    halving = steps[: len(steps) - len(last) + 1]
    doubling = steps[len(halving) :]
    joined = jnp.concatenate(parts, 0)
    for axis, stride in halving:
        pairs = [(i, i ^ stride) for i in range(lax.axis_size(axis))]
        bit = (lax.axis_index(axis) // stride) % 2
        half = joined.shape[0] // 2
        keep = lax.dynamic_slice_in_dim(joined, bit * half, half, 0)
        send = lax.dynamic_slice_in_dim(joined, (1 - bit) * half, half, 0)
        joined = keep + lax.ppermute(send, axis, pairs)
    for axis, stride in doubling:
        pairs = [(i, i ^ stride) for i in range(lax.axis_size(axis))]
        joined = joined + lax.ppermute(joined, axis, pairs)
    joined = doubling_gather(joined, halving)
    out = []
    start = 0
    for part in parts:
        out.append(joined[start : start + part.shape[0]])
        start += part.shape[0]
    return tuple(out)


def on_device(
    patches, w_query, w_key, w_value, w_out, region_memory, region_owner, region_local, grad_out
):
    tile_rows, tile_cols, model_width = patches.shape
    block_rows, block_cols = (tile_rows // BSIDE, tile_cols // BSIDE)
    block_count = block_rows * block_cols
    flat_in = patches.reshape(-1, model_width)
    w_pair = jnp.concatenate([w_key, w_value], 1)
    queries = jnp.dot(flat_in, w_query, preferred_element_type=jnp.float32).astype(jnp.bfloat16)
    keyvals = jnp.dot(flat_in, w_pair, preferred_element_type=jnp.float32).astype(jnp.bfloat16)
    keyvals = keyvals.reshape(tile_rows, tile_cols, 2 * model_width)
    keyval_grid = padded(keyvals, (("gx", 0), ("gy", 1)), BSIDE)
    keyval_pad = to_blocks(keyval_grid)
    gx_count = lax.axis_size("gx")
    gy_count = lax.axis_size("gy")
    row_ids = lax.axis_index("gx") * block_rows - 1 + jnp.arange(block_rows + 2, dtype=jnp.int32)
    col_ids = lax.axis_index("gy") * block_cols - 1 + jnp.arange(block_cols + 2, dtype=jnp.int32)
    row_valid = (row_ids >= 0) & (row_ids < block_rows * gx_count)
    col_valid = (col_ids >= 0) & (col_ids < block_cols * gy_count)
    key_valid = row_valid[:, None] & col_valid[None, :]
    owners = region_owner.reshape(2 * block_count)
    local_ids = region_local.reshape(2 * block_count)
    memory_local = region_memory.reshape(
        region_memory.shape[2], region_memory.shape[3], region_memory.shape[4]
    )
    region_count = memory_local.shape[0]
    row_tables = lax.all_gather(memory_local, "gx", axis=0, tiled=True)
    fetched = jnp.take(row_tables, owners * region_count + local_ids, axis=0)
    region_keyval = fetched.reshape(
        block_rows, block_cols, 2, memory_local.shape[1], memory_local.shape[2]
    )
    query_blocks = to_blocks(queries.reshape(tile_rows, tile_cols, model_width))
    outputs, log_totals = attend_forward(query_blocks, keyval_pad, key_valid, region_keyval)
    attended = from_blocks(outputs).reshape(-1, model_width)
    layer_out = jnp.dot(attended, w_out, preferred_element_type=jnp.float32).astype(jnp.bfloat16)
    grad_flat = grad_out.reshape(-1, model_width)
    d_attended = jnp.dot(grad_flat, w_out.T, preferred_element_type=jnp.float32).astype(
        jnp.bfloat16
    )
    grad_out_local = inner_rows(attended, grad_flat)
    dout_blocks = to_blocks(d_attended.reshape(tile_rows, tile_cols, model_width))
    delta_rows = jnp.sum(
        split_heads(dout_blocks).astype(jnp.float32) * split_heads(outputs).astype(jnp.float32), -1
    )
    delta_rows = delta_rows.transpose(0, 1, 3, 2)
    d_queries = query_grads(
        query_blocks, keyval_pad, key_valid, region_keyval, log_totals, dout_blocks, delta_rows
    )
    query_grid = jnp.concatenate(
        [
            queries.reshape(tile_rows, tile_cols, model_width),
            d_attended.reshape(tile_rows, tile_cols, model_width),
        ],
        -1,
    )
    query_halo = padded(query_grid, (("gx", 0), ("gy", 1)), BSIDE)
    stat_grid = from_blocks(jnp.concatenate([log_totals, delta_rows], 2).transpose(0, 1, 3, 2))
    stat_halo = padded(stat_grid, (("gx", 0), ("gy", 1)), BSIDE)
    query_all = to_blocks(query_halo)
    stat_pad = to_blocks(stat_halo).transpose(0, 1, 3, 2)
    d_keys, d_values = key_grads(
        keyval_pad[1:-1, 1:-1],
        query_all[..., :model_width],
        query_all[..., model_width:],
        stat_pad[:, :, :HEADS],
        stat_pad[:, :, HEADS:],
        key_valid,
    )
    dq_flat = from_blocks(d_queries).reshape(-1, model_width)
    dk_flat = from_blocks(d_keys).reshape(-1, model_width)
    dv_flat = from_blocks(d_values).reshape(-1, model_width)
    grads_joined = jnp.concatenate([dq_flat, dk_flat, dv_flat], 1)
    w_stacked = jnp.concatenate([w_query.T, w_key.T, w_value.T], 0)
    grad_patches = jnp.dot(grads_joined, w_stacked, preferred_element_type=jnp.float32).astype(
        jnp.bfloat16
    )
    partials = (
        inner_rows(flat_in, dq_flat),
        inner_rows(flat_in, dk_flat),
        inner_rows(flat_in, dv_flat),
        grad_out_local,
    )
    summed = tree_sum(partials, ("gy", "gx"))
    return (
        layer_out.reshape(tile_rows, tile_cols, model_width),
        grad_patches.reshape(tile_rows, tile_cols, model_width),
        summed[0],
        summed[1],
        summed[2],
        summed[3],
    )


def solution(mesh):
    return jax.shard_map(
        on_device,
        mesh=mesh,
        in_specs=(
            P("gx", "gy", None),
            P(),
            P(),
            P(),
            P(),
            P("gx", "gy", None, None, None),
            P("gx", "gy", None, None),
            P("gx", "gy", None, None),
            P("gx", "gy", None),
        ),
        out_specs=(P("gx", "gy", None), P("gx", "gy", None), P(), P(), P(), P()),
        check_vma=False,
    )
```

```python
import math

import jax
import jax.numpy as jnp
from jax import lax
from jax.sharding import PartitionSpec as P

D = 256
HEADS = 2
HEAD_DIM = 128
BSIDE = 8
BT = 64


masked_score = -1000000000.0


def padded(block, sides, width):
    for axis, dim in sides:
        count = lax.axis_size(axis)
        forward = [(i, i + 1) for i in range(count - 1)]
        backward = [(target, source) for source, target in forward]
        low = lax.ppermute(
            lax.slice_in_dim(block, block.shape[dim] - width, None, axis=dim), axis, forward
        )
        high = lax.ppermute(lax.slice_in_dim(block, 0, width, axis=dim), axis, backward)
        block = jnp.concatenate([low, block, high], axis=dim)
    return block


def halo(block, width):
    axes = ("gx", "gy")
    rows_n, cols_n = lax.axis_size("gx"), lax.axis_size("gy")
    rows, cols = block.shape[0], block.shape[1]
    row_parts = {-1: slice(rows - width, rows), 0: slice(0, rows), 1: slice(0, width)}
    col_parts = {-1: slice(cols - width, cols), 0: slice(0, cols), 1: slice(0, width)}
    grid = []
    for row_off in (-1, 0, 1):
        line = []
        for col_off in (-1, 0, 1):
            piece = block[row_parts[row_off], col_parts[col_off]]
            if row_off or col_off:
                pairs = [
                    ((i + row_off) * cols_n + j + col_off, i * cols_n + j)
                    for i in range(rows_n)
                    for j in range(cols_n)
                    if 0 <= i + row_off < rows_n and 0 <= j + col_off < cols_n
                ]
                piece = lax.ppermute(piece, axes, pairs)
            line.append(piece)
        grid.append(jnp.concatenate(line, axis=1))
    return jnp.concatenate(grid, axis=0)


def to_blocks(grid_array):
    grid_rows, grid_cols, feature_width = grid_array.shape
    shaped = grid_array.reshape(grid_rows // BSIDE, BSIDE, grid_cols // BSIDE, BSIDE, feature_width)
    return shaped.transpose(0, 2, 1, 3, 4).reshape(
        grid_rows // BSIDE, grid_cols // BSIDE, BSIDE * BSIDE, feature_width
    )


def from_blocks(block_array):
    block_rows, block_cols, block_tokens, feature_width = block_array.shape
    shaped = block_array.reshape(block_rows, block_cols, BSIDE, BSIDE, feature_width)
    return shaped.transpose(0, 2, 1, 3, 4).reshape(
        block_rows * BSIDE, block_cols * BSIDE, feature_width
    )


def split_heads(source):
    return source.reshape(source.shape[:-1] + (HEADS, source.shape[-1] // HEADS))


def key_pieces(keyval_pad, key_valid, region_keyval):
    block_rows, block_cols = (region_keyval.shape[0], region_keyval.shape[1])
    pieces = []
    for row_off in range(3):
        for col_off in range(3):
            key_block = keyval_pad[row_off : row_off + block_rows, col_off : col_off + block_cols]
            valid_mask = key_valid[row_off : row_off + block_rows, col_off : col_off + block_cols]
            pieces.append((key_block[..., :D], key_block[..., D:], valid_mask))
    merged = region_keyval.reshape(block_rows, block_cols, 2 * BT, 2 * D)
    pieces.append(
        (merged[..., :D], merged[..., D:], jnp.ones((block_rows, block_cols), dtype=jnp.bool_))
    )
    return pieces


def piece_scores(query_heads, key_part, valid_mask):
    scores = jnp.einsum(
        "abqhe,abkhe->abhqk", query_heads, split_heads(key_part), preferred_element_type=jnp.float32
    )
    scores = scores * (1.0 / math.sqrt(HEAD_DIM))
    return jnp.where(valid_mask[:, :, None, None, None], scores, masked_score)


def attend_forward(query_blocks, keyval_pad, key_valid, region_keyval):
    query_heads = split_heads(query_blocks)
    pieces = key_pieces(keyval_pad, key_valid, region_keyval)
    scores = [
        piece_scores(query_heads, key_part, valid_mask)
        for key_part, value_part, valid_mask in pieces
    ]
    row_top = jnp.max(jnp.concatenate(scores, -1), -1, keepdims=True)
    row_total = sum(
        (jnp.sum(jnp.exp(part_scores - row_top), -1, keepdims=True) for part_scores in scores)
    )
    log_total = row_top + jnp.log(row_total)
    mixed_sum = jnp.zeros(query_heads.shape, jnp.float32)
    for part_scores, (key_part, value_part, valid_mask) in zip(scores, pieces):
        weights = jnp.exp(part_scores - log_total).astype(jnp.bfloat16)
        mixed_sum = mixed_sum + jnp.einsum(
            "abhqk,abkhe->abqhe",
            weights,
            split_heads(value_part),
            preferred_element_type=jnp.float32,
        )
    output = mixed_sum.reshape(query_blocks.shape).astype(jnp.bfloat16)
    return (output, log_total[..., 0])


def query_grads(
    query_blocks, keyval_pad, key_valid, region_keyval, log_total, dout_blocks, delta_rows
):
    query_heads = split_heads(query_blocks)
    dout_heads = split_heads(dout_blocks)
    accum_sum = jnp.zeros(query_heads.shape, jnp.float32)
    for key_part, value_part, valid_mask in key_pieces(keyval_pad, key_valid, region_keyval):
        part_scores = piece_scores(query_heads, key_part, valid_mask)
        prob_part = jnp.exp(part_scores - log_total[..., None])
        grad_prob = jnp.einsum(
            "abqhe,abkhe->abhqk",
            dout_heads,
            split_heads(value_part),
            preferred_element_type=jnp.float32,
        )
        grad_score = (prob_part * (grad_prob - delta_rows[..., None])).astype(jnp.bfloat16)
        accum_sum = accum_sum + jnp.einsum(
            "abhqk,abkhe->abqhe",
            grad_score,
            split_heads(key_part),
            preferred_element_type=jnp.float32,
        )
    return (
        (accum_sum * (1.0 / math.sqrt(HEAD_DIM))).reshape(query_blocks.shape).astype(jnp.bfloat16)
    )


def key_grads(keyval_center, query_pad, dout_pad, log_pad, delta_pad, query_valid):
    block_rows, block_cols = (keyval_center.shape[0], keyval_center.shape[1])
    key_heads = split_heads(keyval_center[..., :D])
    value_heads = split_heads(keyval_center[..., D:])
    grad_key = jnp.zeros(key_heads.shape, jnp.float32)
    grad_value = jnp.zeros(key_heads.shape, jnp.float32)
    for row_off in range(3):
        for col_off in range(3):
            query_heads = split_heads(
                query_pad[row_off : row_off + block_rows, col_off : col_off + block_cols]
            )
            dout_heads = split_heads(
                dout_pad[row_off : row_off + block_rows, col_off : col_off + block_cols]
            )
            log_part = log_pad[row_off : row_off + block_rows, col_off : col_off + block_cols]
            delta_part = delta_pad[row_off : row_off + block_rows, col_off : col_off + block_cols]
            valid_mask = query_valid[row_off : row_off + block_rows, col_off : col_off + block_cols]
            part_scores = jnp.einsum(
                "abqhe,abkhe->abhqk", query_heads, key_heads, preferred_element_type=jnp.float32
            )
            part_scores = part_scores * (1.0 / math.sqrt(HEAD_DIM))
            prob_part = jnp.where(
                valid_mask[:, :, None, None, None], jnp.exp(part_scores - log_part[..., None]), 0.0
            )
            grad_prob = jnp.einsum(
                "abqhe,abkhe->abhqk", dout_heads, value_heads, preferred_element_type=jnp.float32
            )
            grad_score = (prob_part * (grad_prob - delta_part[..., None])).astype(jnp.bfloat16)
            grad_key = grad_key + jnp.einsum(
                "abhqk,abqhe->abkhe", grad_score, query_heads, preferred_element_type=jnp.float32
            )
            rounded_prob = prob_part.astype(jnp.bfloat16)
            grad_value = grad_value + jnp.einsum(
                "abhqk,abqhe->abkhe", rounded_prob, dout_heads, preferred_element_type=jnp.float32
            )
    out_shape = (block_rows, block_cols, BT, D)
    grad_key = (grad_key * (1.0 / math.sqrt(HEAD_DIM))).reshape(out_shape).astype(jnp.bfloat16)
    return (grad_key, grad_value.reshape(out_shape).astype(jnp.bfloat16))


def inner_rows(left_rows, right_rows):
    return lax.dot_general(
        left_rows, right_rows, (((0,), (0,)), ((), ())), preferred_element_type=jnp.float32
    )


def halving_steps(axes):
    steps = []
    for axis in axes:
        count = lax.axis_size(axis)
        stride = 1
        while stride < count:
            steps.append((axis, stride))
            stride *= 2
    return steps


def doubling_gather(joined, steps):
    for axis, stride in reversed(steps):
        pairs = [(i, i ^ stride) for i in range(lax.axis_size(axis))]
        bit = (lax.axis_index(axis) // stride) % 2
        got = lax.ppermute(joined, axis, pairs)
        low = jnp.where(bit == 0, joined, got)
        high = jnp.where(bit == 0, got, joined)
        joined = jnp.concatenate([low, high], 0)
    return joined


def tree_gather(block, axis):
    count = lax.axis_size(axis)
    if count & (count - 1):
        return lax.all_gather(block, axis, axis=0, tiled=True), lambda index: index
    width = count.bit_length() - 1

    def slot_of(index):
        return sum(((index >> bit) & 1) << (width - 1 - bit) for bit in range(width))

    return doubling_gather(block, halving_steps((axis,))), slot_of


def tree_sum(parts, axes):
    sizes = [lax.axis_size(axis) for axis in axes]
    rows = sum(part.shape[0] for part in parts)
    if any(size & (size - 1) for size in sizes) or rows % math.prod(sizes):
        return lax.psum(parts, axes)
    steps = halving_steps(axes)
    last = [step for step in steps if step[0] == axes[-1]]
    halving = steps[: len(steps) - len(last) + 1]
    doubling = steps[len(halving) :]
    joined = jnp.concatenate(parts, 0)
    for axis, stride in halving:
        pairs = [(i, i ^ stride) for i in range(lax.axis_size(axis))]
        bit = (lax.axis_index(axis) // stride) % 2
        half = joined.shape[0] // 2
        keep = lax.dynamic_slice_in_dim(joined, bit * half, half, 0)
        send = lax.dynamic_slice_in_dim(joined, (1 - bit) * half, half, 0)
        joined = keep + lax.ppermute(send, axis, pairs)
    for axis, stride in doubling:
        pairs = [(i, i ^ stride) for i in range(lax.axis_size(axis))]
        joined = joined + lax.ppermute(joined, axis, pairs)
    joined = doubling_gather(joined, halving)
    out = []
    start = 0
    for part in parts:
        out.append(joined[start : start + part.shape[0]])
        start += part.shape[0]
    return tuple(out)


def on_device(
    patches, w_query, w_key, w_value, w_out, region_memory, region_owner, region_local, grad_out
):
    tile_rows, tile_cols, model_width = patches.shape
    block_rows, block_cols = (tile_rows // BSIDE, tile_cols // BSIDE)
    block_count = block_rows * block_cols
    flat_in = patches.reshape(-1, model_width)
    w_pair = jnp.concatenate([w_key, w_value], 1)
    queries = jnp.dot(flat_in, w_query, preferred_element_type=jnp.float32).astype(jnp.bfloat16)
    keyvals = jnp.dot(flat_in, w_pair, preferred_element_type=jnp.float32).astype(jnp.bfloat16)
    keyvals = keyvals.reshape(tile_rows, tile_cols, 2 * model_width)
    keyval_grid = halo(keyvals, BSIDE)
    keyval_pad = to_blocks(keyval_grid)
    gx_count = lax.axis_size("gx")
    gy_count = lax.axis_size("gy")
    row_ids = lax.axis_index("gx") * block_rows - 1 + jnp.arange(block_rows + 2, dtype=jnp.int32)
    col_ids = lax.axis_index("gy") * block_cols - 1 + jnp.arange(block_cols + 2, dtype=jnp.int32)
    row_valid = (row_ids >= 0) & (row_ids < block_rows * gx_count)
    col_valid = (col_ids >= 0) & (col_ids < block_cols * gy_count)
    key_valid = row_valid[:, None] & col_valid[None, :]
    owners = region_owner.reshape(2 * block_count)
    local_ids = region_local.reshape(2 * block_count)
    memory_local = region_memory.reshape(
        region_memory.shape[2], region_memory.shape[3], region_memory.shape[4]
    )
    region_count = memory_local.shape[0]
    row_tables = lax.all_gather(memory_local, "gx", axis=0, tiled=True)
    fetched = jnp.take(row_tables, owners * region_count + local_ids, axis=0)
    region_keyval = fetched.reshape(
        block_rows, block_cols, 2, memory_local.shape[1], memory_local.shape[2]
    )
    query_blocks = to_blocks(queries.reshape(tile_rows, tile_cols, model_width))
    outputs, log_totals = attend_forward(query_blocks, keyval_pad, key_valid, region_keyval)
    attended = from_blocks(outputs).reshape(-1, model_width)
    layer_out = jnp.dot(attended, w_out, preferred_element_type=jnp.float32).astype(jnp.bfloat16)
    grad_flat = grad_out.reshape(-1, model_width)
    d_attended = jnp.dot(grad_flat, w_out.T, preferred_element_type=jnp.float32).astype(
        jnp.bfloat16
    )
    grad_out_local = inner_rows(attended, grad_flat)
    dout_blocks = to_blocks(d_attended.reshape(tile_rows, tile_cols, model_width))
    delta_rows = jnp.sum(
        split_heads(dout_blocks).astype(jnp.float32) * split_heads(outputs).astype(jnp.float32), -1
    )
    delta_rows = delta_rows.transpose(0, 1, 3, 2)
    d_queries = query_grads(
        query_blocks, keyval_pad, key_valid, region_keyval, log_totals, dout_blocks, delta_rows
    )
    query_grid = jnp.concatenate(
        [
            queries.reshape(tile_rows, tile_cols, model_width),
            d_attended.reshape(tile_rows, tile_cols, model_width),
        ],
        -1,
    )
    query_halo = halo(query_grid, BSIDE)
    stat_grid = from_blocks(jnp.concatenate([log_totals, delta_rows], 2).transpose(0, 1, 3, 2))
    stat_halo = halo(stat_grid, BSIDE)
    query_all = to_blocks(query_halo)
    stat_pad = to_blocks(stat_halo).transpose(0, 1, 3, 2)
    d_keys, d_values = key_grads(
        keyval_pad[1:-1, 1:-1],
        query_all[..., :model_width],
        query_all[..., model_width:],
        stat_pad[:, :, :HEADS],
        stat_pad[:, :, HEADS:],
        key_valid,
    )
    dq_flat = from_blocks(d_queries).reshape(-1, model_width)
    dk_flat = from_blocks(d_keys).reshape(-1, model_width)
    dv_flat = from_blocks(d_values).reshape(-1, model_width)
    grads_joined = jnp.concatenate([dq_flat, dk_flat, dv_flat], 1)
    w_stacked = jnp.concatenate([w_query.T, w_key.T, w_value.T], 0)
    grad_patches = jnp.dot(grads_joined, w_stacked, preferred_element_type=jnp.float32).astype(
        jnp.bfloat16
    )
    partials = (
        inner_rows(flat_in, dq_flat),
        inner_rows(flat_in, dk_flat),
        inner_rows(flat_in, dv_flat),
        grad_out_local,
    )
    summed = tree_sum(partials, ("gy", "gx"))
    return (
        layer_out.reshape(tile_rows, tile_cols, model_width),
        grad_patches.reshape(tile_rows, tile_cols, model_width),
        summed[0],
        summed[1],
        summed[2],
        summed[3],
    )


def solution(mesh):
    return jax.shard_map(
        on_device,
        mesh=mesh,
        in_specs=(
            P("gx", "gy", None),
            P(),
            P(),
            P(),
            P(),
            P("gx", "gy", None, None, None),
            P("gx", "gy", None, None),
            P("gx", "gy", None, None),
            P("gx", "gy", None),
        ),
        out_specs=(P("gx", "gy", None), P("gx", "gy", None), P(), P(), P(), P()),
        check_vma=False,
    )
```

```python
import math

import jax
import jax.numpy as jnp
from jax import lax
from jax.sharding import PartitionSpec as P

D = 256
HEADS = 2
HEAD_DIM = 128
BSIDE = 8
BT = 64


masked_score = -1000000000.0


def padded(block, sides, width):
    for axis, dim in sides:
        count = lax.axis_size(axis)
        forward = [(i, i + 1) for i in range(count - 1)]
        backward = [(target, source) for source, target in forward]
        low = lax.ppermute(
            lax.slice_in_dim(block, block.shape[dim] - width, None, axis=dim), axis, forward
        )
        high = lax.ppermute(lax.slice_in_dim(block, 0, width, axis=dim), axis, backward)
        block = jnp.concatenate([low, block, high], axis=dim)
    return block


def to_blocks(grid_array):
    grid_rows, grid_cols, feature_width = grid_array.shape
    shaped = grid_array.reshape(grid_rows // BSIDE, BSIDE, grid_cols // BSIDE, BSIDE, feature_width)
    return shaped.transpose(0, 2, 1, 3, 4).reshape(
        grid_rows // BSIDE, grid_cols // BSIDE, BSIDE * BSIDE, feature_width
    )


def from_blocks(block_array):
    block_rows, block_cols, block_tokens, feature_width = block_array.shape
    shaped = block_array.reshape(block_rows, block_cols, BSIDE, BSIDE, feature_width)
    return shaped.transpose(0, 2, 1, 3, 4).reshape(
        block_rows * BSIDE, block_cols * BSIDE, feature_width
    )


def split_heads(source):
    return source.reshape(source.shape[:-1] + (HEADS, source.shape[-1] // HEADS))


def key_pieces(keyval_pad, key_valid, region_keyval):
    block_rows, block_cols = (region_keyval.shape[0], region_keyval.shape[1])
    pieces = []
    for row_off in range(3):
        for col_off in range(3):
            key_block = keyval_pad[row_off : row_off + block_rows, col_off : col_off + block_cols]
            valid_mask = key_valid[row_off : row_off + block_rows, col_off : col_off + block_cols]
            pieces.append((key_block[..., :D], key_block[..., D:], valid_mask))
    merged = region_keyval.reshape(block_rows, block_cols, 2 * BT, 2 * D)
    pieces.append(
        (merged[..., :D], merged[..., D:], jnp.ones((block_rows, block_cols), dtype=jnp.bool_))
    )
    return pieces


def piece_scores(query_heads, key_part, valid_mask):
    scores = jnp.einsum(
        "abqhe,abkhe->abhqk", query_heads, split_heads(key_part), preferred_element_type=jnp.float32
    )
    scores = scores * (1.0 / math.sqrt(HEAD_DIM))
    return jnp.where(valid_mask[:, :, None, None, None], scores, masked_score)


def attend_forward(query_blocks, keyval_pad, key_valid, region_keyval):
    query_heads = split_heads(query_blocks)
    pieces = key_pieces(keyval_pad, key_valid, region_keyval)
    scores = [
        piece_scores(query_heads, key_part, valid_mask)
        for key_part, value_part, valid_mask in pieces
    ]
    row_top = jnp.max(jnp.concatenate(scores, -1), -1, keepdims=True)
    row_total = sum(
        (jnp.sum(jnp.exp(part_scores - row_top), -1, keepdims=True) for part_scores in scores)
    )
    log_total = row_top + jnp.log(row_total)
    mixed_sum = jnp.zeros(query_heads.shape, jnp.float32)
    for part_scores, (key_part, value_part, valid_mask) in zip(scores, pieces):
        weights = jnp.exp(part_scores - log_total).astype(jnp.bfloat16)
        mixed_sum = mixed_sum + jnp.einsum(
            "abhqk,abkhe->abqhe",
            weights,
            split_heads(value_part),
            preferred_element_type=jnp.float32,
        )
    output = mixed_sum.reshape(query_blocks.shape).astype(jnp.bfloat16)
    return (output, log_total[..., 0])


def query_grads(
    query_blocks, keyval_pad, key_valid, region_keyval, log_total, dout_blocks, delta_rows
):
    query_heads = split_heads(query_blocks)
    dout_heads = split_heads(dout_blocks)
    accum_sum = jnp.zeros(query_heads.shape, jnp.float32)
    for key_part, value_part, valid_mask in key_pieces(keyval_pad, key_valid, region_keyval):
        part_scores = piece_scores(query_heads, key_part, valid_mask)
        prob_part = jnp.exp(part_scores - log_total[..., None])
        grad_prob = jnp.einsum(
            "abqhe,abkhe->abhqk",
            dout_heads,
            split_heads(value_part),
            preferred_element_type=jnp.float32,
        )
        grad_score = (prob_part * (grad_prob - delta_rows[..., None])).astype(jnp.bfloat16)
        accum_sum = accum_sum + jnp.einsum(
            "abhqk,abkhe->abqhe",
            grad_score,
            split_heads(key_part),
            preferred_element_type=jnp.float32,
        )
    return (
        (accum_sum * (1.0 / math.sqrt(HEAD_DIM))).reshape(query_blocks.shape).astype(jnp.bfloat16)
    )


def key_grads(keyval_center, query_pad, dout_pad, log_pad, delta_pad, query_valid):
    block_rows, block_cols = (keyval_center.shape[0], keyval_center.shape[1])
    key_heads = split_heads(keyval_center[..., :D])
    value_heads = split_heads(keyval_center[..., D:])
    grad_key = jnp.zeros(key_heads.shape, jnp.float32)
    grad_value = jnp.zeros(key_heads.shape, jnp.float32)
    for row_off in range(3):
        for col_off in range(3):
            query_heads = split_heads(
                query_pad[row_off : row_off + block_rows, col_off : col_off + block_cols]
            )
            dout_heads = split_heads(
                dout_pad[row_off : row_off + block_rows, col_off : col_off + block_cols]
            )
            log_part = log_pad[row_off : row_off + block_rows, col_off : col_off + block_cols]
            delta_part = delta_pad[row_off : row_off + block_rows, col_off : col_off + block_cols]
            valid_mask = query_valid[row_off : row_off + block_rows, col_off : col_off + block_cols]
            part_scores = jnp.einsum(
                "abqhe,abkhe->abhqk", query_heads, key_heads, preferred_element_type=jnp.float32
            )
            part_scores = part_scores * (1.0 / math.sqrt(HEAD_DIM))
            prob_part = jnp.where(
                valid_mask[:, :, None, None, None], jnp.exp(part_scores - log_part[..., None]), 0.0
            )
            grad_prob = jnp.einsum(
                "abqhe,abkhe->abhqk", dout_heads, value_heads, preferred_element_type=jnp.float32
            )
            grad_score = (prob_part * (grad_prob - delta_part[..., None])).astype(jnp.bfloat16)
            grad_key = grad_key + jnp.einsum(
                "abhqk,abqhe->abkhe", grad_score, query_heads, preferred_element_type=jnp.float32
            )
            rounded_prob = prob_part.astype(jnp.bfloat16)
            grad_value = grad_value + jnp.einsum(
                "abhqk,abqhe->abkhe", rounded_prob, dout_heads, preferred_element_type=jnp.float32
            )
    out_shape = (block_rows, block_cols, BT, D)
    grad_key = (grad_key * (1.0 / math.sqrt(HEAD_DIM))).reshape(out_shape).astype(jnp.bfloat16)
    return (grad_key, grad_value.reshape(out_shape).astype(jnp.bfloat16))


def inner_rows(left_rows, right_rows):
    return lax.dot_general(
        left_rows, right_rows, (((0,), (0,)), ((), ())), preferred_element_type=jnp.float32
    )


def halving_steps(axes):
    steps = []
    for axis in axes:
        count = lax.axis_size(axis)
        stride = 1
        while stride < count:
            steps.append((axis, stride))
            stride *= 2
    return steps


def doubling_gather(joined, steps):
    for axis, stride in reversed(steps):
        pairs = [(i, i ^ stride) for i in range(lax.axis_size(axis))]
        bit = (lax.axis_index(axis) // stride) % 2
        got = lax.ppermute(joined, axis, pairs)
        low = jnp.where(bit == 0, joined, got)
        high = jnp.where(bit == 0, got, joined)
        joined = jnp.concatenate([low, high], 0)
    return joined


def tree_gather(block, axis):
    count = lax.axis_size(axis)
    if count & (count - 1):
        return lax.all_gather(block, axis, axis=0, tiled=True), lambda index: index
    width = count.bit_length() - 1

    def slot_of(index):
        return sum(((index >> bit) & 1) << (width - 1 - bit) for bit in range(width))

    return doubling_gather(block, halving_steps((axis,))), slot_of


def tree_sum(parts, axes):
    sizes = [lax.axis_size(axis) for axis in axes]
    rows = sum(part.shape[0] for part in parts)
    if any(size & (size - 1) for size in sizes) or rows % math.prod(sizes):
        return lax.psum(parts, axes)
    steps = halving_steps(axes)
    last = [step for step in steps if step[0] == axes[-1]]
    halving = steps[: len(steps) - len(last) + 1]
    doubling = steps[len(halving) :]
    joined = jnp.concatenate(parts, 0)
    for axis, stride in halving:
        pairs = [(i, i ^ stride) for i in range(lax.axis_size(axis))]
        bit = (lax.axis_index(axis) // stride) % 2
        half = joined.shape[0] // 2
        keep = lax.dynamic_slice_in_dim(joined, bit * half, half, 0)
        send = lax.dynamic_slice_in_dim(joined, (1 - bit) * half, half, 0)
        joined = keep + lax.ppermute(send, axis, pairs)
    for axis, stride in doubling:
        pairs = [(i, i ^ stride) for i in range(lax.axis_size(axis))]
        joined = joined + lax.ppermute(joined, axis, pairs)
    joined = doubling_gather(joined, halving)
    out = []
    start = 0
    for part in parts:
        out.append(joined[start : start + part.shape[0]])
        start += part.shape[0]
    return tuple(out)


def on_device(
    patches, w_query, w_key, w_value, w_out, region_memory, region_owner, region_local, grad_out
):
    tile_rows, tile_cols, model_width = patches.shape
    block_rows, block_cols = (tile_rows // BSIDE, tile_cols // BSIDE)
    block_count = block_rows * block_cols
    flat_in = patches.reshape(-1, model_width)
    w_pair = jnp.concatenate([w_key, w_value], 1)
    queries = jnp.dot(flat_in, w_query, preferred_element_type=jnp.float32).astype(jnp.bfloat16)
    keyvals = jnp.dot(flat_in, w_pair, preferred_element_type=jnp.float32).astype(jnp.bfloat16)
    keyvals = keyvals.reshape(tile_rows, tile_cols, 2 * model_width)
    keyval_grid = padded(keyvals, (("gx", 0), ("gy", 1)), BSIDE)
    keyval_pad = to_blocks(keyval_grid)
    gx_count = lax.axis_size("gx")
    gy_count = lax.axis_size("gy")
    row_ids = lax.axis_index("gx") * block_rows - 1 + jnp.arange(block_rows + 2, dtype=jnp.int32)
    col_ids = lax.axis_index("gy") * block_cols - 1 + jnp.arange(block_cols + 2, dtype=jnp.int32)
    row_valid = (row_ids >= 0) & (row_ids < block_rows * gx_count)
    col_valid = (col_ids >= 0) & (col_ids < block_cols * gy_count)
    key_valid = row_valid[:, None] & col_valid[None, :]
    owners = region_owner.reshape(2 * block_count)
    local_ids = region_local.reshape(2 * block_count)
    memory_local = region_memory.reshape(
        region_memory.shape[2], region_memory.shape[3], region_memory.shape[4]
    )
    region_count = memory_local.shape[0]
    row_tables = lax.all_gather(memory_local, "gx", axis=0, tiled=True)
    grad_flat = grad_out.reshape(-1, model_width)
    d_attended = jnp.dot(grad_flat, w_out.T, preferred_element_type=jnp.float32).astype(
        jnp.bfloat16
    )
    query_grid = jnp.concatenate(
        [
            queries.reshape(tile_rows, tile_cols, model_width),
            d_attended.reshape(tile_rows, tile_cols, model_width),
        ],
        -1,
    )
    query_halo = padded(query_grid, (("gx", 0), ("gy", 1)), BSIDE)
    row_tables, query_halo = lax.optimization_barrier((row_tables, query_halo))
    fetched = jnp.take(row_tables, owners * region_count + local_ids, axis=0)
    region_keyval = fetched.reshape(
        block_rows, block_cols, 2, memory_local.shape[1], memory_local.shape[2]
    )
    query_blocks = to_blocks(queries.reshape(tile_rows, tile_cols, model_width))
    outputs, log_totals = attend_forward(query_blocks, keyval_pad, key_valid, region_keyval)
    attended = from_blocks(outputs).reshape(-1, model_width)
    layer_out = jnp.dot(attended, w_out, preferred_element_type=jnp.float32).astype(jnp.bfloat16)
    grad_out_local = inner_rows(attended, grad_flat)
    dout_blocks = to_blocks(d_attended.reshape(tile_rows, tile_cols, model_width))
    delta_rows = jnp.sum(
        split_heads(dout_blocks).astype(jnp.float32) * split_heads(outputs).astype(jnp.float32), -1
    )
    delta_rows = delta_rows.transpose(0, 1, 3, 2)
    d_queries = query_grads(
        query_blocks, keyval_pad, key_valid, region_keyval, log_totals, dout_blocks, delta_rows
    )
    stat_grid = from_blocks(jnp.concatenate([log_totals, delta_rows], 2).transpose(0, 1, 3, 2))
    stat_halo = padded(stat_grid, (("gx", 0), ("gy", 1)), BSIDE)
    query_all = to_blocks(query_halo)
    stat_pad = to_blocks(stat_halo).transpose(0, 1, 3, 2)
    d_keys, d_values = key_grads(
        keyval_pad[1:-1, 1:-1],
        query_all[..., :model_width],
        query_all[..., model_width:],
        stat_pad[:, :, :HEADS],
        stat_pad[:, :, HEADS:],
        key_valid,
    )
    dq_flat = from_blocks(d_queries).reshape(-1, model_width)
    dk_flat = from_blocks(d_keys).reshape(-1, model_width)
    dv_flat = from_blocks(d_values).reshape(-1, model_width)
    grads_joined = jnp.concatenate([dq_flat, dk_flat, dv_flat], 1)
    w_stacked = jnp.concatenate([w_query.T, w_key.T, w_value.T], 0)
    grad_patches = jnp.dot(grads_joined, w_stacked, preferred_element_type=jnp.float32).astype(
        jnp.bfloat16
    )
    partials = (
        inner_rows(flat_in, dq_flat),
        inner_rows(flat_in, dk_flat),
        inner_rows(flat_in, dv_flat),
        grad_out_local,
    )
    summed = tree_sum(partials, ("gy", "gx"))
    return (
        layer_out.reshape(tile_rows, tile_cols, model_width),
        grad_patches.reshape(tile_rows, tile_cols, model_width),
        summed[0],
        summed[1],
        summed[2],
        summed[3],
    )


def solution(mesh):
    return jax.shard_map(
        on_device,
        mesh=mesh,
        in_specs=(
            P("gx", "gy", None),
            P(),
            P(),
            P(),
            P(),
            P("gx", "gy", None, None, None),
            P("gx", "gy", None, None),
            P("gx", "gy", None, None),
            P("gx", "gy", None),
        ),
        out_specs=(P("gx", "gy", None), P("gx", "gy", None), P(), P(), P(), P()),
        check_vma=False,
    )
```

```python
import math

import jax
import jax.numpy as jnp
from jax import lax
from jax.sharding import PartitionSpec as P

D = 256
HEADS = 2
HEAD_DIM = 128
BSIDE = 8
BT = 64
CAP = 2


masked_score = -1000000000.0


def padded(block, sides, width):
    for axis, dim in sides:
        count = lax.axis_size(axis)
        forward = [(i, i + 1) for i in range(count - 1)]
        backward = [(target, source) for source, target in forward]
        low = lax.ppermute(
            lax.slice_in_dim(block, block.shape[dim] - width, None, axis=dim), axis, forward
        )
        high = lax.ppermute(lax.slice_in_dim(block, 0, width, axis=dim), axis, backward)
        block = jnp.concatenate([low, block, high], axis=dim)
    return block


def to_blocks(grid_array):
    grid_rows, grid_cols, feature_width = grid_array.shape
    shaped = grid_array.reshape(grid_rows // BSIDE, BSIDE, grid_cols // BSIDE, BSIDE, feature_width)
    return shaped.transpose(0, 2, 1, 3, 4).reshape(
        grid_rows // BSIDE, grid_cols // BSIDE, BSIDE * BSIDE, feature_width
    )


def from_blocks(block_array):
    block_rows, block_cols, block_tokens, feature_width = block_array.shape
    shaped = block_array.reshape(block_rows, block_cols, BSIDE, BSIDE, feature_width)
    return shaped.transpose(0, 2, 1, 3, 4).reshape(
        block_rows * BSIDE, block_cols * BSIDE, feature_width
    )


def split_heads(source):
    return source.reshape(source.shape[:-1] + (HEADS, source.shape[-1] // HEADS))


def key_pieces(keyval_pad, key_valid, region_keyval):
    block_rows, block_cols = (region_keyval.shape[0], region_keyval.shape[1])
    pieces = []
    for row_off in range(3):
        for col_off in range(3):
            key_block = keyval_pad[row_off : row_off + block_rows, col_off : col_off + block_cols]
            valid_mask = key_valid[row_off : row_off + block_rows, col_off : col_off + block_cols]
            pieces.append((key_block[..., :D], key_block[..., D:], valid_mask))
    merged = region_keyval.reshape(block_rows, block_cols, 2 * BT, 2 * D)
    pieces.append(
        (merged[..., :D], merged[..., D:], jnp.ones((block_rows, block_cols), dtype=jnp.bool_))
    )
    return pieces


def piece_scores(query_heads, key_part, valid_mask):
    scores = jnp.einsum(
        "abqhe,abkhe->abhqk", query_heads, split_heads(key_part), preferred_element_type=jnp.float32
    )
    scores = scores * (1.0 / math.sqrt(HEAD_DIM))
    return jnp.where(valid_mask[:, :, None, None, None], scores, masked_score)


def attend_forward(query_blocks, keyval_pad, key_valid, region_keyval):
    query_heads = split_heads(query_blocks)
    pieces = key_pieces(keyval_pad, key_valid, region_keyval)
    scores = [
        piece_scores(query_heads, key_part, valid_mask)
        for key_part, value_part, valid_mask in pieces
    ]
    row_top = jnp.max(jnp.concatenate(scores, -1), -1, keepdims=True)
    row_total = sum(
        (jnp.sum(jnp.exp(part_scores - row_top), -1, keepdims=True) for part_scores in scores)
    )
    log_total = row_top + jnp.log(row_total)
    mixed_sum = jnp.zeros(query_heads.shape, jnp.float32)
    for part_scores, (key_part, value_part, valid_mask) in zip(scores, pieces):
        weights = jnp.exp(part_scores - log_total).astype(jnp.bfloat16)
        mixed_sum = mixed_sum + jnp.einsum(
            "abhqk,abkhe->abqhe",
            weights,
            split_heads(value_part),
            preferred_element_type=jnp.float32,
        )
    output = mixed_sum.reshape(query_blocks.shape).astype(jnp.bfloat16)
    return (output, log_total[..., 0])


def query_grads(
    query_blocks, keyval_pad, key_valid, region_keyval, log_total, dout_blocks, delta_rows
):
    query_heads = split_heads(query_blocks)
    dout_heads = split_heads(dout_blocks)
    accum_sum = jnp.zeros(query_heads.shape, jnp.float32)
    for key_part, value_part, valid_mask in key_pieces(keyval_pad, key_valid, region_keyval):
        part_scores = piece_scores(query_heads, key_part, valid_mask)
        prob_part = jnp.exp(part_scores - log_total[..., None])
        grad_prob = jnp.einsum(
            "abqhe,abkhe->abhqk",
            dout_heads,
            split_heads(value_part),
            preferred_element_type=jnp.float32,
        )
        grad_score = (prob_part * (grad_prob - delta_rows[..., None])).astype(jnp.bfloat16)
        accum_sum = accum_sum + jnp.einsum(
            "abhqk,abkhe->abqhe",
            grad_score,
            split_heads(key_part),
            preferred_element_type=jnp.float32,
        )
    return (
        (accum_sum * (1.0 / math.sqrt(HEAD_DIM))).reshape(query_blocks.shape).astype(jnp.bfloat16)
    )


def key_grads(keyval_center, query_pad, dout_pad, log_pad, delta_pad, query_valid):
    block_rows, block_cols = (keyval_center.shape[0], keyval_center.shape[1])
    key_heads = split_heads(keyval_center[..., :D])
    value_heads = split_heads(keyval_center[..., D:])
    grad_key = jnp.zeros(key_heads.shape, jnp.float32)
    grad_value = jnp.zeros(key_heads.shape, jnp.float32)
    for row_off in range(3):
        for col_off in range(3):
            query_heads = split_heads(
                query_pad[row_off : row_off + block_rows, col_off : col_off + block_cols]
            )
            dout_heads = split_heads(
                dout_pad[row_off : row_off + block_rows, col_off : col_off + block_cols]
            )
            log_part = log_pad[row_off : row_off + block_rows, col_off : col_off + block_cols]
            delta_part = delta_pad[row_off : row_off + block_rows, col_off : col_off + block_cols]
            valid_mask = query_valid[row_off : row_off + block_rows, col_off : col_off + block_cols]
            part_scores = jnp.einsum(
                "abqhe,abkhe->abhqk", query_heads, key_heads, preferred_element_type=jnp.float32
            )
            part_scores = part_scores * (1.0 / math.sqrt(HEAD_DIM))
            prob_part = jnp.where(
                valid_mask[:, :, None, None, None], jnp.exp(part_scores - log_part[..., None]), 0.0
            )
            grad_prob = jnp.einsum(
                "abqhe,abkhe->abhqk", dout_heads, value_heads, preferred_element_type=jnp.float32
            )
            grad_score = (prob_part * (grad_prob - delta_part[..., None])).astype(jnp.bfloat16)
            grad_key = grad_key + jnp.einsum(
                "abhqk,abqhe->abkhe", grad_score, query_heads, preferred_element_type=jnp.float32
            )
            rounded_prob = prob_part.astype(jnp.bfloat16)
            grad_value = grad_value + jnp.einsum(
                "abhqk,abqhe->abkhe", rounded_prob, dout_heads, preferred_element_type=jnp.float32
            )
    out_shape = (block_rows, block_cols, BT, D)
    grad_key = (grad_key * (1.0 / math.sqrt(HEAD_DIM))).reshape(out_shape).astype(jnp.bfloat16)
    return (grad_key, grad_value.reshape(out_shape).astype(jnp.bfloat16))


def inner_rows(left_rows, right_rows):
    return lax.dot_general(
        left_rows, right_rows, (((0,), (0,)), ((), ())), preferred_element_type=jnp.float32
    )


def halving_steps(axes):
    steps = []
    for axis in axes:
        count = lax.axis_size(axis)
        stride = 1
        while stride < count:
            steps.append((axis, stride))
            stride *= 2
    return steps


def doubling_gather(joined, steps):
    for axis, stride in reversed(steps):
        pairs = [(i, i ^ stride) for i in range(lax.axis_size(axis))]
        bit = (lax.axis_index(axis) // stride) % 2
        got = lax.ppermute(joined, axis, pairs)
        low = jnp.where(bit == 0, joined, got)
        high = jnp.where(bit == 0, got, joined)
        joined = jnp.concatenate([low, high], 0)
    return joined


def tree_gather(block, axis):
    count = lax.axis_size(axis)
    if count & (count - 1):
        return lax.all_gather(block, axis, axis=0, tiled=True), lambda index: index
    width = count.bit_length() - 1

    def slot_of(index):
        return sum(((index >> bit) & 1) << (width - 1 - bit) for bit in range(width))

    return doubling_gather(block, halving_steps((axis,))), slot_of


def tree_sum(parts, axes):
    sizes = [lax.axis_size(axis) for axis in axes]
    rows = sum(part.shape[0] for part in parts)
    if any(size & (size - 1) for size in sizes) or rows % math.prod(sizes):
        return lax.psum(parts, axes)
    steps = halving_steps(axes)
    last = [step for step in steps if step[0] == axes[-1]]
    halving = steps[: len(steps) - len(last) + 1]
    doubling = steps[len(halving) :]
    joined = jnp.concatenate(parts, 0)
    for axis, stride in halving:
        pairs = [(i, i ^ stride) for i in range(lax.axis_size(axis))]
        bit = (lax.axis_index(axis) // stride) % 2
        half = joined.shape[0] // 2
        keep = lax.dynamic_slice_in_dim(joined, bit * half, half, 0)
        send = lax.dynamic_slice_in_dim(joined, (1 - bit) * half, half, 0)
        joined = keep + lax.ppermute(send, axis, pairs)
    for axis, stride in doubling:
        pairs = [(i, i ^ stride) for i in range(lax.axis_size(axis))]
        joined = joined + lax.ppermute(joined, axis, pairs)
    joined = doubling_gather(joined, halving)
    out = []
    start = 0
    for part in parts:
        out.append(joined[start : start + part.shape[0]])
        start += part.shape[0]
    return tuple(out)


def fetch_regions(memory_local, owners, local_ids, axis):
    count = lax.axis_size(axis)
    entries = owners.shape[0]
    order = jnp.arange(entries)
    same = owners[:, None] == owners[None, :]
    rank = jnp.sum(same & (order[None, :] < order[:, None]), axis=1)
    wanted = (owners[:, None, None] == jnp.arange(count)[None, :, None]) & (
        rank[:, None, None] == jnp.arange(CAP)[None, None, :]
    )
    requests = jnp.sum(jnp.where(wanted, local_ids[:, None, None], 0), axis=0)
    asked = lax.all_to_all(requests, axis, 0, 0, tiled=True)
    sent = jnp.take(memory_local, asked.reshape(-1), axis=0)
    sent = sent.reshape((count, CAP) + memory_local.shape[1:])
    received = lax.all_to_all(sent, axis, 0, 0, tiled=True)
    received = received.reshape((count * CAP,) + memory_local.shape[1:])
    return jnp.take(received, owners * CAP + rank, axis=0)


def on_device(
    patches, w_query, w_key, w_value, w_out, region_memory, region_owner, region_local, grad_out
):
    tile_rows, tile_cols, model_width = patches.shape
    block_rows, block_cols = (tile_rows // BSIDE, tile_cols // BSIDE)
    block_count = block_rows * block_cols
    flat_in = patches.reshape(-1, model_width)
    w_pair = jnp.concatenate([w_key, w_value], 1)
    queries = jnp.dot(flat_in, w_query, preferred_element_type=jnp.float32).astype(jnp.bfloat16)
    keyvals = jnp.dot(flat_in, w_pair, preferred_element_type=jnp.float32).astype(jnp.bfloat16)
    keyvals = keyvals.reshape(tile_rows, tile_cols, 2 * model_width)
    keyval_grid = padded(keyvals, (("gx", 0), ("gy", 1)), BSIDE)
    keyval_pad = to_blocks(keyval_grid)
    gx_count = lax.axis_size("gx")
    gy_count = lax.axis_size("gy")
    row_ids = lax.axis_index("gx") * block_rows - 1 + jnp.arange(block_rows + 2, dtype=jnp.int32)
    col_ids = lax.axis_index("gy") * block_cols - 1 + jnp.arange(block_cols + 2, dtype=jnp.int32)
    row_valid = (row_ids >= 0) & (row_ids < block_rows * gx_count)
    col_valid = (col_ids >= 0) & (col_ids < block_cols * gy_count)
    key_valid = row_valid[:, None] & col_valid[None, :]
    owners = region_owner.reshape(2 * block_count)
    local_ids = region_local.reshape(2 * block_count)
    memory_local = region_memory.reshape(
        region_memory.shape[2], region_memory.shape[3], region_memory.shape[4]
    )
    fetched = fetch_regions(memory_local, owners, local_ids, "gx")
    region_keyval = fetched.reshape(
        block_rows, block_cols, 2, memory_local.shape[1], memory_local.shape[2]
    )
    query_blocks = to_blocks(queries.reshape(tile_rows, tile_cols, model_width))
    outputs, log_totals = attend_forward(query_blocks, keyval_pad, key_valid, region_keyval)
    attended = from_blocks(outputs).reshape(-1, model_width)
    layer_out = jnp.dot(attended, w_out, preferred_element_type=jnp.float32).astype(jnp.bfloat16)
    grad_flat = grad_out.reshape(-1, model_width)
    d_attended = jnp.dot(grad_flat, w_out.T, preferred_element_type=jnp.float32).astype(
        jnp.bfloat16
    )
    grad_out_local = inner_rows(attended, grad_flat)
    dout_blocks = to_blocks(d_attended.reshape(tile_rows, tile_cols, model_width))
    delta_rows = jnp.sum(
        split_heads(dout_blocks).astype(jnp.float32) * split_heads(outputs).astype(jnp.float32), -1
    )
    delta_rows = delta_rows.transpose(0, 1, 3, 2)
    d_queries = query_grads(
        query_blocks, keyval_pad, key_valid, region_keyval, log_totals, dout_blocks, delta_rows
    )
    query_grid = jnp.concatenate(
        [
            queries.reshape(tile_rows, tile_cols, model_width),
            d_attended.reshape(tile_rows, tile_cols, model_width),
        ],
        -1,
    )
    query_halo = padded(query_grid, (("gx", 0), ("gy", 1)), BSIDE)
    stat_grid = from_blocks(jnp.concatenate([log_totals, delta_rows], 2).transpose(0, 1, 3, 2))
    stat_halo = padded(stat_grid, (("gx", 0), ("gy", 1)), BSIDE)
    query_all = to_blocks(query_halo)
    stat_pad = to_blocks(stat_halo).transpose(0, 1, 3, 2)
    d_keys, d_values = key_grads(
        keyval_pad[1:-1, 1:-1],
        query_all[..., :model_width],
        query_all[..., model_width:],
        stat_pad[:, :, :HEADS],
        stat_pad[:, :, HEADS:],
        key_valid,
    )
    dq_flat = from_blocks(d_queries).reshape(-1, model_width)
    dk_flat = from_blocks(d_keys).reshape(-1, model_width)
    dv_flat = from_blocks(d_values).reshape(-1, model_width)
    grads_joined = jnp.concatenate([dq_flat, dk_flat, dv_flat], 1)
    w_stacked = jnp.concatenate([w_query.T, w_key.T, w_value.T], 0)
    grad_patches = jnp.dot(grads_joined, w_stacked, preferred_element_type=jnp.float32).astype(
        jnp.bfloat16
    )
    partials = (
        inner_rows(flat_in, dq_flat),
        inner_rows(flat_in, dk_flat),
        inner_rows(flat_in, dv_flat),
        grad_out_local,
    )
    summed = tree_sum(partials, ("gy", "gx"))
    return (
        layer_out.reshape(tile_rows, tile_cols, model_width),
        grad_patches.reshape(tile_rows, tile_cols, model_width),
        summed[0],
        summed[1],
        summed[2],
        summed[3],
    )


def solution(mesh):
    return jax.shard_map(
        on_device,
        mesh=mesh,
        in_specs=(
            P("gx", "gy", None),
            P(),
            P(),
            P(),
            P(),
            P("gx", "gy", None, None, None),
            P("gx", "gy", None, None),
            P("gx", "gy", None, None),
            P("gx", "gy", None),
        ),
        out_specs=(P("gx", "gy", None), P("gx", "gy", None), P(), P(), P(), P()),
        check_vma=False,
    )
```

```python
import math

import jax
import jax.numpy as jnp
from jax import lax
from jax.sharding import PartitionSpec as P

D = 256
HEADS = 2
HEAD_DIM = 128
BSIDE = 8
BT = 64
CAP = 2


masked_score = -1000000000.0


def padded(block, sides, width):
    for axis, dim in sides:
        count = lax.axis_size(axis)
        forward = [(i, i + 1) for i in range(count - 1)]
        backward = [(target, source) for source, target in forward]
        low = lax.ppermute(
            lax.slice_in_dim(block, block.shape[dim] - width, None, axis=dim), axis, forward
        )
        high = lax.ppermute(lax.slice_in_dim(block, 0, width, axis=dim), axis, backward)
        block = jnp.concatenate([low, block, high], axis=dim)
    return block


def to_blocks(grid_array):
    grid_rows, grid_cols, feature_width = grid_array.shape
    shaped = grid_array.reshape(grid_rows // BSIDE, BSIDE, grid_cols // BSIDE, BSIDE, feature_width)
    return shaped.transpose(0, 2, 1, 3, 4).reshape(
        grid_rows // BSIDE, grid_cols // BSIDE, BSIDE * BSIDE, feature_width
    )


def from_blocks(block_array):
    block_rows, block_cols, block_tokens, feature_width = block_array.shape
    shaped = block_array.reshape(block_rows, block_cols, BSIDE, BSIDE, feature_width)
    return shaped.transpose(0, 2, 1, 3, 4).reshape(
        block_rows * BSIDE, block_cols * BSIDE, feature_width
    )


def split_heads(source):
    return source.reshape(source.shape[:-1] + (HEADS, source.shape[-1] // HEADS))


def key_pieces(keyval_pad, key_valid, region_keyval):
    block_rows, block_cols = (region_keyval.shape[0], region_keyval.shape[1])
    pieces = []
    for row_off in range(3):
        for col_off in range(3):
            key_block = keyval_pad[row_off : row_off + block_rows, col_off : col_off + block_cols]
            valid_mask = key_valid[row_off : row_off + block_rows, col_off : col_off + block_cols]
            pieces.append((key_block[..., :D], key_block[..., D:], valid_mask))
    merged = region_keyval.reshape(block_rows, block_cols, 2 * BT, 2 * D)
    pieces.append(
        (merged[..., :D], merged[..., D:], jnp.ones((block_rows, block_cols), dtype=jnp.bool_))
    )
    return pieces


def piece_scores(query_heads, key_part, valid_mask):
    scores = jnp.einsum(
        "abqhe,abkhe->abhqk", query_heads, split_heads(key_part), preferred_element_type=jnp.float32
    )
    scores = scores * (1.0 / math.sqrt(HEAD_DIM))
    return jnp.where(valid_mask[:, :, None, None, None], scores, masked_score)


def attend_forward(query_blocks, keyval_pad, key_valid, region_keyval):
    query_heads = split_heads(query_blocks)
    pieces = key_pieces(keyval_pad, key_valid, region_keyval)
    scores = [
        piece_scores(query_heads, key_part, valid_mask)
        for key_part, value_part, valid_mask in pieces
    ]
    row_top = jnp.max(jnp.concatenate(scores, -1), -1, keepdims=True)
    row_total = sum(
        (jnp.sum(jnp.exp(part_scores - row_top), -1, keepdims=True) for part_scores in scores)
    )
    log_total = row_top + jnp.log(row_total)
    mixed_sum = jnp.zeros(query_heads.shape, jnp.float32)
    for part_scores, (key_part, value_part, valid_mask) in zip(scores, pieces):
        weights = jnp.exp(part_scores - log_total).astype(jnp.bfloat16)
        mixed_sum = mixed_sum + jnp.einsum(
            "abhqk,abkhe->abqhe",
            weights,
            split_heads(value_part),
            preferred_element_type=jnp.float32,
        )
    output = mixed_sum.reshape(query_blocks.shape).astype(jnp.bfloat16)
    return (output, log_total[..., 0])


def query_grads(
    query_blocks, keyval_pad, key_valid, region_keyval, log_total, dout_blocks, delta_rows
):
    query_heads = split_heads(query_blocks)
    dout_heads = split_heads(dout_blocks)
    accum_sum = jnp.zeros(query_heads.shape, jnp.float32)
    for key_part, value_part, valid_mask in key_pieces(keyval_pad, key_valid, region_keyval):
        part_scores = piece_scores(query_heads, key_part, valid_mask)
        prob_part = jnp.exp(part_scores - log_total[..., None])
        grad_prob = jnp.einsum(
            "abqhe,abkhe->abhqk",
            dout_heads,
            split_heads(value_part),
            preferred_element_type=jnp.float32,
        )
        grad_score = (prob_part * (grad_prob - delta_rows[..., None])).astype(jnp.bfloat16)
        accum_sum = accum_sum + jnp.einsum(
            "abhqk,abkhe->abqhe",
            grad_score,
            split_heads(key_part),
            preferred_element_type=jnp.float32,
        )
    return (
        (accum_sum * (1.0 / math.sqrt(HEAD_DIM))).reshape(query_blocks.shape).astype(jnp.bfloat16)
    )


def key_grads(keyval_center, query_pad, dout_pad, log_pad, delta_pad, query_valid):
    block_rows, block_cols = (keyval_center.shape[0], keyval_center.shape[1])
    key_heads = split_heads(keyval_center[..., :D])
    value_heads = split_heads(keyval_center[..., D:])
    grad_key = jnp.zeros(key_heads.shape, jnp.float32)
    grad_value = jnp.zeros(key_heads.shape, jnp.float32)
    for row_off in range(3):
        for col_off in range(3):
            query_heads = split_heads(
                query_pad[row_off : row_off + block_rows, col_off : col_off + block_cols]
            )
            dout_heads = split_heads(
                dout_pad[row_off : row_off + block_rows, col_off : col_off + block_cols]
            )
            log_part = log_pad[row_off : row_off + block_rows, col_off : col_off + block_cols]
            delta_part = delta_pad[row_off : row_off + block_rows, col_off : col_off + block_cols]
            valid_mask = query_valid[row_off : row_off + block_rows, col_off : col_off + block_cols]
            part_scores = jnp.einsum(
                "abqhe,abkhe->abhqk", query_heads, key_heads, preferred_element_type=jnp.float32
            )
            part_scores = part_scores * (1.0 / math.sqrt(HEAD_DIM))
            prob_part = jnp.where(
                valid_mask[:, :, None, None, None], jnp.exp(part_scores - log_part[..., None]), 0.0
            )
            grad_prob = jnp.einsum(
                "abqhe,abkhe->abhqk", dout_heads, value_heads, preferred_element_type=jnp.float32
            )
            grad_score = (prob_part * (grad_prob - delta_part[..., None])).astype(jnp.bfloat16)
            grad_key = grad_key + jnp.einsum(
                "abhqk,abqhe->abkhe", grad_score, query_heads, preferred_element_type=jnp.float32
            )
            rounded_prob = prob_part.astype(jnp.bfloat16)
            grad_value = grad_value + jnp.einsum(
                "abhqk,abqhe->abkhe", rounded_prob, dout_heads, preferred_element_type=jnp.float32
            )
    out_shape = (block_rows, block_cols, BT, D)
    grad_key = (grad_key * (1.0 / math.sqrt(HEAD_DIM))).reshape(out_shape).astype(jnp.bfloat16)
    return (grad_key, grad_value.reshape(out_shape).astype(jnp.bfloat16))


def inner_rows(left_rows, right_rows):
    return lax.dot_general(
        left_rows, right_rows, (((0,), (0,)), ((), ())), preferred_element_type=jnp.float32
    )


def halving_steps(axes):
    steps = []
    for axis in axes:
        count = lax.axis_size(axis)
        stride = 1
        while stride < count:
            steps.append((axis, stride))
            stride *= 2
    return steps


def doubling_gather(joined, steps):
    for axis, stride in reversed(steps):
        pairs = [(i, i ^ stride) for i in range(lax.axis_size(axis))]
        bit = (lax.axis_index(axis) // stride) % 2
        got = lax.ppermute(joined, axis, pairs)
        low = jnp.where(bit == 0, joined, got)
        high = jnp.where(bit == 0, got, joined)
        joined = jnp.concatenate([low, high], 0)
    return joined


def tree_gather(block, axis):
    count = lax.axis_size(axis)
    if count & (count - 1):
        return lax.all_gather(block, axis, axis=0, tiled=True), lambda index: index
    width = count.bit_length() - 1

    def slot_of(index):
        return sum(((index >> bit) & 1) << (width - 1 - bit) for bit in range(width))

    return doubling_gather(block, halving_steps((axis,))), slot_of


def tree_sum(parts, axes):
    sizes = [lax.axis_size(axis) for axis in axes]
    rows = sum(part.shape[0] for part in parts)
    if any(size & (size - 1) for size in sizes) or rows % math.prod(sizes):
        return lax.psum(parts, axes)
    steps = halving_steps(axes)
    last = [step for step in steps if step[0] == axes[-1]]
    halving = steps[: len(steps) - len(last) + 1]
    doubling = steps[len(halving) :]
    joined = jnp.concatenate(parts, 0)
    for axis, stride in halving:
        pairs = [(i, i ^ stride) for i in range(lax.axis_size(axis))]
        bit = (lax.axis_index(axis) // stride) % 2
        half = joined.shape[0] // 2
        keep = lax.dynamic_slice_in_dim(joined, bit * half, half, 0)
        send = lax.dynamic_slice_in_dim(joined, (1 - bit) * half, half, 0)
        joined = keep + lax.ppermute(send, axis, pairs)
    for axis, stride in doubling:
        pairs = [(i, i ^ stride) for i in range(lax.axis_size(axis))]
        joined = joined + lax.ppermute(joined, axis, pairs)
    joined = doubling_gather(joined, halving)
    out = []
    start = 0
    for part in parts:
        out.append(joined[start : start + part.shape[0]])
        start += part.shape[0]
    return tuple(out)


def fetch_regions(memory_local, owners, local_ids, axis):
    count = lax.axis_size(axis)
    entries = owners.shape[0]
    me = lax.axis_index(axis)
    order = jnp.arange(entries)
    earlier = order[None, :] < order[:, None]
    tables, slot_of = tree_gather(jnp.stack([owners, local_ids])[None], axis)
    tables = tables[jnp.array([slot_of(device) for device in range(count)])]
    mine = tables[:, 0] == me
    rank_here = jnp.sum(mine[:, None, :] & earlier[None], axis=2)
    wanted = mine[:, :, None] & (rank_here[:, :, None] == jnp.arange(CAP)[None, None, :])
    asked = jnp.sum(jnp.where(wanted, tables[:, 1][:, :, None], 0), axis=1)
    sent = jnp.take(memory_local, asked.reshape(-1), axis=0)
    sent = sent.reshape((count, CAP) + memory_local.shape[1:])
    received = lax.all_to_all(sent, axis, 0, 0, tiled=True)
    received = received.reshape((count * CAP,) + memory_local.shape[1:])
    same = owners[:, None] == owners[None, :]
    rank = jnp.sum(same & earlier, axis=1)
    return jnp.take(received, owners * CAP + rank, axis=0)


def on_device(
    patches, w_query, w_key, w_value, w_out, region_memory, region_owner, region_local, grad_out
):
    tile_rows, tile_cols, model_width = patches.shape
    block_rows, block_cols = (tile_rows // BSIDE, tile_cols // BSIDE)
    block_count = block_rows * block_cols
    flat_in = patches.reshape(-1, model_width)
    w_pair = jnp.concatenate([w_key, w_value], 1)
    queries = jnp.dot(flat_in, w_query, preferred_element_type=jnp.float32).astype(jnp.bfloat16)
    keyvals = jnp.dot(flat_in, w_pair, preferred_element_type=jnp.float32).astype(jnp.bfloat16)
    keyvals = keyvals.reshape(tile_rows, tile_cols, 2 * model_width)
    keyval_grid = padded(keyvals, (("gx", 0), ("gy", 1)), BSIDE)
    keyval_pad = to_blocks(keyval_grid)
    gx_count = lax.axis_size("gx")
    gy_count = lax.axis_size("gy")
    row_ids = lax.axis_index("gx") * block_rows - 1 + jnp.arange(block_rows + 2, dtype=jnp.int32)
    col_ids = lax.axis_index("gy") * block_cols - 1 + jnp.arange(block_cols + 2, dtype=jnp.int32)
    row_valid = (row_ids >= 0) & (row_ids < block_rows * gx_count)
    col_valid = (col_ids >= 0) & (col_ids < block_cols * gy_count)
    key_valid = row_valid[:, None] & col_valid[None, :]
    owners = region_owner.reshape(2 * block_count)
    local_ids = region_local.reshape(2 * block_count)
    memory_local = region_memory.reshape(
        region_memory.shape[2], region_memory.shape[3], region_memory.shape[4]
    )
    fetched = fetch_regions(memory_local, owners, local_ids, "gx")
    region_keyval = fetched.reshape(
        block_rows, block_cols, 2, memory_local.shape[1], memory_local.shape[2]
    )
    query_blocks = to_blocks(queries.reshape(tile_rows, tile_cols, model_width))
    outputs, log_totals = attend_forward(query_blocks, keyval_pad, key_valid, region_keyval)
    attended = from_blocks(outputs).reshape(-1, model_width)
    layer_out = jnp.dot(attended, w_out, preferred_element_type=jnp.float32).astype(jnp.bfloat16)
    grad_flat = grad_out.reshape(-1, model_width)
    d_attended = jnp.dot(grad_flat, w_out.T, preferred_element_type=jnp.float32).astype(
        jnp.bfloat16
    )
    grad_out_local = inner_rows(attended, grad_flat)
    dout_blocks = to_blocks(d_attended.reshape(tile_rows, tile_cols, model_width))
    delta_rows = jnp.sum(
        split_heads(dout_blocks).astype(jnp.float32) * split_heads(outputs).astype(jnp.float32), -1
    )
    delta_rows = delta_rows.transpose(0, 1, 3, 2)
    d_queries = query_grads(
        query_blocks, keyval_pad, key_valid, region_keyval, log_totals, dout_blocks, delta_rows
    )
    query_grid = jnp.concatenate(
        [
            queries.reshape(tile_rows, tile_cols, model_width),
            d_attended.reshape(tile_rows, tile_cols, model_width),
        ],
        -1,
    )
    query_halo = padded(query_grid, (("gx", 0), ("gy", 1)), BSIDE)
    stat_grid = from_blocks(jnp.concatenate([log_totals, delta_rows], 2).transpose(0, 1, 3, 2))
    stat_halo = padded(stat_grid, (("gx", 0), ("gy", 1)), BSIDE)
    query_all = to_blocks(query_halo)
    stat_pad = to_blocks(stat_halo).transpose(0, 1, 3, 2)
    d_keys, d_values = key_grads(
        keyval_pad[1:-1, 1:-1],
        query_all[..., :model_width],
        query_all[..., model_width:],
        stat_pad[:, :, :HEADS],
        stat_pad[:, :, HEADS:],
        key_valid,
    )
    dq_flat = from_blocks(d_queries).reshape(-1, model_width)
    dk_flat = from_blocks(d_keys).reshape(-1, model_width)
    dv_flat = from_blocks(d_values).reshape(-1, model_width)
    grads_joined = jnp.concatenate([dq_flat, dk_flat, dv_flat], 1)
    w_stacked = jnp.concatenate([w_query.T, w_key.T, w_value.T], 0)
    grad_patches = jnp.dot(grads_joined, w_stacked, preferred_element_type=jnp.float32).astype(
        jnp.bfloat16
    )
    partials = (
        inner_rows(flat_in, dq_flat),
        inner_rows(flat_in, dk_flat),
        inner_rows(flat_in, dv_flat),
        grad_out_local,
    )
    summed = tree_sum(partials, ("gy", "gx"))
    return (
        layer_out.reshape(tile_rows, tile_cols, model_width),
        grad_patches.reshape(tile_rows, tile_cols, model_width),
        summed[0],
        summed[1],
        summed[2],
        summed[3],
    )


def solution(mesh):
    return jax.shard_map(
        on_device,
        mesh=mesh,
        in_specs=(
            P("gx", "gy", None),
            P(),
            P(),
            P(),
            P(),
            P("gx", "gy", None, None, None),
            P("gx", "gy", None, None),
            P("gx", "gy", None, None),
            P("gx", "gy", None),
        ),
        out_specs=(P("gx", "gy", None), P("gx", "gy", None), P(), P(), P(), P()),
        check_vma=False,
    )
```

```python
import math

import jax
import jax.numpy as jnp
from jax import lax
from jax.sharding import PartitionSpec as P

D = 256
HEADS = 2
HEAD_DIM = 128
BSIDE = 8
BT = 64
CAP = 2


masked_score = -1000000000.0


def padded(block, sides, width):
    for axis, dim in sides:
        count = lax.axis_size(axis)
        forward = [(i, i + 1) for i in range(count - 1)]
        backward = [(target, source) for source, target in forward]
        low = lax.ppermute(
            lax.slice_in_dim(block, block.shape[dim] - width, None, axis=dim), axis, forward
        )
        high = lax.ppermute(lax.slice_in_dim(block, 0, width, axis=dim), axis, backward)
        block = jnp.concatenate([low, block, high], axis=dim)
    return block


def to_blocks(grid_array):
    grid_rows, grid_cols, feature_width = grid_array.shape
    shaped = grid_array.reshape(grid_rows // BSIDE, BSIDE, grid_cols // BSIDE, BSIDE, feature_width)
    return shaped.transpose(0, 2, 1, 3, 4).reshape(
        grid_rows // BSIDE, grid_cols // BSIDE, BSIDE * BSIDE, feature_width
    )


def from_blocks(block_array):
    block_rows, block_cols, block_tokens, feature_width = block_array.shape
    shaped = block_array.reshape(block_rows, block_cols, BSIDE, BSIDE, feature_width)
    return shaped.transpose(0, 2, 1, 3, 4).reshape(
        block_rows * BSIDE, block_cols * BSIDE, feature_width
    )


def split_heads(source):
    return source.reshape(source.shape[:-1] + (HEADS, source.shape[-1] // HEADS))


def key_pieces(keyval_pad, key_valid, region_keyval):
    block_rows, block_cols = (region_keyval.shape[0], region_keyval.shape[1])
    pieces = []
    for row_off in range(3):
        for col_off in range(3):
            key_block = keyval_pad[row_off : row_off + block_rows, col_off : col_off + block_cols]
            valid_mask = key_valid[row_off : row_off + block_rows, col_off : col_off + block_cols]
            pieces.append((key_block[..., :D], key_block[..., D:], valid_mask))
    merged = region_keyval.reshape(block_rows, block_cols, 2 * BT, 2 * D)
    pieces.append(
        (merged[..., :D], merged[..., D:], jnp.ones((block_rows, block_cols), dtype=jnp.bool_))
    )
    return pieces


def piece_scores(query_heads, key_part, valid_mask):
    scores = jnp.einsum(
        "abqhe,abkhe->abhqk", query_heads, split_heads(key_part), preferred_element_type=jnp.float32
    )
    scores = scores * (1.0 / math.sqrt(HEAD_DIM))
    return jnp.where(valid_mask[:, :, None, None, None], scores, masked_score)


def attend_forward(query_blocks, keyval_pad, key_valid, region_keyval):
    query_heads = split_heads(query_blocks)
    pieces = key_pieces(keyval_pad, key_valid, region_keyval)
    scores = [
        piece_scores(query_heads, key_part, valid_mask)
        for key_part, value_part, valid_mask in pieces
    ]
    row_top = jnp.max(jnp.concatenate(scores, -1), -1, keepdims=True)
    row_total = sum(
        (jnp.sum(jnp.exp(part_scores - row_top), -1, keepdims=True) for part_scores in scores)
    )
    log_total = row_top + jnp.log(row_total)
    mixed_sum = jnp.zeros(query_heads.shape, jnp.float32)
    for part_scores, (key_part, value_part, valid_mask) in zip(scores, pieces):
        weights = jnp.exp(part_scores - log_total).astype(jnp.bfloat16)
        mixed_sum = mixed_sum + jnp.einsum(
            "abhqk,abkhe->abqhe",
            weights,
            split_heads(value_part),
            preferred_element_type=jnp.float32,
        )
    output = mixed_sum.reshape(query_blocks.shape).astype(jnp.bfloat16)
    return (output, log_total[..., 0])


def query_grads(
    query_blocks, keyval_pad, key_valid, region_keyval, log_total, dout_blocks, delta_rows
):
    query_heads = split_heads(query_blocks)
    dout_heads = split_heads(dout_blocks)
    accum_sum = jnp.zeros(query_heads.shape, jnp.float32)
    for key_part, value_part, valid_mask in key_pieces(keyval_pad, key_valid, region_keyval):
        part_scores = piece_scores(query_heads, key_part, valid_mask)
        prob_part = jnp.exp(part_scores - log_total[..., None])
        grad_prob = jnp.einsum(
            "abqhe,abkhe->abhqk",
            dout_heads,
            split_heads(value_part),
            preferred_element_type=jnp.float32,
        )
        grad_score = (prob_part * (grad_prob - delta_rows[..., None])).astype(jnp.bfloat16)
        accum_sum = accum_sum + jnp.einsum(
            "abhqk,abkhe->abqhe",
            grad_score,
            split_heads(key_part),
            preferred_element_type=jnp.float32,
        )
    return (
        (accum_sum * (1.0 / math.sqrt(HEAD_DIM))).reshape(query_blocks.shape).astype(jnp.bfloat16)
    )


def key_grads(keyval_center, query_pad, dout_pad, log_pad, delta_pad, query_valid):
    block_rows, block_cols = (keyval_center.shape[0], keyval_center.shape[1])
    key_heads = split_heads(keyval_center[..., :D])
    value_heads = split_heads(keyval_center[..., D:])
    grad_key = jnp.zeros(key_heads.shape, jnp.float32)
    grad_value = jnp.zeros(key_heads.shape, jnp.float32)
    for row_off in range(3):
        for col_off in range(3):
            query_heads = split_heads(
                query_pad[row_off : row_off + block_rows, col_off : col_off + block_cols]
            )
            dout_heads = split_heads(
                dout_pad[row_off : row_off + block_rows, col_off : col_off + block_cols]
            )
            log_part = log_pad[row_off : row_off + block_rows, col_off : col_off + block_cols]
            delta_part = delta_pad[row_off : row_off + block_rows, col_off : col_off + block_cols]
            valid_mask = query_valid[row_off : row_off + block_rows, col_off : col_off + block_cols]
            part_scores = jnp.einsum(
                "abqhe,abkhe->abhqk", query_heads, key_heads, preferred_element_type=jnp.float32
            )
            part_scores = part_scores * (1.0 / math.sqrt(HEAD_DIM))
            prob_part = jnp.where(
                valid_mask[:, :, None, None, None], jnp.exp(part_scores - log_part[..., None]), 0.0
            )
            grad_prob = jnp.einsum(
                "abqhe,abkhe->abhqk", dout_heads, value_heads, preferred_element_type=jnp.float32
            )
            grad_score = (prob_part * (grad_prob - delta_part[..., None])).astype(jnp.bfloat16)
            grad_key = grad_key + jnp.einsum(
                "abhqk,abqhe->abkhe", grad_score, query_heads, preferred_element_type=jnp.float32
            )
            rounded_prob = prob_part.astype(jnp.bfloat16)
            grad_value = grad_value + jnp.einsum(
                "abhqk,abqhe->abkhe", rounded_prob, dout_heads, preferred_element_type=jnp.float32
            )
    out_shape = (block_rows, block_cols, BT, D)
    grad_key = (grad_key * (1.0 / math.sqrt(HEAD_DIM))).reshape(out_shape).astype(jnp.bfloat16)
    return (grad_key, grad_value.reshape(out_shape).astype(jnp.bfloat16))


def inner_rows(left_rows, right_rows):
    return lax.dot_general(
        left_rows, right_rows, (((0,), (0,)), ((), ())), preferred_element_type=jnp.float32
    )


def halving_steps(axes):
    steps = []
    for axis in axes:
        count = lax.axis_size(axis)
        stride = 1
        while stride < count:
            steps.append((axis, stride))
            stride *= 2
    return steps


def doubling_gather(joined, steps):
    for axis, stride in reversed(steps):
        pairs = [(i, i ^ stride) for i in range(lax.axis_size(axis))]
        bit = (lax.axis_index(axis) // stride) % 2
        got = lax.ppermute(joined, axis, pairs)
        low = jnp.where(bit == 0, joined, got)
        high = jnp.where(bit == 0, got, joined)
        joined = jnp.concatenate([low, high], 0)
    return joined


def tree_gather(block, axis):
    count = lax.axis_size(axis)
    if count & (count - 1):
        return lax.all_gather(block, axis, axis=0, tiled=True), lambda index: index
    width = count.bit_length() - 1

    def slot_of(index):
        return sum(((index >> bit) & 1) << (width - 1 - bit) for bit in range(width))

    return doubling_gather(block, halving_steps((axis,))), slot_of


def tree_sum(parts, axes):
    sizes = [lax.axis_size(axis) for axis in axes]
    rows = sum(part.shape[0] for part in parts)
    if any(size & (size - 1) for size in sizes) or rows % math.prod(sizes):
        return lax.psum(parts, axes)
    steps = halving_steps(axes)
    last = [step for step in steps if step[0] == axes[-1]]
    halving = steps[: len(steps) - len(last) + 1]
    doubling = steps[len(halving) :]
    joined = jnp.concatenate(parts, 0)
    for axis, stride in halving:
        pairs = [(i, i ^ stride) for i in range(lax.axis_size(axis))]
        bit = (lax.axis_index(axis) // stride) % 2
        half = joined.shape[0] // 2
        keep = lax.dynamic_slice_in_dim(joined, bit * half, half, 0)
        send = lax.dynamic_slice_in_dim(joined, (1 - bit) * half, half, 0)
        joined = keep + lax.ppermute(send, axis, pairs)
    for axis, stride in doubling:
        pairs = [(i, i ^ stride) for i in range(lax.axis_size(axis))]
        joined = joined + lax.ppermute(joined, axis, pairs)
    joined = doubling_gather(joined, halving)
    out = []
    start = 0
    for part in parts:
        out.append(joined[start : start + part.shape[0]])
        start += part.shape[0]
    return tuple(out)


def fetch_regions(memory_local, owners, local_ids, axis, ready):
    count = lax.axis_size(axis)
    entries = owners.shape[0]
    me = lax.axis_index(axis)
    order = jnp.arange(entries)
    earlier = order[None, :] < order[:, None]
    tables, slot_of = tree_gather(jnp.stack([owners, local_ids])[None], axis)
    tables = tables[jnp.array([slot_of(device) for device in range(count)])]
    mine = tables[:, 0] == me
    rank_here = jnp.sum(mine[:, None, :] & earlier[None], axis=2)
    wanted = mine[:, :, None] & (rank_here[:, :, None] == jnp.arange(CAP)[None, None, :])
    asked = jnp.sum(jnp.where(wanted, tables[:, 1][:, :, None], 0), axis=1)
    sent = jnp.take(memory_local, asked.reshape(-1), axis=0)
    sent = sent.reshape((count, CAP) + memory_local.shape[1:])
    sent, ready = lax.optimization_barrier((sent, ready))
    received = lax.all_to_all(sent, axis, 0, 0, tiled=True)
    received = received.reshape((count * CAP,) + memory_local.shape[1:])
    same = owners[:, None] == owners[None, :]
    rank = jnp.sum(same & earlier, axis=1)
    return jnp.take(received, owners * CAP + rank, axis=0), ready


def on_device(
    patches, w_query, w_key, w_value, w_out, region_memory, region_owner, region_local, grad_out
):
    tile_rows, tile_cols, model_width = patches.shape
    block_rows, block_cols = (tile_rows // BSIDE, tile_cols // BSIDE)
    block_count = block_rows * block_cols
    flat_in = patches.reshape(-1, model_width)
    w_pair = jnp.concatenate([w_key, w_value], 1)
    queries = jnp.dot(flat_in, w_query, preferred_element_type=jnp.float32).astype(jnp.bfloat16)
    keyvals = jnp.dot(flat_in, w_pair, preferred_element_type=jnp.float32).astype(jnp.bfloat16)
    keyvals = keyvals.reshape(tile_rows, tile_cols, 2 * model_width)
    owners = region_owner.reshape(2 * block_count)
    local_ids = region_local.reshape(2 * block_count)
    memory_local = region_memory.reshape(
        region_memory.shape[2], region_memory.shape[3], region_memory.shape[4]
    )
    fetched, keyvals = fetch_regions(memory_local, owners, local_ids, "gx", keyvals)
    keyval_grid = padded(keyvals, (("gx", 0), ("gy", 1)), BSIDE)
    keyval_pad = to_blocks(keyval_grid)
    gx_count = lax.axis_size("gx")
    gy_count = lax.axis_size("gy")
    row_ids = lax.axis_index("gx") * block_rows - 1 + jnp.arange(block_rows + 2, dtype=jnp.int32)
    col_ids = lax.axis_index("gy") * block_cols - 1 + jnp.arange(block_cols + 2, dtype=jnp.int32)
    row_valid = (row_ids >= 0) & (row_ids < block_rows * gx_count)
    col_valid = (col_ids >= 0) & (col_ids < block_cols * gy_count)
    key_valid = row_valid[:, None] & col_valid[None, :]
    region_keyval = fetched.reshape(
        block_rows, block_cols, 2, memory_local.shape[1], memory_local.shape[2]
    )
    query_blocks = to_blocks(queries.reshape(tile_rows, tile_cols, model_width))
    outputs, log_totals = attend_forward(query_blocks, keyval_pad, key_valid, region_keyval)
    attended = from_blocks(outputs).reshape(-1, model_width)
    layer_out = jnp.dot(attended, w_out, preferred_element_type=jnp.float32).astype(jnp.bfloat16)
    grad_flat = grad_out.reshape(-1, model_width)
    d_attended = jnp.dot(grad_flat, w_out.T, preferred_element_type=jnp.float32).astype(
        jnp.bfloat16
    )
    grad_out_local = inner_rows(attended, grad_flat)
    dout_blocks = to_blocks(d_attended.reshape(tile_rows, tile_cols, model_width))
    delta_rows = jnp.sum(
        split_heads(dout_blocks).astype(jnp.float32) * split_heads(outputs).astype(jnp.float32), -1
    )
    delta_rows = delta_rows.transpose(0, 1, 3, 2)
    d_queries = query_grads(
        query_blocks, keyval_pad, key_valid, region_keyval, log_totals, dout_blocks, delta_rows
    )
    query_grid = jnp.concatenate(
        [
            queries.reshape(tile_rows, tile_cols, model_width),
            d_attended.reshape(tile_rows, tile_cols, model_width),
        ],
        -1,
    )
    query_halo = padded(query_grid, (("gx", 0), ("gy", 1)), BSIDE)
    stat_grid = from_blocks(jnp.concatenate([log_totals, delta_rows], 2).transpose(0, 1, 3, 2))
    stat_halo = padded(stat_grid, (("gx", 0), ("gy", 1)), BSIDE)
    query_all = to_blocks(query_halo)
    stat_pad = to_blocks(stat_halo).transpose(0, 1, 3, 2)
    d_keys, d_values = key_grads(
        keyval_pad[1:-1, 1:-1],
        query_all[..., :model_width],
        query_all[..., model_width:],
        stat_pad[:, :, :HEADS],
        stat_pad[:, :, HEADS:],
        key_valid,
    )
    dq_flat = from_blocks(d_queries).reshape(-1, model_width)
    dk_flat = from_blocks(d_keys).reshape(-1, model_width)
    dv_flat = from_blocks(d_values).reshape(-1, model_width)
    grads_joined = jnp.concatenate([dq_flat, dk_flat, dv_flat], 1)
    w_stacked = jnp.concatenate([w_query.T, w_key.T, w_value.T], 0)
    grad_patches = jnp.dot(grads_joined, w_stacked, preferred_element_type=jnp.float32).astype(
        jnp.bfloat16
    )
    partials = (
        inner_rows(flat_in, dq_flat),
        inner_rows(flat_in, dk_flat),
        inner_rows(flat_in, dv_flat),
        grad_out_local,
    )
    summed = tree_sum(partials, ("gy", "gx"))
    return (
        layer_out.reshape(tile_rows, tile_cols, model_width),
        grad_patches.reshape(tile_rows, tile_cols, model_width),
        summed[0],
        summed[1],
        summed[2],
        summed[3],
    )


def solution(mesh):
    return jax.shard_map(
        on_device,
        mesh=mesh,
        in_specs=(
            P("gx", "gy", None),
            P(),
            P(),
            P(),
            P(),
            P("gx", "gy", None, None, None),
            P("gx", "gy", None, None),
            P("gx", "gy", None, None),
            P("gx", "gy", None),
        ),
        out_specs=(P("gx", "gy", None), P("gx", "gy", None), P(), P(), P(), P()),
        check_vma=False,
    )
```

```python
import math

import jax
import jax.numpy as jnp
from jax import lax
from jax.sharding import PartitionSpec as P

D = 256
HEADS = 2
HEAD_DIM = 128
BSIDE = 8
BT = 64
CAP = 2


masked_score = -1000000000.0


def padded(block, sides, width):
    for axis, dim in sides:
        count = lax.axis_size(axis)
        forward = [(i, i + 1) for i in range(count - 1)]
        backward = [(target, source) for source, target in forward]
        low = lax.ppermute(
            lax.slice_in_dim(block, block.shape[dim] - width, None, axis=dim), axis, forward
        )
        high = lax.ppermute(lax.slice_in_dim(block, 0, width, axis=dim), axis, backward)
        block = jnp.concatenate([low, block, high], axis=dim)
    return block


def to_blocks(grid_array):
    grid_rows, grid_cols, feature_width = grid_array.shape
    shaped = grid_array.reshape(grid_rows // BSIDE, BSIDE, grid_cols // BSIDE, BSIDE, feature_width)
    return shaped.transpose(0, 2, 1, 3, 4).reshape(
        grid_rows // BSIDE, grid_cols // BSIDE, BSIDE * BSIDE, feature_width
    )


def from_blocks(block_array):
    block_rows, block_cols, block_tokens, feature_width = block_array.shape
    shaped = block_array.reshape(block_rows, block_cols, BSIDE, BSIDE, feature_width)
    return shaped.transpose(0, 2, 1, 3, 4).reshape(
        block_rows * BSIDE, block_cols * BSIDE, feature_width
    )


def split_heads(source):
    return source.reshape(source.shape[:-1] + (HEADS, source.shape[-1] // HEADS))


def key_pieces(keyval_pad, key_valid, region_keyval):
    block_rows, block_cols = (region_keyval.shape[0], region_keyval.shape[1])
    pieces = []
    for row_off in range(3):
        for col_off in range(3):
            key_block = keyval_pad[row_off : row_off + block_rows, col_off : col_off + block_cols]
            valid_mask = key_valid[row_off : row_off + block_rows, col_off : col_off + block_cols]
            pieces.append((key_block[..., :D], key_block[..., D:], valid_mask))
    merged = region_keyval.reshape(block_rows, block_cols, 2 * BT, 2 * D)
    pieces.append(
        (merged[..., :D], merged[..., D:], jnp.ones((block_rows, block_cols), dtype=jnp.bool_))
    )
    return pieces


def piece_scores(query_heads, key_part, valid_mask):
    scores = jnp.einsum(
        "abqhe,abkhe->abhqk", query_heads, split_heads(key_part), preferred_element_type=jnp.float32
    )
    scores = scores * (1.0 / math.sqrt(HEAD_DIM))
    return jnp.where(valid_mask[:, :, None, None, None], scores, masked_score)


def attend_forward(query_blocks, keyval_pad, key_valid, region_keyval):
    query_heads = split_heads(query_blocks)
    pieces = key_pieces(keyval_pad, key_valid, region_keyval)
    scores = [
        piece_scores(query_heads, key_part, valid_mask)
        for key_part, value_part, valid_mask in pieces
    ]
    row_top = jnp.max(jnp.concatenate(scores, -1), -1, keepdims=True)
    row_total = sum(
        (jnp.sum(jnp.exp(part_scores - row_top), -1, keepdims=True) for part_scores in scores)
    )
    log_total = row_top + jnp.log(row_total)
    mixed_sum = jnp.zeros(query_heads.shape, jnp.float32)
    for part_scores, (key_part, value_part, valid_mask) in zip(scores, pieces):
        weights = jnp.exp(part_scores - log_total).astype(jnp.bfloat16)
        mixed_sum = mixed_sum + jnp.einsum(
            "abhqk,abkhe->abqhe",
            weights,
            split_heads(value_part),
            preferred_element_type=jnp.float32,
        )
    output = mixed_sum.reshape(query_blocks.shape).astype(jnp.bfloat16)
    return (output, log_total[..., 0])


def query_grads(
    query_blocks, keyval_pad, key_valid, region_keyval, log_total, dout_blocks, delta_rows
):
    query_heads = split_heads(query_blocks)
    dout_heads = split_heads(dout_blocks)
    accum_sum = jnp.zeros(query_heads.shape, jnp.float32)
    for key_part, value_part, valid_mask in key_pieces(keyval_pad, key_valid, region_keyval):
        part_scores = piece_scores(query_heads, key_part, valid_mask)
        prob_part = jnp.exp(part_scores - log_total[..., None])
        grad_prob = jnp.einsum(
            "abqhe,abkhe->abhqk",
            dout_heads,
            split_heads(value_part),
            preferred_element_type=jnp.float32,
        )
        grad_score = (prob_part * (grad_prob - delta_rows[..., None])).astype(jnp.bfloat16)
        accum_sum = accum_sum + jnp.einsum(
            "abhqk,abkhe->abqhe",
            grad_score,
            split_heads(key_part),
            preferred_element_type=jnp.float32,
        )
    return (
        (accum_sum * (1.0 / math.sqrt(HEAD_DIM))).reshape(query_blocks.shape).astype(jnp.bfloat16)
    )


def key_grads(keyval_center, query_pad, dout_pad, log_pad, delta_pad, query_valid):
    block_rows, block_cols = (keyval_center.shape[0], keyval_center.shape[1])
    key_heads = split_heads(keyval_center[..., :D])
    value_heads = split_heads(keyval_center[..., D:])
    grad_key = jnp.zeros(key_heads.shape, jnp.float32)
    grad_value = jnp.zeros(key_heads.shape, jnp.float32)
    for row_off in range(3):
        for col_off in range(3):
            query_heads = split_heads(
                query_pad[row_off : row_off + block_rows, col_off : col_off + block_cols]
            )
            dout_heads = split_heads(
                dout_pad[row_off : row_off + block_rows, col_off : col_off + block_cols]
            )
            log_part = log_pad[row_off : row_off + block_rows, col_off : col_off + block_cols]
            delta_part = delta_pad[row_off : row_off + block_rows, col_off : col_off + block_cols]
            valid_mask = query_valid[row_off : row_off + block_rows, col_off : col_off + block_cols]
            part_scores = jnp.einsum(
                "abqhe,abkhe->abhqk", query_heads, key_heads, preferred_element_type=jnp.float32
            )
            part_scores = part_scores * (1.0 / math.sqrt(HEAD_DIM))
            prob_part = jnp.where(
                valid_mask[:, :, None, None, None], jnp.exp(part_scores - log_part[..., None]), 0.0
            )
            grad_prob = jnp.einsum(
                "abqhe,abkhe->abhqk", dout_heads, value_heads, preferred_element_type=jnp.float32
            )
            grad_score = (prob_part * (grad_prob - delta_part[..., None])).astype(jnp.bfloat16)
            grad_key = grad_key + jnp.einsum(
                "abhqk,abqhe->abkhe", grad_score, query_heads, preferred_element_type=jnp.float32
            )
            rounded_prob = prob_part.astype(jnp.bfloat16)
            grad_value = grad_value + jnp.einsum(
                "abhqk,abqhe->abkhe", rounded_prob, dout_heads, preferred_element_type=jnp.float32
            )
    out_shape = (block_rows, block_cols, BT, D)
    grad_key = (grad_key * (1.0 / math.sqrt(HEAD_DIM))).reshape(out_shape).astype(jnp.bfloat16)
    return (grad_key, grad_value.reshape(out_shape).astype(jnp.bfloat16))


def inner_rows(left_rows, right_rows):
    return lax.dot_general(
        left_rows, right_rows, (((0,), (0,)), ((), ())), preferred_element_type=jnp.float32
    )


def halving_steps(axes):
    steps = []
    for axis in axes:
        count = lax.axis_size(axis)
        stride = 1
        while stride < count:
            steps.append((axis, stride))
            stride *= 2
    return steps


def doubling_gather(joined, steps):
    for axis, stride in reversed(steps):
        pairs = [(i, i ^ stride) for i in range(lax.axis_size(axis))]
        bit = (lax.axis_index(axis) // stride) % 2
        got = lax.ppermute(joined, axis, pairs)
        low = jnp.where(bit == 0, joined, got)
        high = jnp.where(bit == 0, got, joined)
        joined = jnp.concatenate([low, high], 0)
    return joined


def tree_gather(block, axis):
    count = lax.axis_size(axis)
    if count & (count - 1):
        return lax.all_gather(block, axis, axis=0, tiled=True), lambda index: index
    width = count.bit_length() - 1

    def slot_of(index):
        return sum(((index >> bit) & 1) << (width - 1 - bit) for bit in range(width))

    return doubling_gather(block, halving_steps((axis,))), slot_of


def tree_sum(parts, axes):
    sizes = [lax.axis_size(axis) for axis in axes]
    rows = sum(part.shape[0] for part in parts)
    if any(size & (size - 1) for size in sizes) or rows % math.prod(sizes):
        return lax.psum(parts, axes)
    steps = halving_steps(axes)
    last = [step for step in steps if step[0] == axes[-1]]
    halving = steps[: len(steps) - len(last) + 1]
    doubling = steps[len(halving) :]
    joined = jnp.concatenate(parts, 0)
    for axis, stride in halving:
        pairs = [(i, i ^ stride) for i in range(lax.axis_size(axis))]
        bit = (lax.axis_index(axis) // stride) % 2
        half = joined.shape[0] // 2
        keep = lax.dynamic_slice_in_dim(joined, bit * half, half, 0)
        send = lax.dynamic_slice_in_dim(joined, (1 - bit) * half, half, 0)
        joined = keep + lax.ppermute(send, axis, pairs)
    for axis, stride in doubling:
        pairs = [(i, i ^ stride) for i in range(lax.axis_size(axis))]
        joined = joined + lax.ppermute(joined, axis, pairs)
    joined = doubling_gather(joined, halving)
    out = []
    start = 0
    for part in parts:
        out.append(joined[start : start + part.shape[0]])
        start += part.shape[0]
    return tuple(out)


def fetch_regions(memory_local, owners, local_ids, axis):
    count = lax.axis_size(axis)
    entries = owners.shape[0]
    me = lax.axis_index(axis)
    order = jnp.arange(entries)
    earlier = order[None, :] < order[:, None]
    tables, slot_of = tree_gather(jnp.stack([owners, local_ids])[None], axis)
    tables = tables[jnp.array([slot_of(device) for device in range(count)])]
    mine = tables[:, 0] == me
    rank_here = jnp.sum(mine[:, None, :] & earlier[None], axis=2)
    wanted = mine[:, :, None] & (rank_here[:, :, None] == jnp.arange(CAP)[None, None, :])
    asked = jnp.sum(jnp.where(wanted, tables[:, 1][:, :, None], 0), axis=1)
    sent = jnp.take(memory_local, asked.reshape(-1), axis=0)
    sent = sent.reshape((count, CAP) + memory_local.shape[1:])
    received = lax.all_to_all(sent, axis, 0, 0, tiled=True)
    received = received.reshape((count * CAP,) + memory_local.shape[1:])
    same = owners[:, None] == owners[None, :]
    rank = jnp.sum(same & earlier, axis=1)
    return jnp.take(received, owners * CAP + rank, axis=0)


def on_device(
    patches, w_query, w_key, w_value, w_out, region_memory, region_owner, region_local, grad_out
):
    tile_rows, tile_cols, model_width = patches.shape
    block_rows, block_cols = (tile_rows // BSIDE, tile_cols // BSIDE)
    block_count = block_rows * block_cols
    flat_in = patches.reshape(-1, model_width)
    w_pair = jnp.concatenate([w_key, w_value], 1)
    queries = jnp.dot(flat_in, w_query, preferred_element_type=jnp.float32).astype(jnp.bfloat16)
    keyvals = jnp.dot(flat_in, w_pair, preferred_element_type=jnp.float32).astype(jnp.bfloat16)
    keyvals = keyvals.reshape(tile_rows, tile_cols, 2 * model_width)
    keyval_grid = padded(keyvals, (("gx", 0), ("gy", 1)), BSIDE)
    keyval_pad = to_blocks(keyval_grid)
    gx_count = lax.axis_size("gx")
    gy_count = lax.axis_size("gy")
    row_ids = lax.axis_index("gx") * block_rows - 1 + jnp.arange(block_rows + 2, dtype=jnp.int32)
    col_ids = lax.axis_index("gy") * block_cols - 1 + jnp.arange(block_cols + 2, dtype=jnp.int32)
    row_valid = (row_ids >= 0) & (row_ids < block_rows * gx_count)
    col_valid = (col_ids >= 0) & (col_ids < block_cols * gy_count)
    key_valid = row_valid[:, None] & col_valid[None, :]
    owners = region_owner.reshape(2 * block_count)
    local_ids = region_local.reshape(2 * block_count)
    memory_local = region_memory.reshape(
        region_memory.shape[2], region_memory.shape[3], region_memory.shape[4]
    )
    fetched = fetch_regions(memory_local, owners, local_ids, "gx")
    region_keyval = fetched.reshape(
        block_rows, block_cols, 2, memory_local.shape[1], memory_local.shape[2]
    )
    query_blocks = to_blocks(queries.reshape(tile_rows, tile_cols, model_width))
    outputs, log_totals = attend_forward(query_blocks, keyval_pad, key_valid, region_keyval)
    attended = from_blocks(outputs).reshape(-1, model_width)
    layer_out = jnp.dot(attended, w_out, preferred_element_type=jnp.float32).astype(jnp.bfloat16)
    grad_flat = grad_out.reshape(-1, model_width)
    d_attended = jnp.dot(grad_flat, w_out.T, preferred_element_type=jnp.float32).astype(
        jnp.bfloat16
    )
    grad_out_local = inner_rows(attended, grad_flat)
    dout_blocks = to_blocks(d_attended.reshape(tile_rows, tile_cols, model_width))
    delta_rows = jnp.sum(
        split_heads(dout_blocks).astype(jnp.float32) * split_heads(outputs).astype(jnp.float32), -1
    )
    delta_rows = delta_rows.transpose(0, 1, 3, 2)
    d_queries = query_grads(
        query_blocks, keyval_pad, key_valid, region_keyval, log_totals, dout_blocks, delta_rows
    )
    query_grid = jnp.concatenate(
        [
            queries.reshape(tile_rows, tile_cols, model_width),
            d_attended.reshape(tile_rows, tile_cols, model_width),
        ],
        -1,
    )
    query_halo = padded(query_grid, (("gx", 0), ("gy", 1)), BSIDE)
    stat_grid = from_blocks(jnp.concatenate([log_totals, delta_rows], 2).transpose(0, 1, 3, 2))
    stat_halo = padded(stat_grid, (("gx", 0), ("gy", 1)), BSIDE)
    query_all = to_blocks(query_halo)
    stat_pad = to_blocks(stat_halo).transpose(0, 1, 3, 2)
    d_keys, d_values = key_grads(
        keyval_pad[1:-1, 1:-1],
        query_all[..., :model_width],
        query_all[..., model_width:],
        stat_pad[:, :, :HEADS],
        stat_pad[:, :, HEADS:],
        key_valid,
    )
    dq_flat = from_blocks(d_queries).reshape(-1, model_width)
    dk_flat = from_blocks(d_keys).reshape(-1, model_width)
    dv_flat = from_blocks(d_values).reshape(-1, model_width)
    grads_joined = jnp.concatenate([dq_flat, dk_flat, dv_flat], 1)
    w_stacked = jnp.concatenate([w_query.T, w_key.T, w_value.T], 0)
    grad_patches = jnp.dot(grads_joined, w_stacked, preferred_element_type=jnp.float32).astype(
        jnp.bfloat16
    )
    early = tree_sum((grad_out_local, inner_rows(flat_in, dq_flat)), ("gy", "gx"))
    late = tree_sum((inner_rows(flat_in, dk_flat), inner_rows(flat_in, dv_flat)), ("gy", "gx"))
    summed = (early[1], late[0], late[1], early[0])
    return (
        layer_out.reshape(tile_rows, tile_cols, model_width),
        grad_patches.reshape(tile_rows, tile_cols, model_width),
        summed[0],
        summed[1],
        summed[2],
        summed[3],
    )


def solution(mesh):
    return jax.shard_map(
        on_device,
        mesh=mesh,
        in_specs=(
            P("gx", "gy", None),
            P(),
            P(),
            P(),
            P(),
            P("gx", "gy", None, None, None),
            P("gx", "gy", None, None),
            P("gx", "gy", None, None),
            P("gx", "gy", None),
        ),
        out_specs=(P("gx", "gy", None), P("gx", "gy", None), P(), P(), P(), P()),
        check_vma=False,
    )
```

```python
import math

import jax
import jax.numpy as jnp
from jax import lax
from jax.sharding import PartitionSpec as P

D = 256
HEADS = 2
HEAD_DIM = 128
BSIDE = 8
BT = 64
CAP = 2


masked_score = -1000000000.0


def padded(block, sides, width):
    for axis, dim in sides:
        count = lax.axis_size(axis)
        forward = [(i, i + 1) for i in range(count - 1)]
        backward = [(target, source) for source, target in forward]
        low = lax.ppermute(
            lax.slice_in_dim(block, block.shape[dim] - width, None, axis=dim), axis, forward
        )
        high = lax.ppermute(lax.slice_in_dim(block, 0, width, axis=dim), axis, backward)
        block = jnp.concatenate([low, block, high], axis=dim)
    return block


def to_blocks(grid_array):
    grid_rows, grid_cols, feature_width = grid_array.shape
    shaped = grid_array.reshape(grid_rows // BSIDE, BSIDE, grid_cols // BSIDE, BSIDE, feature_width)
    return shaped.transpose(0, 2, 1, 3, 4).reshape(
        grid_rows // BSIDE, grid_cols // BSIDE, BSIDE * BSIDE, feature_width
    )


def from_blocks(block_array):
    block_rows, block_cols, block_tokens, feature_width = block_array.shape
    shaped = block_array.reshape(block_rows, block_cols, BSIDE, BSIDE, feature_width)
    return shaped.transpose(0, 2, 1, 3, 4).reshape(
        block_rows * BSIDE, block_cols * BSIDE, feature_width
    )


def split_heads(source):
    return source.reshape(source.shape[:-1] + (HEADS, source.shape[-1] // HEADS))


def neighbour_set(padded_blocks, valid_blocks, block_rows, block_cols, axis):
    parts = []
    valid = []
    for row_off in range(3):
        for col_off in range(3):
            part = padded_blocks[row_off : row_off + block_rows, col_off : col_off + block_cols]
            parts.append(part)
            mask = valid_blocks[row_off : row_off + block_rows, col_off : col_off + block_cols]
            valid.append(jnp.broadcast_to(mask[:, :, None], (block_rows, block_cols, BT)))
    return jnp.concatenate(parts, axis), jnp.concatenate(valid, 2)


def key_set(keyval_pad, key_valid, region_keyval):
    block_rows, block_cols = (region_keyval.shape[0], region_keyval.shape[1])
    keyvals, valid = neighbour_set(keyval_pad, key_valid, block_rows, block_cols, 2)
    merged = region_keyval.reshape(block_rows, block_cols, 2 * BT, 2 * D)
    keyvals = jnp.concatenate([keyvals, merged], 2)
    valid = jnp.concatenate([valid, jnp.ones((block_rows, block_cols, 2 * BT), jnp.bool_)], 2)
    return keyvals[..., :D], keyvals[..., D:], valid


def set_scores(query_heads, key_part, valid):
    scores = jnp.einsum(
        "abqhe,abkhe->abhqk", query_heads, split_heads(key_part), preferred_element_type=jnp.float32
    )
    scores = scores * (1.0 / math.sqrt(HEAD_DIM))
    return jnp.where(valid[:, :, None, None, :], scores, masked_score)


def attend_forward(query_blocks, keyval_pad, key_valid, region_keyval):
    query_heads = split_heads(query_blocks)
    key_part, value_part, valid = key_set(keyval_pad, key_valid, region_keyval)
    scores = set_scores(query_heads, key_part, valid)
    row_top = jnp.max(scores, -1, keepdims=True)
    row_total = jnp.sum(jnp.exp(scores - row_top), -1, keepdims=True)
    log_total = row_top + jnp.log(row_total)
    weights = jnp.exp(scores - log_total).astype(jnp.bfloat16)
    mixed_sum = jnp.einsum(
        "abhqk,abkhe->abqhe", weights, split_heads(value_part), preferred_element_type=jnp.float32
    )
    output = mixed_sum.reshape(query_blocks.shape).astype(jnp.bfloat16)
    return (output, log_total[..., 0])


def query_grads(
    query_blocks, keyval_pad, key_valid, region_keyval, log_total, dout_blocks, delta_rows
):
    query_heads = split_heads(query_blocks)
    dout_heads = split_heads(dout_blocks)
    key_part, value_part, valid = key_set(keyval_pad, key_valid, region_keyval)
    scores = set_scores(query_heads, key_part, valid)
    prob = jnp.exp(scores - log_total[..., None])
    grad_prob = jnp.einsum(
        "abqhe,abkhe->abhqk", dout_heads, split_heads(value_part), preferred_element_type=jnp.float32
    )
    grad_score = (prob * (grad_prob - delta_rows[..., None])).astype(jnp.bfloat16)
    accum_sum = jnp.einsum(
        "abhqk,abkhe->abqhe", grad_score, split_heads(key_part), preferred_element_type=jnp.float32
    )
    return (
        (accum_sum * (1.0 / math.sqrt(HEAD_DIM))).reshape(query_blocks.shape).astype(jnp.bfloat16)
    )


def key_grads(keyval_center, query_pad, dout_pad, log_pad, delta_pad, query_valid):
    block_rows, block_cols = (keyval_center.shape[0], keyval_center.shape[1])
    key_heads = split_heads(keyval_center[..., :D])
    value_heads = split_heads(keyval_center[..., D:])
    queries, valid = neighbour_set(query_pad, query_valid, block_rows, block_cols, 2)
    douts, _ = neighbour_set(dout_pad, query_valid, block_rows, block_cols, 2)
    logs, _ = neighbour_set(log_pad, query_valid, block_rows, block_cols, 3)
    deltas, _ = neighbour_set(delta_pad, query_valid, block_rows, block_cols, 3)
    query_heads = split_heads(queries)
    dout_heads = split_heads(douts)
    scores = jnp.einsum(
        "abqhe,abkhe->abhqk", query_heads, key_heads, preferred_element_type=jnp.float32
    )
    scores = scores * (1.0 / math.sqrt(HEAD_DIM))
    prob = jnp.where(valid[:, :, None, :, None], jnp.exp(scores - logs[..., None]), 0.0)
    grad_prob = jnp.einsum(
        "abqhe,abkhe->abhqk", dout_heads, value_heads, preferred_element_type=jnp.float32
    )
    grad_score = (prob * (grad_prob - deltas[..., None])).astype(jnp.bfloat16)
    grad_key = jnp.einsum(
        "abhqk,abqhe->abkhe", grad_score, query_heads, preferred_element_type=jnp.float32
    )
    grad_value = jnp.einsum(
        "abhqk,abqhe->abkhe", prob.astype(jnp.bfloat16), dout_heads, preferred_element_type=jnp.float32
    )
    out_shape = (block_rows, block_cols, BT, D)
    grad_key = (grad_key * (1.0 / math.sqrt(HEAD_DIM))).reshape(out_shape).astype(jnp.bfloat16)
    return (grad_key, grad_value.reshape(out_shape).astype(jnp.bfloat16))


def inner_rows(left_rows, right_rows):
    return lax.dot_general(
        left_rows, right_rows, (((0,), (0,)), ((), ())), preferred_element_type=jnp.float32
    )


def halving_steps(axes):
    steps = []
    for axis in axes:
        count = lax.axis_size(axis)
        stride = 1
        while stride < count:
            steps.append((axis, stride))
            stride *= 2
    return steps


def doubling_gather(joined, steps):
    for axis, stride in reversed(steps):
        pairs = [(i, i ^ stride) for i in range(lax.axis_size(axis))]
        bit = (lax.axis_index(axis) // stride) % 2
        got = lax.ppermute(joined, axis, pairs)
        low = jnp.where(bit == 0, joined, got)
        high = jnp.where(bit == 0, got, joined)
        joined = jnp.concatenate([low, high], 0)
    return joined


def tree_gather(block, axis):
    count = lax.axis_size(axis)
    if count & (count - 1):
        return lax.all_gather(block, axis, axis=0, tiled=True), lambda index: index
    width = count.bit_length() - 1

    def slot_of(index):
        return sum(((index >> bit) & 1) << (width - 1 - bit) for bit in range(width))

    return doubling_gather(block, halving_steps((axis,))), slot_of


def tree_sum(parts, axes):
    sizes = [lax.axis_size(axis) for axis in axes]
    rows = sum(part.shape[0] for part in parts)
    if any(size & (size - 1) for size in sizes) or rows % math.prod(sizes):
        return lax.psum(parts, axes)
    steps = halving_steps(axes)
    last = [step for step in steps if step[0] == axes[-1]]
    halving = steps[: len(steps) - len(last) + 1]
    doubling = steps[len(halving) :]
    joined = jnp.concatenate(parts, 0)
    for axis, stride in halving:
        pairs = [(i, i ^ stride) for i in range(lax.axis_size(axis))]
        bit = (lax.axis_index(axis) // stride) % 2
        half = joined.shape[0] // 2
        keep = lax.dynamic_slice_in_dim(joined, bit * half, half, 0)
        send = lax.dynamic_slice_in_dim(joined, (1 - bit) * half, half, 0)
        joined = keep + lax.ppermute(send, axis, pairs)
    for axis, stride in doubling:
        pairs = [(i, i ^ stride) for i in range(lax.axis_size(axis))]
        joined = joined + lax.ppermute(joined, axis, pairs)
    joined = doubling_gather(joined, halving)
    out = []
    start = 0
    for part in parts:
        out.append(joined[start : start + part.shape[0]])
        start += part.shape[0]
    return tuple(out)


def fetch_regions(memory_local, owners, local_ids, axis):
    count = lax.axis_size(axis)
    entries = owners.shape[0]
    me = lax.axis_index(axis)
    order = jnp.arange(entries)
    earlier = order[None, :] < order[:, None]
    tables, slot_of = tree_gather(jnp.stack([owners, local_ids])[None], axis)
    tables = tables[jnp.array([slot_of(device) for device in range(count)])]
    mine = tables[:, 0] == me
    rank_here = jnp.sum(mine[:, None, :] & earlier[None], axis=2)
    wanted = mine[:, :, None] & (rank_here[:, :, None] == jnp.arange(CAP)[None, None, :])
    asked = jnp.sum(jnp.where(wanted, tables[:, 1][:, :, None], 0), axis=1)
    sent = jnp.take(memory_local, asked.reshape(-1), axis=0)
    sent = sent.reshape((count, CAP) + memory_local.shape[1:])
    received = lax.all_to_all(sent, axis, 0, 0, tiled=True)
    received = received.reshape((count * CAP,) + memory_local.shape[1:])
    same = owners[:, None] == owners[None, :]
    rank = jnp.sum(same & earlier, axis=1)
    return jnp.take(received, owners * CAP + rank, axis=0)


def on_device(
    patches, w_query, w_key, w_value, w_out, region_memory, region_owner, region_local, grad_out
):
    tile_rows, tile_cols, model_width = patches.shape
    block_rows, block_cols = (tile_rows // BSIDE, tile_cols // BSIDE)
    block_count = block_rows * block_cols
    flat_in = patches.reshape(-1, model_width)
    w_pair = jnp.concatenate([w_key, w_value], 1)
    queries = jnp.dot(flat_in, w_query, preferred_element_type=jnp.float32).astype(jnp.bfloat16)
    keyvals = jnp.dot(flat_in, w_pair, preferred_element_type=jnp.float32).astype(jnp.bfloat16)
    keyvals = keyvals.reshape(tile_rows, tile_cols, 2 * model_width)
    keyval_grid = padded(keyvals, (("gx", 0), ("gy", 1)), BSIDE)
    keyval_pad = to_blocks(keyval_grid)
    gx_count = lax.axis_size("gx")
    gy_count = lax.axis_size("gy")
    row_ids = lax.axis_index("gx") * block_rows - 1 + jnp.arange(block_rows + 2, dtype=jnp.int32)
    col_ids = lax.axis_index("gy") * block_cols - 1 + jnp.arange(block_cols + 2, dtype=jnp.int32)
    row_valid = (row_ids >= 0) & (row_ids < block_rows * gx_count)
    col_valid = (col_ids >= 0) & (col_ids < block_cols * gy_count)
    key_valid = row_valid[:, None] & col_valid[None, :]
    owners = region_owner.reshape(2 * block_count)
    local_ids = region_local.reshape(2 * block_count)
    memory_local = region_memory.reshape(
        region_memory.shape[2], region_memory.shape[3], region_memory.shape[4]
    )
    fetched = fetch_regions(memory_local, owners, local_ids, "gx")
    region_keyval = fetched.reshape(
        block_rows, block_cols, 2, memory_local.shape[1], memory_local.shape[2]
    )
    query_blocks = to_blocks(queries.reshape(tile_rows, tile_cols, model_width))
    outputs, log_totals = attend_forward(query_blocks, keyval_pad, key_valid, region_keyval)
    attended = from_blocks(outputs).reshape(-1, model_width)
    layer_out = jnp.dot(attended, w_out, preferred_element_type=jnp.float32).astype(jnp.bfloat16)
    grad_flat = grad_out.reshape(-1, model_width)
    d_attended = jnp.dot(grad_flat, w_out.T, preferred_element_type=jnp.float32).astype(
        jnp.bfloat16
    )
    grad_out_local = inner_rows(attended, grad_flat)
    dout_blocks = to_blocks(d_attended.reshape(tile_rows, tile_cols, model_width))
    delta_rows = jnp.sum(
        split_heads(dout_blocks).astype(jnp.float32) * split_heads(outputs).astype(jnp.float32), -1
    )
    delta_rows = delta_rows.transpose(0, 1, 3, 2)
    d_queries = query_grads(
        query_blocks, keyval_pad, key_valid, region_keyval, log_totals, dout_blocks, delta_rows
    )
    query_grid = jnp.concatenate(
        [
            queries.reshape(tile_rows, tile_cols, model_width),
            d_attended.reshape(tile_rows, tile_cols, model_width),
        ],
        -1,
    )
    query_halo = padded(query_grid, (("gx", 0), ("gy", 1)), BSIDE)
    stat_grid = from_blocks(jnp.concatenate([log_totals, delta_rows], 2).transpose(0, 1, 3, 2))
    stat_halo = padded(stat_grid, (("gx", 0), ("gy", 1)), BSIDE)
    query_all = to_blocks(query_halo)
    stat_pad = to_blocks(stat_halo).transpose(0, 1, 3, 2)
    d_keys, d_values = key_grads(
        keyval_pad[1:-1, 1:-1],
        query_all[..., :model_width],
        query_all[..., model_width:],
        stat_pad[:, :, :HEADS],
        stat_pad[:, :, HEADS:],
        key_valid,
    )
    dq_flat = from_blocks(d_queries).reshape(-1, model_width)
    dk_flat = from_blocks(d_keys).reshape(-1, model_width)
    dv_flat = from_blocks(d_values).reshape(-1, model_width)
    grads_joined = jnp.concatenate([dq_flat, dk_flat, dv_flat], 1)
    w_stacked = jnp.concatenate([w_query.T, w_key.T, w_value.T], 0)
    grad_patches = jnp.dot(grads_joined, w_stacked, preferred_element_type=jnp.float32).astype(
        jnp.bfloat16
    )
    partials = (
        inner_rows(flat_in, dq_flat),
        inner_rows(flat_in, dk_flat),
        inner_rows(flat_in, dv_flat),
        grad_out_local,
    )
    summed = tree_sum(partials, ("gy", "gx"))
    return (
        layer_out.reshape(tile_rows, tile_cols, model_width),
        grad_patches.reshape(tile_rows, tile_cols, model_width),
        summed[0],
        summed[1],
        summed[2],
        summed[3],
    )


def solution(mesh):
    return jax.shard_map(
        on_device,
        mesh=mesh,
        in_specs=(
            P("gx", "gy", None),
            P(),
            P(),
            P(),
            P(),
            P("gx", "gy", None, None, None),
            P("gx", "gy", None, None),
            P("gx", "gy", None, None),
            P("gx", "gy", None),
        ),
        out_specs=(P("gx", "gy", None), P("gx", "gy", None), P(), P(), P(), P()),
        check_vma=False,
    )
```

```python
import math

import jax
import jax.numpy as jnp
from jax import lax
from jax.sharding import PartitionSpec as P

D = 256
HEADS = 2
HEAD_DIM = 128
BSIDE = 8
BT = 64
CAP = 2


masked_score = -1000000000.0


def padded(block, sides, width):
    for axis, dim in sides:
        count = lax.axis_size(axis)
        forward = [(i, i + 1) for i in range(count - 1)]
        backward = [(target, source) for source, target in forward]
        low = lax.ppermute(
            lax.slice_in_dim(block, block.shape[dim] - width, None, axis=dim), axis, forward
        )
        high = lax.ppermute(lax.slice_in_dim(block, 0, width, axis=dim), axis, backward)
        block = jnp.concatenate([low, block, high], axis=dim)
    return block


def halo(block, width):
    axes = ("gx", "gy")
    rows_n, cols_n = lax.axis_size("gx"), lax.axis_size("gy")
    rows, cols = block.shape[0], block.shape[1]
    row_parts = {-1: slice(rows - width, rows), 0: slice(0, rows), 1: slice(0, width)}
    col_parts = {-1: slice(cols - width, cols), 0: slice(0, cols), 1: slice(0, width)}
    grid = []
    for row_off in (-1, 0, 1):
        line = []
        for col_off in (-1, 0, 1):
            piece = block[row_parts[row_off], col_parts[col_off]]
            if row_off or col_off:
                pairs = [
                    ((i + row_off) * cols_n + j + col_off, i * cols_n + j)
                    for i in range(rows_n)
                    for j in range(cols_n)
                    if 0 <= i + row_off < rows_n and 0 <= j + col_off < cols_n
                ]
                piece = lax.ppermute(piece, axes, pairs)
            line.append(piece)
        grid.append(jnp.concatenate(line, axis=1))
    return jnp.concatenate(grid, axis=0)


def to_blocks(grid_array):
    grid_rows, grid_cols, feature_width = grid_array.shape
    shaped = grid_array.reshape(grid_rows // BSIDE, BSIDE, grid_cols // BSIDE, BSIDE, feature_width)
    return shaped.transpose(0, 2, 1, 3, 4).reshape(
        grid_rows // BSIDE, grid_cols // BSIDE, BSIDE * BSIDE, feature_width
    )


def from_blocks(block_array):
    block_rows, block_cols, block_tokens, feature_width = block_array.shape
    shaped = block_array.reshape(block_rows, block_cols, BSIDE, BSIDE, feature_width)
    return shaped.transpose(0, 2, 1, 3, 4).reshape(
        block_rows * BSIDE, block_cols * BSIDE, feature_width
    )


def split_heads(source):
    return source.reshape(source.shape[:-1] + (HEADS, source.shape[-1] // HEADS))


def neighbour_set(padded_blocks, valid_blocks, block_rows, block_cols, axis):
    parts = []
    valid = []
    for row_off in range(3):
        for col_off in range(3):
            part = padded_blocks[row_off : row_off + block_rows, col_off : col_off + block_cols]
            parts.append(part)
            mask = valid_blocks[row_off : row_off + block_rows, col_off : col_off + block_cols]
            valid.append(jnp.broadcast_to(mask[:, :, None], (block_rows, block_cols, BT)))
    return jnp.concatenate(parts, axis), jnp.concatenate(valid, 2)


def key_set(keyval_pad, key_valid, region_keyval):
    block_rows, block_cols = (region_keyval.shape[0], region_keyval.shape[1])
    keyvals, valid = neighbour_set(keyval_pad, key_valid, block_rows, block_cols, 2)
    merged = region_keyval.reshape(block_rows, block_cols, 2 * BT, 2 * D)
    keyvals = jnp.concatenate([keyvals, merged], 2)
    valid = jnp.concatenate([valid, jnp.ones((block_rows, block_cols, 2 * BT), jnp.bool_)], 2)
    return keyvals[..., :D], keyvals[..., D:], valid


def set_scores(query_heads, key_part, valid):
    scores = jnp.einsum(
        "abqhe,abkhe->abhqk", query_heads, split_heads(key_part), preferred_element_type=jnp.float32
    )
    scores = scores * (1.0 / math.sqrt(HEAD_DIM))
    return jnp.where(valid[:, :, None, None, :], scores, masked_score)


def attend_forward(query_blocks, keyval_pad, key_valid, region_keyval):
    query_heads = split_heads(query_blocks)
    key_part, value_part, valid = key_set(keyval_pad, key_valid, region_keyval)
    scores = set_scores(query_heads, key_part, valid)
    row_top = jnp.max(scores, -1, keepdims=True)
    row_total = jnp.sum(jnp.exp(scores - row_top), -1, keepdims=True)
    log_total = row_top + jnp.log(row_total)
    weights = jnp.exp(scores - log_total).astype(jnp.bfloat16)
    mixed_sum = jnp.einsum(
        "abhqk,abkhe->abqhe", weights, split_heads(value_part), preferred_element_type=jnp.float32
    )
    output = mixed_sum.reshape(query_blocks.shape).astype(jnp.bfloat16)
    return (output, log_total[..., 0])


def query_grads(
    query_blocks, keyval_pad, key_valid, region_keyval, log_total, dout_blocks, delta_rows
):
    query_heads = split_heads(query_blocks)
    dout_heads = split_heads(dout_blocks)
    key_part, value_part, valid = key_set(keyval_pad, key_valid, region_keyval)
    scores = set_scores(query_heads, key_part, valid)
    prob = jnp.exp(scores - log_total[..., None])
    grad_prob = jnp.einsum(
        "abqhe,abkhe->abhqk", dout_heads, split_heads(value_part), preferred_element_type=jnp.float32
    )
    grad_score = (prob * (grad_prob - delta_rows[..., None])).astype(jnp.bfloat16)
    accum_sum = jnp.einsum(
        "abhqk,abkhe->abqhe", grad_score, split_heads(key_part), preferred_element_type=jnp.float32
    )
    return (
        (accum_sum * (1.0 / math.sqrt(HEAD_DIM))).reshape(query_blocks.shape).astype(jnp.bfloat16)
    )


def key_grads(keyval_center, query_pad, dout_pad, log_pad, delta_pad, query_valid):
    block_rows, block_cols = (keyval_center.shape[0], keyval_center.shape[1])
    key_heads = split_heads(keyval_center[..., :D])
    value_heads = split_heads(keyval_center[..., D:])
    queries, valid = neighbour_set(query_pad, query_valid, block_rows, block_cols, 2)
    douts, _ = neighbour_set(dout_pad, query_valid, block_rows, block_cols, 2)
    logs, _ = neighbour_set(log_pad, query_valid, block_rows, block_cols, 3)
    deltas, _ = neighbour_set(delta_pad, query_valid, block_rows, block_cols, 3)
    query_heads = split_heads(queries)
    dout_heads = split_heads(douts)
    scores = jnp.einsum(
        "abqhe,abkhe->abhqk", query_heads, key_heads, preferred_element_type=jnp.float32
    )
    scores = scores * (1.0 / math.sqrt(HEAD_DIM))
    prob = jnp.where(valid[:, :, None, :, None], jnp.exp(scores - logs[..., None]), 0.0)
    grad_prob = jnp.einsum(
        "abqhe,abkhe->abhqk", dout_heads, value_heads, preferred_element_type=jnp.float32
    )
    grad_score = (prob * (grad_prob - deltas[..., None])).astype(jnp.bfloat16)
    grad_key = jnp.einsum(
        "abhqk,abqhe->abkhe", grad_score, query_heads, preferred_element_type=jnp.float32
    )
    grad_value = jnp.einsum(
        "abhqk,abqhe->abkhe", prob.astype(jnp.bfloat16), dout_heads, preferred_element_type=jnp.float32
    )
    out_shape = (block_rows, block_cols, BT, D)
    grad_key = (grad_key * (1.0 / math.sqrt(HEAD_DIM))).reshape(out_shape).astype(jnp.bfloat16)
    return (grad_key, grad_value.reshape(out_shape).astype(jnp.bfloat16))


def inner_rows(left_rows, right_rows):
    return lax.dot_general(
        left_rows, right_rows, (((0,), (0,)), ((), ())), preferred_element_type=jnp.float32
    )


def halving_steps(axes):
    steps = []
    for axis in axes:
        count = lax.axis_size(axis)
        stride = 1
        while stride < count:
            steps.append((axis, stride))
            stride *= 2
    return steps


def doubling_gather(joined, steps):
    for axis, stride in reversed(steps):
        pairs = [(i, i ^ stride) for i in range(lax.axis_size(axis))]
        bit = (lax.axis_index(axis) // stride) % 2
        got = lax.ppermute(joined, axis, pairs)
        low = jnp.where(bit == 0, joined, got)
        high = jnp.where(bit == 0, got, joined)
        joined = jnp.concatenate([low, high], 0)
    return joined


def tree_gather(block, axis):
    count = lax.axis_size(axis)
    if count & (count - 1):
        return lax.all_gather(block, axis, axis=0, tiled=True), lambda index: index
    width = count.bit_length() - 1

    def slot_of(index):
        return sum(((index >> bit) & 1) << (width - 1 - bit) for bit in range(width))

    return doubling_gather(block, halving_steps((axis,))), slot_of


def tree_sum(parts, axes):
    sizes = [lax.axis_size(axis) for axis in axes]
    rows = sum(part.shape[0] for part in parts)
    if any(size & (size - 1) for size in sizes) or rows % math.prod(sizes):
        return lax.psum(parts, axes)
    steps = halving_steps(axes)
    last = [step for step in steps if step[0] == axes[-1]]
    halving = steps[: len(steps) - len(last) + 1]
    doubling = steps[len(halving) :]
    joined = jnp.concatenate(parts, 0)
    for axis, stride in halving:
        pairs = [(i, i ^ stride) for i in range(lax.axis_size(axis))]
        bit = (lax.axis_index(axis) // stride) % 2
        half = joined.shape[0] // 2
        keep = lax.dynamic_slice_in_dim(joined, bit * half, half, 0)
        send = lax.dynamic_slice_in_dim(joined, (1 - bit) * half, half, 0)
        joined = keep + lax.ppermute(send, axis, pairs)
    for axis, stride in doubling:
        pairs = [(i, i ^ stride) for i in range(lax.axis_size(axis))]
        joined = joined + lax.ppermute(joined, axis, pairs)
    joined = doubling_gather(joined, halving)
    out = []
    start = 0
    for part in parts:
        out.append(joined[start : start + part.shape[0]])
        start += part.shape[0]
    return tuple(out)


def fetch_regions(memory_local, owners, local_ids, axis):
    count = lax.axis_size(axis)
    entries = owners.shape[0]
    me = lax.axis_index(axis)
    order = jnp.arange(entries)
    earlier = order[None, :] < order[:, None]
    tables, slot_of = tree_gather(jnp.stack([owners, local_ids])[None], axis)
    tables = tables[jnp.array([slot_of(device) for device in range(count)])]
    mine = tables[:, 0] == me
    rank_here = jnp.sum(mine[:, None, :] & earlier[None], axis=2)
    wanted = mine[:, :, None] & (rank_here[:, :, None] == jnp.arange(CAP)[None, None, :])
    asked = jnp.sum(jnp.where(wanted, tables[:, 1][:, :, None], 0), axis=1)
    sent = jnp.take(memory_local, asked.reshape(-1), axis=0)
    sent = sent.reshape((count, CAP) + memory_local.shape[1:])
    received = lax.all_to_all(sent, axis, 0, 0, tiled=True)
    received = received.reshape((count * CAP,) + memory_local.shape[1:])
    same = owners[:, None] == owners[None, :]
    rank = jnp.sum(same & earlier, axis=1)
    return jnp.take(received, owners * CAP + rank, axis=0)


def on_device(
    patches, w_query, w_key, w_value, w_out, region_memory, region_owner, region_local, grad_out
):
    tile_rows, tile_cols, model_width = patches.shape
    block_rows, block_cols = (tile_rows // BSIDE, tile_cols // BSIDE)
    block_count = block_rows * block_cols
    flat_in = patches.reshape(-1, model_width)
    w_pair = jnp.concatenate([w_key, w_value], 1)
    queries = jnp.dot(flat_in, w_query, preferred_element_type=jnp.float32).astype(jnp.bfloat16)
    keyvals = jnp.dot(flat_in, w_pair, preferred_element_type=jnp.float32).astype(jnp.bfloat16)
    keyvals = keyvals.reshape(tile_rows, tile_cols, 2 * model_width)
    keyval_grid = padded(keyvals, (("gx", 0), ("gy", 1)), BSIDE)
    keyval_pad = to_blocks(keyval_grid)
    gx_count = lax.axis_size("gx")
    gy_count = lax.axis_size("gy")
    row_ids = lax.axis_index("gx") * block_rows - 1 + jnp.arange(block_rows + 2, dtype=jnp.int32)
    col_ids = lax.axis_index("gy") * block_cols - 1 + jnp.arange(block_cols + 2, dtype=jnp.int32)
    row_valid = (row_ids >= 0) & (row_ids < block_rows * gx_count)
    col_valid = (col_ids >= 0) & (col_ids < block_cols * gy_count)
    key_valid = row_valid[:, None] & col_valid[None, :]
    owners = region_owner.reshape(2 * block_count)
    local_ids = region_local.reshape(2 * block_count)
    memory_local = region_memory.reshape(
        region_memory.shape[2], region_memory.shape[3], region_memory.shape[4]
    )
    fetched = fetch_regions(memory_local, owners, local_ids, "gx")
    grad_flat = grad_out.reshape(-1, model_width)
    d_attended = jnp.dot(grad_flat, w_out.T, preferred_element_type=jnp.float32).astype(
        jnp.bfloat16
    )
    query_grid = jnp.concatenate(
        [
            queries.reshape(tile_rows, tile_cols, model_width),
            d_attended.reshape(tile_rows, tile_cols, model_width),
        ],
        -1,
    )
    query_halo = padded(query_grid, (("gx", 0), ("gy", 1)), BSIDE)
    fetched, query_halo = lax.optimization_barrier((fetched, query_halo))
    region_keyval = fetched.reshape(
        block_rows, block_cols, 2, memory_local.shape[1], memory_local.shape[2]
    )
    query_blocks = to_blocks(queries.reshape(tile_rows, tile_cols, model_width))
    outputs, log_totals = attend_forward(query_blocks, keyval_pad, key_valid, region_keyval)
    attended = from_blocks(outputs).reshape(-1, model_width)
    layer_out = jnp.dot(attended, w_out, preferred_element_type=jnp.float32).astype(jnp.bfloat16)
    grad_out_local = inner_rows(attended, grad_flat)
    dout_blocks = to_blocks(d_attended.reshape(tile_rows, tile_cols, model_width))
    delta_rows = jnp.sum(
        split_heads(dout_blocks).astype(jnp.float32) * split_heads(outputs).astype(jnp.float32), -1
    )
    delta_rows = delta_rows.transpose(0, 1, 3, 2)
    d_queries = query_grads(
        query_blocks, keyval_pad, key_valid, region_keyval, log_totals, dout_blocks, delta_rows
    )
    stat_grid = from_blocks(jnp.concatenate([log_totals, delta_rows], 2).transpose(0, 1, 3, 2))
    stat_halo = halo(stat_grid, BSIDE)
    query_all = to_blocks(query_halo)
    stat_pad = to_blocks(stat_halo).transpose(0, 1, 3, 2)
    d_keys, d_values = key_grads(
        keyval_pad[1:-1, 1:-1],
        query_all[..., :model_width],
        query_all[..., model_width:],
        stat_pad[:, :, :HEADS],
        stat_pad[:, :, HEADS:],
        key_valid,
    )
    dq_flat = from_blocks(d_queries).reshape(-1, model_width)
    dk_flat = from_blocks(d_keys).reshape(-1, model_width)
    dv_flat = from_blocks(d_values).reshape(-1, model_width)
    grads_joined = jnp.concatenate([dq_flat, dk_flat, dv_flat], 1)
    w_stacked = jnp.concatenate([w_query.T, w_key.T, w_value.T], 0)
    grad_patches = jnp.dot(grads_joined, w_stacked, preferred_element_type=jnp.float32).astype(
        jnp.bfloat16
    )
    partials = (
        inner_rows(flat_in, dq_flat),
        inner_rows(flat_in, dk_flat),
        inner_rows(flat_in, dv_flat),
        grad_out_local,
    )
    summed = tree_sum(partials, ("gy", "gx"))
    return (
        layer_out.reshape(tile_rows, tile_cols, model_width),
        grad_patches.reshape(tile_rows, tile_cols, model_width),
        summed[0],
        summed[1],
        summed[2],
        summed[3],
    )


def solution(mesh):
    return jax.shard_map(
        on_device,
        mesh=mesh,
        in_specs=(
            P("gx", "gy", None),
            P(),
            P(),
            P(),
            P(),
            P("gx", "gy", None, None, None),
            P("gx", "gy", None, None),
            P("gx", "gy", None, None),
            P("gx", "gy", None),
        ),
        out_specs=(P("gx", "gy", None), P("gx", "gy", None), P(), P(), P(), P()),
        check_vma=False,
    )
```

```python
import math

import jax
import jax.numpy as jnp
from jax import lax
from jax.sharding import PartitionSpec as P

D = 256
HEADS = 2
HEAD_DIM = 128
BSIDE = 8
BT = 64
CAP = 2


masked_score = -1000000000.0


def padded(block, sides, width):
    for axis, dim in sides:
        count = lax.axis_size(axis)
        forward = [(i, i + 1) for i in range(count - 1)]
        backward = [(target, source) for source, target in forward]
        low = lax.ppermute(
            lax.slice_in_dim(block, block.shape[dim] - width, None, axis=dim), axis, forward
        )
        high = lax.ppermute(lax.slice_in_dim(block, 0, width, axis=dim), axis, backward)
        block = jnp.concatenate([low, block, high], axis=dim)
    return block


def to_blocks(grid_array):
    grid_rows, grid_cols, feature_width = grid_array.shape
    shaped = grid_array.reshape(grid_rows // BSIDE, BSIDE, grid_cols // BSIDE, BSIDE, feature_width)
    return shaped.transpose(0, 2, 1, 3, 4).reshape(
        grid_rows // BSIDE, grid_cols // BSIDE, BSIDE * BSIDE, feature_width
    )


def from_blocks(block_array):
    block_rows, block_cols, block_tokens, feature_width = block_array.shape
    shaped = block_array.reshape(block_rows, block_cols, BSIDE, BSIDE, feature_width)
    return shaped.transpose(0, 2, 1, 3, 4).reshape(
        block_rows * BSIDE, block_cols * BSIDE, feature_width
    )


def split_heads(source):
    return source.reshape(source.shape[:-1] + (HEADS, source.shape[-1] // HEADS))


def neighbour_set(padded_blocks, valid_blocks, block_rows, block_cols, axis):
    parts = []
    valid = []
    for row_off in range(3):
        for col_off in range(3):
            part = padded_blocks[row_off : row_off + block_rows, col_off : col_off + block_cols]
            parts.append(part)
            mask = valid_blocks[row_off : row_off + block_rows, col_off : col_off + block_cols]
            valid.append(jnp.broadcast_to(mask[:, :, None], (block_rows, block_cols, BT)))
    return jnp.concatenate(parts, axis), jnp.concatenate(valid, 2)


def key_set(keyval_pad, key_valid, region_keyval):
    block_rows, block_cols = (region_keyval.shape[0], region_keyval.shape[1])
    keyvals, valid = neighbour_set(keyval_pad, key_valid, block_rows, block_cols, 2)
    merged = region_keyval.reshape(block_rows, block_cols, 2 * BT, 2 * D)
    keyvals = jnp.concatenate([keyvals, merged], 2)
    valid = jnp.concatenate([valid, jnp.ones((block_rows, block_cols, 2 * BT), jnp.bool_)], 2)
    return keyvals[..., :D], keyvals[..., D:], valid


def set_scores(query_heads, key_part, valid):
    scores = jnp.einsum(
        "abqhe,abkhe->abhqk", query_heads, split_heads(key_part), preferred_element_type=jnp.float32
    )
    scores = scores * (1.0 / math.sqrt(HEAD_DIM))
    return jnp.where(valid[:, :, None, None, :], scores, masked_score)


def attend_forward(query_blocks, keyval_pad, key_valid, region_keyval):
    query_heads = split_heads(query_blocks)
    key_part, value_part, valid = key_set(keyval_pad, key_valid, region_keyval)
    scores = set_scores(query_heads, key_part, valid)
    row_top = jnp.max(scores, -1, keepdims=True)
    row_total = jnp.sum(jnp.exp(scores - row_top), -1, keepdims=True)
    log_total = row_top + jnp.log(row_total)
    weights = jnp.exp(scores - log_total).astype(jnp.bfloat16)
    mixed_sum = jnp.einsum(
        "abhqk,abkhe->abqhe", weights, split_heads(value_part), preferred_element_type=jnp.float32
    )
    output = mixed_sum.reshape(query_blocks.shape).astype(jnp.bfloat16)
    return (output, log_total[..., 0])


def query_grads(
    query_blocks, keyval_pad, key_valid, region_keyval, log_total, dout_blocks, delta_rows
):
    query_heads = split_heads(query_blocks)
    dout_heads = split_heads(dout_blocks)
    key_part, value_part, valid = key_set(keyval_pad, key_valid, region_keyval)
    scores = set_scores(query_heads, key_part, valid)
    prob = jnp.exp(scores - log_total[..., None])
    grad_prob = jnp.einsum(
        "abqhe,abkhe->abhqk", dout_heads, split_heads(value_part), preferred_element_type=jnp.float32
    )
    grad_score = (prob * (grad_prob - delta_rows[..., None])).astype(jnp.bfloat16)
    accum_sum = jnp.einsum(
        "abhqk,abkhe->abqhe", grad_score, split_heads(key_part), preferred_element_type=jnp.float32
    )
    return (
        (accum_sum * (1.0 / math.sqrt(HEAD_DIM))).reshape(query_blocks.shape).astype(jnp.bfloat16)
    )


def key_grads(keyval_center, query_pad, dout_pad, log_pad, delta_pad, query_valid):
    block_rows, block_cols = (keyval_center.shape[0], keyval_center.shape[1])
    key_heads = split_heads(keyval_center[..., :D])
    value_heads = split_heads(keyval_center[..., D:])
    queries, valid = neighbour_set(query_pad, query_valid, block_rows, block_cols, 2)
    douts, _ = neighbour_set(dout_pad, query_valid, block_rows, block_cols, 2)
    logs, _ = neighbour_set(log_pad, query_valid, block_rows, block_cols, 3)
    deltas, _ = neighbour_set(delta_pad, query_valid, block_rows, block_cols, 3)
    query_heads = split_heads(queries)
    dout_heads = split_heads(douts)
    scores = jnp.einsum(
        "abqhe,abkhe->abhqk", query_heads, key_heads, preferred_element_type=jnp.float32
    )
    scores = scores * (1.0 / math.sqrt(HEAD_DIM))
    prob = jnp.where(valid[:, :, None, :, None], jnp.exp(scores - logs[..., None]), 0.0)
    grad_prob = jnp.einsum(
        "abqhe,abkhe->abhqk", dout_heads, value_heads, preferred_element_type=jnp.float32
    )
    grad_score = (prob * (grad_prob - deltas[..., None])).astype(jnp.bfloat16)
    grad_key = jnp.einsum(
        "abhqk,abqhe->abkhe", grad_score, query_heads, preferred_element_type=jnp.float32
    )
    grad_value = jnp.einsum(
        "abhqk,abqhe->abkhe", prob.astype(jnp.bfloat16), dout_heads, preferred_element_type=jnp.float32
    )
    out_shape = (block_rows, block_cols, BT, D)
    grad_key = (grad_key * (1.0 / math.sqrt(HEAD_DIM))).reshape(out_shape).astype(jnp.bfloat16)
    return (grad_key, grad_value.reshape(out_shape).astype(jnp.bfloat16))


def inner_rows(left_rows, right_rows):
    return lax.dot_general(
        left_rows, right_rows, (((0,), (0,)), ((), ())), preferred_element_type=jnp.float32
    )


def halving_steps(axes):
    steps = []
    for axis in axes:
        count = lax.axis_size(axis)
        stride = 1
        while stride < count:
            steps.append((axis, stride))
            stride *= 2
    return steps


def doubling_gather(joined, steps):
    for axis, stride in reversed(steps):
        pairs = [(i, i ^ stride) for i in range(lax.axis_size(axis))]
        bit = (lax.axis_index(axis) // stride) % 2
        got = lax.ppermute(joined, axis, pairs)
        low = jnp.where(bit == 0, joined, got)
        high = jnp.where(bit == 0, got, joined)
        joined = jnp.concatenate([low, high], 0)
    return joined


def tree_gather(block, axis):
    count = lax.axis_size(axis)
    if count & (count - 1):
        return lax.all_gather(block, axis, axis=0, tiled=True), lambda index: index
    width = count.bit_length() - 1

    def slot_of(index):
        return sum(((index >> bit) & 1) << (width - 1 - bit) for bit in range(width))

    return doubling_gather(block, halving_steps((axis,))), slot_of


def tree_sum(parts, axes):
    sizes = [lax.axis_size(axis) for axis in axes]
    rows = sum(part.shape[0] for part in parts)
    if any(size & (size - 1) for size in sizes) or rows % math.prod(sizes):
        return lax.psum(parts, axes)
    steps = halving_steps(axes)
    last = [step for step in steps if step[0] == axes[-1]]
    halving = steps[: len(steps) - len(last) + 1]
    doubling = steps[len(halving) :]
    joined = jnp.concatenate(parts, 0)
    for axis, stride in halving:
        pairs = [(i, i ^ stride) for i in range(lax.axis_size(axis))]
        bit = (lax.axis_index(axis) // stride) % 2
        half = joined.shape[0] // 2
        keep = lax.dynamic_slice_in_dim(joined, bit * half, half, 0)
        send = lax.dynamic_slice_in_dim(joined, (1 - bit) * half, half, 0)
        joined = keep + lax.ppermute(send, axis, pairs)
    for axis, stride in doubling:
        pairs = [(i, i ^ stride) for i in range(lax.axis_size(axis))]
        joined = joined + lax.ppermute(joined, axis, pairs)
    joined = doubling_gather(joined, halving)
    out = []
    start = 0
    for part in parts:
        out.append(joined[start : start + part.shape[0]])
        start += part.shape[0]
    return tuple(out)


def fetch_regions(memory_local, owners, local_ids, axis, held):
    count = lax.axis_size(axis)
    entries = owners.shape[0]
    me = lax.axis_index(axis)
    order = jnp.arange(entries)
    earlier = order[None, :] < order[:, None]
    tables, slot_of = tree_gather(jnp.stack([owners, local_ids])[None], axis)
    tables = tables[jnp.array([slot_of(device) for device in range(count)])]
    tables, held = lax.optimization_barrier((tables, held))
    mine = tables[:, 0] == me
    rank_here = jnp.sum(mine[:, None, :] & earlier[None], axis=2)
    wanted = mine[:, :, None] & (rank_here[:, :, None] == jnp.arange(CAP)[None, None, :])
    asked = jnp.sum(jnp.where(wanted, tables[:, 1][:, :, None], 0), axis=1)
    sent = jnp.take(memory_local, asked.reshape(-1), axis=0)
    sent = sent.reshape((count, CAP) + memory_local.shape[1:])
    received = lax.all_to_all(sent, axis, 0, 0, tiled=True)
    received = received.reshape((count * CAP,) + memory_local.shape[1:])
    same = owners[:, None] == owners[None, :]
    rank = jnp.sum(same & earlier, axis=1)
    return jnp.take(received, owners * CAP + rank, axis=0), held


def on_device(
    patches, w_query, w_key, w_value, w_out, region_memory, region_owner, region_local, grad_out
):
    tile_rows, tile_cols, model_width = patches.shape
    block_rows, block_cols = (tile_rows // BSIDE, tile_cols // BSIDE)
    block_count = block_rows * block_cols
    flat_in = patches.reshape(-1, model_width)
    owners = region_owner.reshape(2 * block_count)
    local_ids = region_local.reshape(2 * block_count)
    memory_local = region_memory.reshape(
        region_memory.shape[2], region_memory.shape[3], region_memory.shape[4]
    )
    fetched, flat_in = fetch_regions(memory_local, owners, local_ids, "gx", flat_in)
    w_pair = jnp.concatenate([w_key, w_value], 1)
    queries = jnp.dot(flat_in, w_query, preferred_element_type=jnp.float32).astype(jnp.bfloat16)
    keyvals = jnp.dot(flat_in, w_pair, preferred_element_type=jnp.float32).astype(jnp.bfloat16)
    keyvals = keyvals.reshape(tile_rows, tile_cols, 2 * model_width)
    keyval_grid = padded(keyvals, (("gx", 0), ("gy", 1)), BSIDE)
    keyval_pad = to_blocks(keyval_grid)
    gx_count = lax.axis_size("gx")
    gy_count = lax.axis_size("gy")
    row_ids = lax.axis_index("gx") * block_rows - 1 + jnp.arange(block_rows + 2, dtype=jnp.int32)
    col_ids = lax.axis_index("gy") * block_cols - 1 + jnp.arange(block_cols + 2, dtype=jnp.int32)
    row_valid = (row_ids >= 0) & (row_ids < block_rows * gx_count)
    col_valid = (col_ids >= 0) & (col_ids < block_cols * gy_count)
    key_valid = row_valid[:, None] & col_valid[None, :]
    region_keyval = fetched.reshape(
        block_rows, block_cols, 2, memory_local.shape[1], memory_local.shape[2]
    )
    query_blocks = to_blocks(queries.reshape(tile_rows, tile_cols, model_width))
    outputs, log_totals = attend_forward(query_blocks, keyval_pad, key_valid, region_keyval)
    attended = from_blocks(outputs).reshape(-1, model_width)
    layer_out = jnp.dot(attended, w_out, preferred_element_type=jnp.float32).astype(jnp.bfloat16)
    grad_flat = grad_out.reshape(-1, model_width)
    d_attended = jnp.dot(grad_flat, w_out.T, preferred_element_type=jnp.float32).astype(
        jnp.bfloat16
    )
    grad_out_local = inner_rows(attended, grad_flat)
    dout_blocks = to_blocks(d_attended.reshape(tile_rows, tile_cols, model_width))
    delta_rows = jnp.sum(
        split_heads(dout_blocks).astype(jnp.float32) * split_heads(outputs).astype(jnp.float32), -1
    )
    delta_rows = delta_rows.transpose(0, 1, 3, 2)
    d_queries = query_grads(
        query_blocks, keyval_pad, key_valid, region_keyval, log_totals, dout_blocks, delta_rows
    )
    query_grid = jnp.concatenate(
        [
            queries.reshape(tile_rows, tile_cols, model_width),
            d_attended.reshape(tile_rows, tile_cols, model_width),
        ],
        -1,
    )
    query_halo = padded(query_grid, (("gx", 0), ("gy", 1)), BSIDE)
    stat_grid = from_blocks(jnp.concatenate([log_totals, delta_rows], 2).transpose(0, 1, 3, 2))
    stat_halo = padded(stat_grid, (("gx", 0), ("gy", 1)), BSIDE)
    query_all = to_blocks(query_halo)
    stat_pad = to_blocks(stat_halo).transpose(0, 1, 3, 2)
    d_keys, d_values = key_grads(
        keyval_pad[1:-1, 1:-1],
        query_all[..., :model_width],
        query_all[..., model_width:],
        stat_pad[:, :, :HEADS],
        stat_pad[:, :, HEADS:],
        key_valid,
    )
    dq_flat = from_blocks(d_queries).reshape(-1, model_width)
    dk_flat = from_blocks(d_keys).reshape(-1, model_width)
    dv_flat = from_blocks(d_values).reshape(-1, model_width)
    grads_joined = jnp.concatenate([dq_flat, dk_flat, dv_flat], 1)
    w_stacked = jnp.concatenate([w_query.T, w_key.T, w_value.T], 0)
    grad_patches = jnp.dot(grads_joined, w_stacked, preferred_element_type=jnp.float32).astype(
        jnp.bfloat16
    )
    partials = (
        inner_rows(flat_in, dq_flat),
        inner_rows(flat_in, dk_flat),
        inner_rows(flat_in, dv_flat),
        grad_out_local,
    )
    summed = tree_sum(partials, ("gy", "gx"))
    return (
        layer_out.reshape(tile_rows, tile_cols, model_width),
        grad_patches.reshape(tile_rows, tile_cols, model_width),
        summed[0],
        summed[1],
        summed[2],
        summed[3],
    )


def solution(mesh):
    return jax.shard_map(
        on_device,
        mesh=mesh,
        in_specs=(
            P("gx", "gy", None),
            P(),
            P(),
            P(),
            P(),
            P("gx", "gy", None, None, None),
            P("gx", "gy", None, None),
            P("gx", "gy", None, None),
            P("gx", "gy", None),
        ),
        out_specs=(P("gx", "gy", None), P("gx", "gy", None), P(), P(), P(), P()),
        check_vma=False,
    )
```

```python
import math

import jax
import jax.numpy as jnp
from jax import lax
from jax.sharding import PartitionSpec as P

D = 256
HEADS = 2
HEAD_DIM = 128
BSIDE = 8
BT = 64
CAP = 2


masked_score = -1000000000.0


def padded(block, sides, width):
    for axis, dim in sides:
        count = lax.axis_size(axis)
        forward = [(i, i + 1) for i in range(count - 1)]
        backward = [(target, source) for source, target in forward]
        low = lax.ppermute(
            lax.slice_in_dim(block, block.shape[dim] - width, None, axis=dim), axis, forward
        )
        high = lax.ppermute(lax.slice_in_dim(block, 0, width, axis=dim), axis, backward)
        block = jnp.concatenate([low, block, high], axis=dim)
    return block


def to_blocks(grid_array):
    grid_rows, grid_cols, feature_width = grid_array.shape
    shaped = grid_array.reshape(grid_rows // BSIDE, BSIDE, grid_cols // BSIDE, BSIDE, feature_width)
    return shaped.transpose(0, 2, 1, 3, 4).reshape(
        grid_rows // BSIDE, grid_cols // BSIDE, BSIDE * BSIDE, feature_width
    )


def from_blocks(block_array):
    block_rows, block_cols, block_tokens, feature_width = block_array.shape
    shaped = block_array.reshape(block_rows, block_cols, BSIDE, BSIDE, feature_width)
    return shaped.transpose(0, 2, 1, 3, 4).reshape(
        block_rows * BSIDE, block_cols * BSIDE, feature_width
    )


def split_heads(source):
    return source.reshape(source.shape[:-1] + (HEADS, source.shape[-1] // HEADS))


def neighbour_set(padded_blocks, valid_blocks, block_rows, block_cols, axis):
    parts = []
    valid = []
    for row_off in range(3):
        for col_off in range(3):
            part = padded_blocks[row_off : row_off + block_rows, col_off : col_off + block_cols]
            parts.append(part)
            mask = valid_blocks[row_off : row_off + block_rows, col_off : col_off + block_cols]
            valid.append(jnp.broadcast_to(mask[:, :, None], (block_rows, block_cols, BT)))
    return jnp.concatenate(parts, axis), jnp.concatenate(valid, 2)


def key_set(keyval_pad, key_valid, region_keyval):
    block_rows, block_cols = (region_keyval.shape[0], region_keyval.shape[1])
    keyvals, valid = neighbour_set(keyval_pad, key_valid, block_rows, block_cols, 2)
    merged = region_keyval.reshape(block_rows, block_cols, 2 * BT, 2 * D)
    keyvals = jnp.concatenate([keyvals, merged], 2)
    valid = jnp.concatenate([valid, jnp.ones((block_rows, block_cols, 2 * BT), jnp.bool_)], 2)
    return keyvals[..., :D], keyvals[..., D:], valid


def set_scores(query_heads, key_part, valid):
    scores = jnp.einsum(
        "abqhe,abkhe->abhqk", query_heads, split_heads(key_part), preferred_element_type=jnp.float32
    )
    scores = scores * (1.0 / math.sqrt(HEAD_DIM))
    return jnp.where(valid[:, :, None, None, :], scores, masked_score)


def attend_forward(query_blocks, keyval_pad, key_valid, region_keyval):
    query_heads = split_heads(query_blocks)
    key_part, value_part, valid = key_set(keyval_pad, key_valid, region_keyval)
    scores = set_scores(query_heads, key_part, valid)
    row_top = jnp.max(scores, -1, keepdims=True)
    row_total = jnp.sum(jnp.exp(scores - row_top), -1, keepdims=True)
    log_total = row_top + jnp.log(row_total)
    weights = jnp.exp(scores - log_total).astype(jnp.bfloat16)
    mixed_sum = jnp.einsum(
        "abhqk,abkhe->abqhe", weights, split_heads(value_part), preferred_element_type=jnp.float32
    )
    output = mixed_sum.reshape(query_blocks.shape).astype(jnp.bfloat16)
    return (output, log_total[..., 0])


def query_grads(
    query_blocks, keyval_pad, key_valid, region_keyval, log_total, dout_blocks, delta_rows
):
    query_heads = split_heads(query_blocks)
    dout_heads = split_heads(dout_blocks)
    key_part, value_part, valid = key_set(keyval_pad, key_valid, region_keyval)
    scores = set_scores(query_heads, key_part, valid)
    prob = jnp.exp(scores - log_total[..., None])
    grad_prob = jnp.einsum(
        "abqhe,abkhe->abhqk", dout_heads, split_heads(value_part), preferred_element_type=jnp.float32
    )
    grad_score = (prob * (grad_prob - delta_rows[..., None])).astype(jnp.bfloat16)
    accum_sum = jnp.einsum(
        "abhqk,abkhe->abqhe", grad_score, split_heads(key_part), preferred_element_type=jnp.float32
    )
    return (
        (accum_sum * (1.0 / math.sqrt(HEAD_DIM))).reshape(query_blocks.shape).astype(jnp.bfloat16)
    )


def key_grads(keyval_center, query_pad, dout_pad, log_pad, delta_pad, query_valid):
    block_rows, block_cols = (keyval_center.shape[0], keyval_center.shape[1])
    key_heads = split_heads(keyval_center[..., :D])
    value_heads = split_heads(keyval_center[..., D:])
    queries, valid = neighbour_set(query_pad, query_valid, block_rows, block_cols, 2)
    douts, _ = neighbour_set(dout_pad, query_valid, block_rows, block_cols, 2)
    logs, _ = neighbour_set(log_pad, query_valid, block_rows, block_cols, 3)
    deltas, _ = neighbour_set(delta_pad, query_valid, block_rows, block_cols, 3)
    query_heads = split_heads(queries)
    dout_heads = split_heads(douts)
    scores = jnp.einsum(
        "abqhe,abkhe->abhqk", query_heads, key_heads, preferred_element_type=jnp.float32
    )
    scores = scores * (1.0 / math.sqrt(HEAD_DIM))
    prob = jnp.where(valid[:, :, None, :, None], jnp.exp(scores - logs[..., None]), 0.0)
    grad_prob = jnp.einsum(
        "abqhe,abkhe->abhqk", dout_heads, value_heads, preferred_element_type=jnp.float32
    )
    grad_score = (prob * (grad_prob - deltas[..., None])).astype(jnp.bfloat16)
    grad_key = jnp.einsum(
        "abhqk,abqhe->abkhe", grad_score, query_heads, preferred_element_type=jnp.float32
    )
    grad_value = jnp.einsum(
        "abhqk,abqhe->abkhe", prob.astype(jnp.bfloat16), dout_heads, preferred_element_type=jnp.float32
    )
    out_shape = (block_rows, block_cols, BT, D)
    grad_key = (grad_key * (1.0 / math.sqrt(HEAD_DIM))).reshape(out_shape).astype(jnp.bfloat16)
    return (grad_key, grad_value.reshape(out_shape).astype(jnp.bfloat16))


def inner_rows(left_rows, right_rows):
    return lax.dot_general(
        left_rows, right_rows, (((0,), (0,)), ((), ())), preferred_element_type=jnp.float32
    )


def halving_steps(axes):
    steps = []
    for axis in axes:
        count = lax.axis_size(axis)
        stride = 1
        while stride < count:
            steps.append((axis, stride))
            stride *= 2
    return steps


def doubling_gather(joined, steps):
    for axis, stride in reversed(steps):
        pairs = [(i, i ^ stride) for i in range(lax.axis_size(axis))]
        bit = (lax.axis_index(axis) // stride) % 2
        got = lax.ppermute(joined, axis, pairs)
        low = jnp.where(bit == 0, joined, got)
        high = jnp.where(bit == 0, got, joined)
        joined = jnp.concatenate([low, high], 0)
    return joined


def tree_gather(block, axis):
    count = lax.axis_size(axis)
    if count & (count - 1):
        return lax.all_gather(block, axis, axis=0, tiled=True), lambda index: index
    width = count.bit_length() - 1

    def slot_of(index):
        return sum(((index >> bit) & 1) << (width - 1 - bit) for bit in range(width))

    return doubling_gather(block, halving_steps((axis,))), slot_of


def tree_sum(parts, axes):
    sizes = [lax.axis_size(axis) for axis in axes]
    rows = sum(part.shape[0] for part in parts)
    if any(size & (size - 1) for size in sizes) or rows % math.prod(sizes):
        return lax.psum(parts, axes)
    steps = halving_steps(axes)
    last = [step for step in steps if step[0] == axes[-1]]
    halving = steps[: len(steps) - len(last) + 1]
    doubling = steps[len(halving) :]
    joined = jnp.concatenate(parts, 0)
    for axis, stride in halving:
        pairs = [(i, i ^ stride) for i in range(lax.axis_size(axis))]
        bit = (lax.axis_index(axis) // stride) % 2
        half = joined.shape[0] // 2
        keep = lax.dynamic_slice_in_dim(joined, bit * half, half, 0)
        send = lax.dynamic_slice_in_dim(joined, (1 - bit) * half, half, 0)
        joined = keep + lax.ppermute(send, axis, pairs)
    for axis, stride in doubling:
        pairs = [(i, i ^ stride) for i in range(lax.axis_size(axis))]
        joined = joined + lax.ppermute(joined, axis, pairs)
    joined = doubling_gather(joined, halving)
    out = []
    start = 0
    for part in parts:
        out.append(joined[start : start + part.shape[0]])
        start += part.shape[0]
    return tuple(out)


def fetch_regions(memory_local, owners, local_ids, axis):
    count = lax.axis_size(axis)
    entries = owners.shape[0]
    me = lax.axis_index(axis)
    order = jnp.arange(entries)
    earlier = order[None, :] < order[:, None]
    tables, slot_of = tree_gather(jnp.stack([owners, local_ids])[None], axis)
    tables = tables[jnp.array([slot_of(device) for device in range(count)])]
    mine = tables[:, 0] == me
    rank_here = jnp.sum(mine[:, None, :] & earlier[None], axis=2)
    wanted = mine[:, :, None] & (rank_here[:, :, None] == jnp.arange(CAP)[None, None, :])
    asked = jnp.sum(jnp.where(wanted, tables[:, 1][:, :, None], 0), axis=1)
    sent = jnp.take(memory_local, asked.reshape(-1), axis=0)
    sent = sent.reshape((count, CAP) + memory_local.shape[1:])
    width = memory_local.shape[-1] // 2
    same = owners[:, None] == owners[None, :]
    rank = jnp.sum(same & earlier, axis=1)
    halves = []
    for half in (sent[..., :width], sent[..., width:]):
        received = lax.all_to_all(half, axis, 0, 0, tiled=True)
        received = received.reshape((count * CAP,) + half.shape[2:])
        halves.append(jnp.take(received, owners * CAP + rank, axis=0))
    return jnp.concatenate(halves, -1)


def on_device(
    patches, w_query, w_key, w_value, w_out, region_memory, region_owner, region_local, grad_out
):
    tile_rows, tile_cols, model_width = patches.shape
    block_rows, block_cols = (tile_rows // BSIDE, tile_cols // BSIDE)
    block_count = block_rows * block_cols
    flat_in = patches.reshape(-1, model_width)
    w_pair = jnp.concatenate([w_key, w_value], 1)
    queries = jnp.dot(flat_in, w_query, preferred_element_type=jnp.float32).astype(jnp.bfloat16)
    keyvals = jnp.dot(flat_in, w_pair, preferred_element_type=jnp.float32).astype(jnp.bfloat16)
    keyvals = keyvals.reshape(tile_rows, tile_cols, 2 * model_width)
    keyval_grid = padded(keyvals, (("gx", 0), ("gy", 1)), BSIDE)
    keyval_pad = to_blocks(keyval_grid)
    gx_count = lax.axis_size("gx")
    gy_count = lax.axis_size("gy")
    row_ids = lax.axis_index("gx") * block_rows - 1 + jnp.arange(block_rows + 2, dtype=jnp.int32)
    col_ids = lax.axis_index("gy") * block_cols - 1 + jnp.arange(block_cols + 2, dtype=jnp.int32)
    row_valid = (row_ids >= 0) & (row_ids < block_rows * gx_count)
    col_valid = (col_ids >= 0) & (col_ids < block_cols * gy_count)
    key_valid = row_valid[:, None] & col_valid[None, :]
    owners = region_owner.reshape(2 * block_count)
    local_ids = region_local.reshape(2 * block_count)
    memory_local = region_memory.reshape(
        region_memory.shape[2], region_memory.shape[3], region_memory.shape[4]
    )
    fetched = fetch_regions(memory_local, owners, local_ids, "gx")
    region_keyval = fetched.reshape(
        block_rows, block_cols, 2, memory_local.shape[1], memory_local.shape[2]
    )
    query_blocks = to_blocks(queries.reshape(tile_rows, tile_cols, model_width))
    outputs, log_totals = attend_forward(query_blocks, keyval_pad, key_valid, region_keyval)
    attended = from_blocks(outputs).reshape(-1, model_width)
    layer_out = jnp.dot(attended, w_out, preferred_element_type=jnp.float32).astype(jnp.bfloat16)
    grad_flat = grad_out.reshape(-1, model_width)
    d_attended = jnp.dot(grad_flat, w_out.T, preferred_element_type=jnp.float32).astype(
        jnp.bfloat16
    )
    grad_out_local = inner_rows(attended, grad_flat)
    dout_blocks = to_blocks(d_attended.reshape(tile_rows, tile_cols, model_width))
    delta_rows = jnp.sum(
        split_heads(dout_blocks).astype(jnp.float32) * split_heads(outputs).astype(jnp.float32), -1
    )
    delta_rows = delta_rows.transpose(0, 1, 3, 2)
    d_queries = query_grads(
        query_blocks, keyval_pad, key_valid, region_keyval, log_totals, dout_blocks, delta_rows
    )
    query_grid = jnp.concatenate(
        [
            queries.reshape(tile_rows, tile_cols, model_width),
            d_attended.reshape(tile_rows, tile_cols, model_width),
        ],
        -1,
    )
    query_halo = padded(query_grid, (("gx", 0), ("gy", 1)), BSIDE)
    stat_grid = from_blocks(jnp.concatenate([log_totals, delta_rows], 2).transpose(0, 1, 3, 2))
    stat_halo = padded(stat_grid, (("gx", 0), ("gy", 1)), BSIDE)
    query_all = to_blocks(query_halo)
    stat_pad = to_blocks(stat_halo).transpose(0, 1, 3, 2)
    d_keys, d_values = key_grads(
        keyval_pad[1:-1, 1:-1],
        query_all[..., :model_width],
        query_all[..., model_width:],
        stat_pad[:, :, :HEADS],
        stat_pad[:, :, HEADS:],
        key_valid,
    )
    dq_flat = from_blocks(d_queries).reshape(-1, model_width)
    dk_flat = from_blocks(d_keys).reshape(-1, model_width)
    dv_flat = from_blocks(d_values).reshape(-1, model_width)
    grads_joined = jnp.concatenate([dq_flat, dk_flat, dv_flat], 1)
    w_stacked = jnp.concatenate([w_query.T, w_key.T, w_value.T], 0)
    grad_patches = jnp.dot(grads_joined, w_stacked, preferred_element_type=jnp.float32).astype(
        jnp.bfloat16
    )
    partials = (
        inner_rows(flat_in, dq_flat),
        inner_rows(flat_in, dk_flat),
        inner_rows(flat_in, dv_flat),
        grad_out_local,
    )
    summed = tree_sum(partials, ("gy", "gx"))
    return (
        layer_out.reshape(tile_rows, tile_cols, model_width),
        grad_patches.reshape(tile_rows, tile_cols, model_width),
        summed[0],
        summed[1],
        summed[2],
        summed[3],
    )


def solution(mesh):
    return jax.shard_map(
        on_device,
        mesh=mesh,
        in_specs=(
            P("gx", "gy", None),
            P(),
            P(),
            P(),
            P(),
            P("gx", "gy", None, None, None),
            P("gx", "gy", None, None),
            P("gx", "gy", None, None),
            P("gx", "gy", None),
        ),
        out_specs=(P("gx", "gy", None), P("gx", "gy", None), P(), P(), P(), P()),
        check_vma=False,
    )
```

```python
import math

import jax
import jax.numpy as jnp
from jax import lax
from jax.sharding import PartitionSpec as P

D = 256
HEADS = 2
HEAD_DIM = 128
BSIDE = 8
BT = 64
CAP = 2


masked_score = -1000000000.0


def padded(block, sides, width):
    for axis, dim in sides:
        count = lax.axis_size(axis)
        forward = [(i, i + 1) for i in range(count - 1)]
        backward = [(target, source) for source, target in forward]
        low = lax.ppermute(
            lax.slice_in_dim(block, block.shape[dim] - width, None, axis=dim), axis, forward
        )
        high = lax.ppermute(lax.slice_in_dim(block, 0, width, axis=dim), axis, backward)
        block = jnp.concatenate([low, block, high], axis=dim)
    return block


def to_blocks(grid_array):
    grid_rows, grid_cols, feature_width = grid_array.shape
    shaped = grid_array.reshape(grid_rows // BSIDE, BSIDE, grid_cols // BSIDE, BSIDE, feature_width)
    return shaped.transpose(0, 2, 1, 3, 4).reshape(
        grid_rows // BSIDE, grid_cols // BSIDE, BSIDE * BSIDE, feature_width
    )


def from_blocks(block_array):
    block_rows, block_cols, block_tokens, feature_width = block_array.shape
    shaped = block_array.reshape(block_rows, block_cols, BSIDE, BSIDE, feature_width)
    return shaped.transpose(0, 2, 1, 3, 4).reshape(
        block_rows * BSIDE, block_cols * BSIDE, feature_width
    )


def split_heads(source):
    return source.reshape(source.shape[:-1] + (HEADS, source.shape[-1] // HEADS))


def neighbour_set(padded_blocks, valid_blocks, block_rows, block_cols, axis):
    parts = []
    valid = []
    for row_off in range(3):
        for col_off in range(3):
            part = padded_blocks[row_off : row_off + block_rows, col_off : col_off + block_cols]
            parts.append(part)
            mask = valid_blocks[row_off : row_off + block_rows, col_off : col_off + block_cols]
            valid.append(jnp.broadcast_to(mask[:, :, None], (block_rows, block_cols, BT)))
    return jnp.concatenate(parts, axis), jnp.concatenate(valid, 2)


def key_set(keyval_pad, key_valid, region_keyval):
    block_rows, block_cols = (region_keyval.shape[0], region_keyval.shape[1])
    keyvals, valid = neighbour_set(keyval_pad, key_valid, block_rows, block_cols, 2)
    merged = region_keyval.reshape(block_rows, block_cols, 2 * BT, 2 * D)
    return (keyvals[..., :D], keyvals[..., D:], valid), (merged[..., :D], merged[..., D:])


def set_scores(query_heads, near, region):
    near_keys, _, valid = near
    near_scores = jnp.einsum(
        "abqhe,abkhe->abhqk", query_heads, split_heads(near_keys), preferred_element_type=jnp.float32
    )
    near_scores = jnp.where(
        valid[:, :, None, None, :], near_scores * (1.0 / math.sqrt(HEAD_DIM)), masked_score
    )
    region_scores = jnp.einsum(
        "abqhe,abkhe->abhqk", query_heads, split_heads(region[0]), preferred_element_type=jnp.float32
    )
    region_scores = region_scores * (1.0 / math.sqrt(HEAD_DIM))
    return jnp.concatenate([near_scores, region_scores], -1)


def set_sum(weights, near_part, region_part):
    split = near_part.shape[2]
    near_sum = jnp.einsum(
        "abhqk,abkhe->abqhe",
        weights[..., :split],
        split_heads(near_part),
        preferred_element_type=jnp.float32,
    )
    region_sum = jnp.einsum(
        "abhqk,abkhe->abqhe",
        weights[..., split:],
        split_heads(region_part),
        preferred_element_type=jnp.float32,
    )
    return near_sum + region_sum


def attend_forward(query_blocks, keyval_pad, key_valid, region_keyval):
    query_heads = split_heads(query_blocks)
    near, region = key_set(keyval_pad, key_valid, region_keyval)
    scores = set_scores(query_heads, near, region)
    row_top = jnp.max(scores, -1, keepdims=True)
    row_total = jnp.sum(jnp.exp(scores - row_top), -1, keepdims=True)
    log_total = row_top + jnp.log(row_total)
    weights = jnp.exp(scores - log_total).astype(jnp.bfloat16)
    mixed_sum = set_sum(weights, near[1], region[1])
    output = mixed_sum.reshape(query_blocks.shape).astype(jnp.bfloat16)
    return (output, log_total[..., 0])


def query_grads(
    query_blocks, keyval_pad, key_valid, region_keyval, log_total, dout_blocks, delta_rows
):
    query_heads = split_heads(query_blocks)
    dout_heads = split_heads(dout_blocks)
    near, region = key_set(keyval_pad, key_valid, region_keyval)
    scores = set_scores(query_heads, near, region)
    prob = jnp.exp(scores - log_total[..., None])
    grad_prob = jnp.concatenate(
        [
            jnp.einsum(
                "abqhe,abkhe->abhqk",
                dout_heads,
                split_heads(part),
                preferred_element_type=jnp.float32,
            )
            for part in (near[1], region[1])
        ],
        -1,
    )
    grad_score = (prob * (grad_prob - delta_rows[..., None])).astype(jnp.bfloat16)
    accum_sum = set_sum(grad_score, near[0], region[0])
    return (
        (accum_sum * (1.0 / math.sqrt(HEAD_DIM))).reshape(query_blocks.shape).astype(jnp.bfloat16)
    )


def key_grads(keyval_center, query_pad, dout_pad, log_pad, delta_pad, query_valid):
    block_rows, block_cols = (keyval_center.shape[0], keyval_center.shape[1])
    key_heads = split_heads(keyval_center[..., :D])
    value_heads = split_heads(keyval_center[..., D:])
    queries, valid = neighbour_set(query_pad, query_valid, block_rows, block_cols, 2)
    douts, _ = neighbour_set(dout_pad, query_valid, block_rows, block_cols, 2)
    logs, _ = neighbour_set(log_pad, query_valid, block_rows, block_cols, 3)
    deltas, _ = neighbour_set(delta_pad, query_valid, block_rows, block_cols, 3)
    query_heads = split_heads(queries)
    dout_heads = split_heads(douts)
    scores = jnp.einsum(
        "abqhe,abkhe->abhqk", query_heads, key_heads, preferred_element_type=jnp.float32
    )
    scores = scores * (1.0 / math.sqrt(HEAD_DIM))
    prob = jnp.where(valid[:, :, None, :, None], jnp.exp(scores - logs[..., None]), 0.0)
    grad_prob = jnp.einsum(
        "abqhe,abkhe->abhqk", dout_heads, value_heads, preferred_element_type=jnp.float32
    )
    grad_score = (prob * (grad_prob - deltas[..., None])).astype(jnp.bfloat16)
    grad_key = jnp.einsum(
        "abhqk,abqhe->abkhe", grad_score, query_heads, preferred_element_type=jnp.float32
    )
    grad_value = jnp.einsum(
        "abhqk,abqhe->abkhe", prob.astype(jnp.bfloat16), dout_heads, preferred_element_type=jnp.float32
    )
    out_shape = (block_rows, block_cols, BT, D)
    grad_key = (grad_key * (1.0 / math.sqrt(HEAD_DIM))).reshape(out_shape).astype(jnp.bfloat16)
    return (grad_key, grad_value.reshape(out_shape).astype(jnp.bfloat16))


def inner_rows(left_rows, right_rows):
    return lax.dot_general(
        left_rows, right_rows, (((0,), (0,)), ((), ())), preferred_element_type=jnp.float32
    )


def halving_steps(axes):
    steps = []
    for axis in axes:
        count = lax.axis_size(axis)
        stride = 1
        while stride < count:
            steps.append((axis, stride))
            stride *= 2
    return steps


def doubling_gather(joined, steps):
    for axis, stride in reversed(steps):
        pairs = [(i, i ^ stride) for i in range(lax.axis_size(axis))]
        bit = (lax.axis_index(axis) // stride) % 2
        got = lax.ppermute(joined, axis, pairs)
        low = jnp.where(bit == 0, joined, got)
        high = jnp.where(bit == 0, got, joined)
        joined = jnp.concatenate([low, high], 0)
    return joined


def tree_gather(block, axis):
    count = lax.axis_size(axis)
    if count & (count - 1):
        return lax.all_gather(block, axis, axis=0, tiled=True), lambda index: index
    width = count.bit_length() - 1

    def slot_of(index):
        return sum(((index >> bit) & 1) << (width - 1 - bit) for bit in range(width))

    return doubling_gather(block, halving_steps((axis,))), slot_of


def tree_sum(parts, axes):
    sizes = [lax.axis_size(axis) for axis in axes]
    rows = sum(part.shape[0] for part in parts)
    if any(size & (size - 1) for size in sizes) or rows % math.prod(sizes):
        return lax.psum(parts, axes)
    steps = halving_steps(axes)
    last = [step for step in steps if step[0] == axes[-1]]
    halving = steps[: len(steps) - len(last) + 1]
    doubling = steps[len(halving) :]
    joined = jnp.concatenate(parts, 0)
    for axis, stride in halving:
        pairs = [(i, i ^ stride) for i in range(lax.axis_size(axis))]
        bit = (lax.axis_index(axis) // stride) % 2
        half = joined.shape[0] // 2
        keep = lax.dynamic_slice_in_dim(joined, bit * half, half, 0)
        send = lax.dynamic_slice_in_dim(joined, (1 - bit) * half, half, 0)
        joined = keep + lax.ppermute(send, axis, pairs)
    for axis, stride in doubling:
        pairs = [(i, i ^ stride) for i in range(lax.axis_size(axis))]
        joined = joined + lax.ppermute(joined, axis, pairs)
    joined = doubling_gather(joined, halving)
    out = []
    start = 0
    for part in parts:
        out.append(joined[start : start + part.shape[0]])
        start += part.shape[0]
    return tuple(out)


def fetch_regions(memory_local, owners, local_ids, axis):
    count = lax.axis_size(axis)
    entries = owners.shape[0]
    me = lax.axis_index(axis)
    order = jnp.arange(entries)
    earlier = order[None, :] < order[:, None]
    tables, slot_of = tree_gather(jnp.stack([owners, local_ids])[None], axis)
    tables = tables[jnp.array([slot_of(device) for device in range(count)])]
    mine = tables[:, 0] == me
    rank_here = jnp.sum(mine[:, None, :] & earlier[None], axis=2)
    wanted = mine[:, :, None] & (rank_here[:, :, None] == jnp.arange(CAP)[None, None, :])
    asked = jnp.sum(jnp.where(wanted, tables[:, 1][:, :, None], 0), axis=1)
    sent = jnp.take(memory_local, asked.reshape(-1), axis=0)
    sent = sent.reshape((count, CAP) + memory_local.shape[1:])
    received = lax.all_to_all(sent, axis, 0, 0, tiled=True)
    received = received.reshape((count * CAP,) + memory_local.shape[1:])
    same = owners[:, None] == owners[None, :]
    rank = jnp.sum(same & earlier, axis=1)
    return jnp.take(received, owners * CAP + rank, axis=0)


def on_device(
    patches, w_query, w_key, w_value, w_out, region_memory, region_owner, region_local, grad_out
):
    tile_rows, tile_cols, model_width = patches.shape
    block_rows, block_cols = (tile_rows // BSIDE, tile_cols // BSIDE)
    block_count = block_rows * block_cols
    flat_in = patches.reshape(-1, model_width)
    w_pair = jnp.concatenate([w_key, w_value], 1)
    queries = jnp.dot(flat_in, w_query, preferred_element_type=jnp.float32).astype(jnp.bfloat16)
    keyvals = jnp.dot(flat_in, w_pair, preferred_element_type=jnp.float32).astype(jnp.bfloat16)
    keyvals = keyvals.reshape(tile_rows, tile_cols, 2 * model_width)
    keyval_grid = padded(keyvals, (("gx", 0), ("gy", 1)), BSIDE)
    keyval_pad = to_blocks(keyval_grid)
    gx_count = lax.axis_size("gx")
    gy_count = lax.axis_size("gy")
    row_ids = lax.axis_index("gx") * block_rows - 1 + jnp.arange(block_rows + 2, dtype=jnp.int32)
    col_ids = lax.axis_index("gy") * block_cols - 1 + jnp.arange(block_cols + 2, dtype=jnp.int32)
    row_valid = (row_ids >= 0) & (row_ids < block_rows * gx_count)
    col_valid = (col_ids >= 0) & (col_ids < block_cols * gy_count)
    key_valid = row_valid[:, None] & col_valid[None, :]
    owners = region_owner.reshape(2 * block_count)
    local_ids = region_local.reshape(2 * block_count)
    memory_local = region_memory.reshape(
        region_memory.shape[2], region_memory.shape[3], region_memory.shape[4]
    )
    fetched = fetch_regions(memory_local, owners, local_ids, "gx")
    region_keyval = fetched.reshape(
        block_rows, block_cols, 2, memory_local.shape[1], memory_local.shape[2]
    )
    query_blocks = to_blocks(queries.reshape(tile_rows, tile_cols, model_width))
    outputs, log_totals = attend_forward(query_blocks, keyval_pad, key_valid, region_keyval)
    attended = from_blocks(outputs).reshape(-1, model_width)
    layer_out = jnp.dot(attended, w_out, preferred_element_type=jnp.float32).astype(jnp.bfloat16)
    grad_flat = grad_out.reshape(-1, model_width)
    d_attended = jnp.dot(grad_flat, w_out.T, preferred_element_type=jnp.float32).astype(
        jnp.bfloat16
    )
    grad_out_local = inner_rows(attended, grad_flat)
    dout_blocks = to_blocks(d_attended.reshape(tile_rows, tile_cols, model_width))
    delta_rows = jnp.sum(
        split_heads(dout_blocks).astype(jnp.float32) * split_heads(outputs).astype(jnp.float32), -1
    )
    delta_rows = delta_rows.transpose(0, 1, 3, 2)
    d_queries = query_grads(
        query_blocks, keyval_pad, key_valid, region_keyval, log_totals, dout_blocks, delta_rows
    )
    query_grid = jnp.concatenate(
        [
            queries.reshape(tile_rows, tile_cols, model_width),
            d_attended.reshape(tile_rows, tile_cols, model_width),
        ],
        -1,
    )
    query_halo = padded(query_grid, (("gx", 0), ("gy", 1)), BSIDE)
    stat_grid = from_blocks(jnp.concatenate([log_totals, delta_rows], 2).transpose(0, 1, 3, 2))
    stat_halo = padded(stat_grid, (("gx", 0), ("gy", 1)), BSIDE)
    query_all = to_blocks(query_halo)
    stat_pad = to_blocks(stat_halo).transpose(0, 1, 3, 2)
    d_keys, d_values = key_grads(
        keyval_pad[1:-1, 1:-1],
        query_all[..., :model_width],
        query_all[..., model_width:],
        stat_pad[:, :, :HEADS],
        stat_pad[:, :, HEADS:],
        key_valid,
    )
    dq_flat = from_blocks(d_queries).reshape(-1, model_width)
    dk_flat = from_blocks(d_keys).reshape(-1, model_width)
    dv_flat = from_blocks(d_values).reshape(-1, model_width)
    grads_joined = jnp.concatenate([dq_flat, dk_flat, dv_flat], 1)
    w_stacked = jnp.concatenate([w_query.T, w_key.T, w_value.T], 0)
    grad_patches = jnp.dot(grads_joined, w_stacked, preferred_element_type=jnp.float32).astype(
        jnp.bfloat16
    )
    partials = (
        inner_rows(flat_in, dq_flat),
        inner_rows(flat_in, dk_flat),
        inner_rows(flat_in, dv_flat),
        grad_out_local,
    )
    summed = tree_sum(partials, ("gy", "gx"))
    return (
        layer_out.reshape(tile_rows, tile_cols, model_width),
        grad_patches.reshape(tile_rows, tile_cols, model_width),
        summed[0],
        summed[1],
        summed[2],
        summed[3],
    )


def solution(mesh):
    return jax.shard_map(
        on_device,
        mesh=mesh,
        in_specs=(
            P("gx", "gy", None),
            P(),
            P(),
            P(),
            P(),
            P("gx", "gy", None, None, None),
            P("gx", "gy", None, None),
            P("gx", "gy", None, None),
            P("gx", "gy", None),
        ),
        out_specs=(P("gx", "gy", None), P("gx", "gy", None), P(), P(), P(), P()),
        check_vma=False,
    )
```

```python
import math

import jax
import jax.numpy as jnp
from jax import lax
from jax.sharding import PartitionSpec as P

D = 256
HEADS = 2
HEAD_DIM = 128
BSIDE = 8
BT = 64
CAP = 2


masked_score = -1000000000.0


def padded(block, sides, width):
    for axis, dim in sides:
        count = lax.axis_size(axis)
        forward = [(i, i + 1) for i in range(count - 1)]
        backward = [(target, source) for source, target in forward]
        low = lax.ppermute(
            lax.slice_in_dim(block, block.shape[dim] - width, None, axis=dim), axis, forward
        )
        high = lax.ppermute(lax.slice_in_dim(block, 0, width, axis=dim), axis, backward)
        block = jnp.concatenate([low, block, high], axis=dim)
    return block


def to_blocks(grid_array):
    grid_rows, grid_cols, feature_width = grid_array.shape
    shaped = grid_array.reshape(grid_rows // BSIDE, BSIDE, grid_cols // BSIDE, BSIDE, feature_width)
    return shaped.transpose(0, 2, 1, 3, 4).reshape(
        grid_rows // BSIDE, grid_cols // BSIDE, BSIDE * BSIDE, feature_width
    )


def from_blocks(block_array):
    block_rows, block_cols, block_tokens, feature_width = block_array.shape
    shaped = block_array.reshape(block_rows, block_cols, BSIDE, BSIDE, feature_width)
    return shaped.transpose(0, 2, 1, 3, 4).reshape(
        block_rows * BSIDE, block_cols * BSIDE, feature_width
    )


def split_heads(source):
    return source.reshape(source.shape[:-1] + (HEADS, source.shape[-1] // HEADS))


def neighbour_set(padded_blocks, valid_blocks, block_rows, block_cols, axis):
    parts = []
    valid = []
    for row_off in range(3):
        for col_off in range(3):
            part = padded_blocks[row_off : row_off + block_rows, col_off : col_off + block_cols]
            parts.append(part)
            mask = valid_blocks[row_off : row_off + block_rows, col_off : col_off + block_cols]
            valid.append(jnp.broadcast_to(mask[:, :, None], (block_rows, block_cols, BT)))
    return jnp.concatenate(parts, axis), jnp.concatenate(valid, 2)


def key_set(keyval_pad, key_valid, region_keyval):
    block_rows, block_cols = (region_keyval.shape[0], region_keyval.shape[1])
    keyvals, valid = neighbour_set(keyval_pad, key_valid, block_rows, block_cols, 2)
    merged = region_keyval.reshape(block_rows, block_cols, 2 * BT, 2 * D)
    keyvals = jnp.concatenate([keyvals, merged], 2)
    valid = jnp.concatenate([valid, jnp.ones((block_rows, block_cols, 2 * BT), jnp.bool_)], 2)
    return keyvals[..., :D], keyvals[..., D:], valid


def set_scores(query_heads, key_part, valid):
    scores = jnp.einsum(
        "abqhe,abkhe->abhqk", query_heads, split_heads(key_part), preferred_element_type=jnp.float32
    )
    scores = scores * (1.0 / math.sqrt(HEAD_DIM))
    return jnp.where(valid[:, :, None, None, :], scores, masked_score)


def attend_forward(query_blocks, keyval_pad, key_valid, region_keyval):
    query_heads = split_heads(query_blocks)
    key_part, value_part, valid = key_set(keyval_pad, key_valid, region_keyval)
    scores = set_scores(query_heads, key_part, valid)
    row_top = jnp.max(scores, -1, keepdims=True)
    row_total = jnp.sum(jnp.exp(scores - row_top), -1, keepdims=True)
    log_total = row_top + jnp.log(row_total)
    weights = jnp.exp(scores - log_total).astype(jnp.bfloat16)
    mixed_sum = jnp.einsum(
        "abhqk,abkhe->abqhe", weights, split_heads(value_part), preferred_element_type=jnp.float32
    )
    output = mixed_sum.reshape(query_blocks.shape).astype(jnp.bfloat16)
    return (output, log_total[..., 0])


def query_grads(
    query_blocks, keyval_pad, key_valid, region_keyval, log_total, dout_blocks, delta_rows
):
    query_heads = split_heads(query_blocks)
    dout_heads = split_heads(dout_blocks)
    key_part, value_part, valid = key_set(keyval_pad, key_valid, region_keyval)
    scores = set_scores(query_heads, key_part, valid)
    prob = jnp.exp(scores - log_total[..., None])
    grad_prob = jnp.einsum(
        "abqhe,abkhe->abhqk", dout_heads, split_heads(value_part), preferred_element_type=jnp.float32
    )
    grad_score = (prob * (grad_prob - delta_rows[..., None])).astype(jnp.bfloat16)
    accum_sum = jnp.einsum(
        "abhqk,abkhe->abqhe", grad_score, split_heads(key_part), preferred_element_type=jnp.float32
    )
    return (
        (accum_sum * (1.0 / math.sqrt(HEAD_DIM))).reshape(query_blocks.shape).astype(jnp.bfloat16)
    )


def key_grads(keyval_center, query_pad, dout_pad, log_pad, delta_pad, query_valid):
    block_rows, block_cols = (keyval_center.shape[0], keyval_center.shape[1])
    key_heads = split_heads(keyval_center[..., :D])
    value_heads = split_heads(keyval_center[..., D:])
    queries, valid = neighbour_set(query_pad, query_valid, block_rows, block_cols, 2)
    douts, _ = neighbour_set(dout_pad, query_valid, block_rows, block_cols, 2)
    logs, _ = neighbour_set(log_pad, query_valid, block_rows, block_cols, 3)
    deltas, _ = neighbour_set(delta_pad, query_valid, block_rows, block_cols, 3)
    query_heads = split_heads(queries)
    dout_heads = split_heads(douts)
    scores = jnp.einsum(
        "abqhe,abkhe->abhqk", query_heads, key_heads, preferred_element_type=jnp.float32
    )
    scores = scores * (1.0 / math.sqrt(HEAD_DIM))
    prob = jnp.where(valid[:, :, None, :, None], jnp.exp(scores - logs[..., None]), 0.0)
    grad_prob = jnp.einsum(
        "abqhe,abkhe->abhqk", dout_heads, value_heads, preferred_element_type=jnp.float32
    )
    grad_score = (prob * (grad_prob - deltas[..., None])).astype(jnp.bfloat16)
    grad_key = jnp.einsum(
        "abhqk,abqhe->abkhe", grad_score, query_heads, preferred_element_type=jnp.float32
    )
    grad_value = jnp.einsum(
        "abhqk,abqhe->abkhe", prob.astype(jnp.bfloat16), dout_heads, preferred_element_type=jnp.float32
    )
    out_shape = (block_rows, block_cols, BT, D)
    grad_key = (grad_key * (1.0 / math.sqrt(HEAD_DIM))).reshape(out_shape).astype(jnp.bfloat16)
    return (grad_key, grad_value.reshape(out_shape).astype(jnp.bfloat16))


def inner_rows(left_rows, right_rows):
    return lax.dot_general(
        left_rows, right_rows, (((0,), (0,)), ((), ())), preferred_element_type=jnp.float32
    )


def halving_steps(axes):
    steps = []
    for axis in axes:
        count = lax.axis_size(axis)
        stride = 1
        while stride < count:
            steps.append((axis, stride))
            stride *= 2
    return steps


def doubling_gather(joined, steps):
    for axis, stride in reversed(steps):
        pairs = [(i, i ^ stride) for i in range(lax.axis_size(axis))]
        bit = (lax.axis_index(axis) // stride) % 2
        got = lax.ppermute(joined, axis, pairs)
        low = jnp.where(bit == 0, joined, got)
        high = jnp.where(bit == 0, got, joined)
        joined = jnp.concatenate([low, high], 0)
    return joined


def tree_gather(block, axis):
    count = lax.axis_size(axis)
    if count & (count - 1):
        return lax.all_gather(block, axis, axis=0, tiled=True), lambda index: index
    width = count.bit_length() - 1

    def slot_of(index):
        return sum(((index >> bit) & 1) << (width - 1 - bit) for bit in range(width))

    return doubling_gather(block, halving_steps((axis,))), slot_of


def tree_sum(parts, axes):
    sizes = [lax.axis_size(axis) for axis in axes]
    rows = sum(part.shape[0] for part in parts)
    if any(size & (size - 1) for size in sizes) or rows % math.prod(sizes):
        return lax.psum(parts, axes)
    steps = halving_steps(axes)
    last = [step for step in steps if step[0] == axes[-1]]
    halving = steps[: len(steps) - len(last) + 1]
    doubling = steps[len(halving) :]
    joined = jnp.concatenate(parts, 0)
    for axis, stride in halving:
        pairs = [(i, i ^ stride) for i in range(lax.axis_size(axis))]
        bit = (lax.axis_index(axis) // stride) % 2
        half = joined.shape[0] // 2
        keep = lax.dynamic_slice_in_dim(joined, bit * half, half, 0)
        send = lax.dynamic_slice_in_dim(joined, (1 - bit) * half, half, 0)
        joined = keep + lax.ppermute(send, axis, pairs)
    for axis, stride in doubling:
        pairs = [(i, i ^ stride) for i in range(lax.axis_size(axis))]
        joined = joined + lax.ppermute(joined, axis, pairs)
    joined = doubling_gather(joined, halving)
    out = []
    start = 0
    for part in parts:
        out.append(joined[start : start + part.shape[0]])
        start += part.shape[0]
    return tuple(out)


def fetch_regions(memory_local, owners, local_ids, axis):
    count = lax.axis_size(axis)
    entries = owners.shape[0]
    me = lax.axis_index(axis)
    order = jnp.arange(entries)
    earlier = order[None, :] < order[:, None]
    tables, slot_of = tree_gather(jnp.stack([owners, local_ids])[None], axis)
    tables = tables[jnp.array([slot_of(device) for device in range(count)])]
    mine = tables[:, 0] == me
    rank_here = jnp.sum(mine[:, None, :] & earlier[None], axis=2)
    wanted = mine[:, :, None] & (rank_here[:, :, None] == jnp.arange(CAP)[None, None, :])
    asked = jnp.sum(jnp.where(wanted, tables[:, 1][:, :, None], 0), axis=1)
    sent = jnp.take(memory_local, asked.reshape(-1), axis=0)
    sent = sent.reshape((count, CAP) + memory_local.shape[1:])
    received = lax.all_to_all(sent, axis, 0, 0, tiled=True)
    received = received.reshape((count * CAP,) + memory_local.shape[1:])
    same = owners[:, None] == owners[None, :]
    rank = jnp.sum(same & earlier, axis=1)
    return jnp.take(received, owners * CAP + rank, axis=0)


def on_device(
    patches, w_query, w_key, w_value, w_out, region_memory, region_owner, region_local, grad_out
):
    tile_rows, tile_cols, model_width = patches.shape
    block_rows, block_cols = (tile_rows // BSIDE, tile_cols // BSIDE)
    block_count = block_rows * block_cols
    flat_in = patches.reshape(-1, model_width)
    w_pair = jnp.concatenate([w_key, w_value], 1)
    queries = jnp.dot(flat_in, w_query, preferred_element_type=jnp.float32).astype(jnp.bfloat16)
    keyvals = jnp.dot(flat_in, w_pair, preferred_element_type=jnp.float32).astype(jnp.bfloat16)
    keyvals = keyvals.reshape(tile_rows, tile_cols, 2 * model_width)
    keyval_grid = padded(keyvals, (("gx", 0), ("gy", 1)), BSIDE)
    keyval_pad = to_blocks(keyval_grid)
    gx_count = lax.axis_size("gx")
    gy_count = lax.axis_size("gy")
    row_ids = lax.axis_index("gx") * block_rows - 1 + jnp.arange(block_rows + 2, dtype=jnp.int32)
    col_ids = lax.axis_index("gy") * block_cols - 1 + jnp.arange(block_cols + 2, dtype=jnp.int32)
    row_valid = (row_ids >= 0) & (row_ids < block_rows * gx_count)
    col_valid = (col_ids >= 0) & (col_ids < block_cols * gy_count)
    key_valid = row_valid[:, None] & col_valid[None, :]
    owners = region_owner.reshape(2 * block_count)
    local_ids = region_local.reshape(2 * block_count)
    memory_local = region_memory.reshape(
        region_memory.shape[2], region_memory.shape[3], region_memory.shape[4]
    )
    fetched = fetch_regions(memory_local, owners, local_ids, "gx")
    region_keyval = fetched.reshape(
        block_rows, block_cols, 2, memory_local.shape[1], memory_local.shape[2]
    )
    query_blocks = to_blocks(queries.reshape(tile_rows, tile_cols, model_width))
    outputs, log_totals = attend_forward(query_blocks, keyval_pad, key_valid, region_keyval)
    attended = from_blocks(outputs).reshape(-1, model_width)
    layer_out = jnp.dot(attended, w_out, preferred_element_type=jnp.float32).astype(jnp.bfloat16)
    grad_flat = grad_out.reshape(-1, model_width)
    d_attended = jnp.dot(grad_flat, w_out.T, preferred_element_type=jnp.float32).astype(
        jnp.bfloat16
    )
    grad_out_local = inner_rows(attended, grad_flat)
    dout_blocks = to_blocks(d_attended.reshape(tile_rows, tile_cols, model_width))
    delta_rows = jnp.sum(
        split_heads(dout_blocks).astype(jnp.float32) * split_heads(outputs).astype(jnp.float32), -1
    )
    delta_rows = delta_rows.transpose(0, 1, 3, 2)
    d_queries = query_grads(
        query_blocks, keyval_pad, key_valid, region_keyval, log_totals, dout_blocks, delta_rows
    )
    query_grid = jnp.concatenate(
        [
            queries.reshape(tile_rows, tile_cols, model_width),
            d_attended.reshape(tile_rows, tile_cols, model_width),
        ],
        -1,
    )
    query_halo = padded(query_grid, (("gx", 0), ("gy", 1)), BSIDE)
    stat_grid = from_blocks(jnp.concatenate([log_totals, delta_rows], 2).transpose(0, 1, 3, 2))
    stat_halo = padded(stat_grid, (("gy", 1), ("gx", 0)), BSIDE)
    query_all = to_blocks(query_halo)
    stat_pad = to_blocks(stat_halo).transpose(0, 1, 3, 2)
    d_keys, d_values = key_grads(
        keyval_pad[1:-1, 1:-1],
        query_all[..., :model_width],
        query_all[..., model_width:],
        stat_pad[:, :, :HEADS],
        stat_pad[:, :, HEADS:],
        key_valid,
    )
    dq_flat = from_blocks(d_queries).reshape(-1, model_width)
    dk_flat = from_blocks(d_keys).reshape(-1, model_width)
    dv_flat = from_blocks(d_values).reshape(-1, model_width)
    grads_joined = jnp.concatenate([dq_flat, dk_flat, dv_flat], 1)
    w_stacked = jnp.concatenate([w_query.T, w_key.T, w_value.T], 0)
    grad_patches = jnp.dot(grads_joined, w_stacked, preferred_element_type=jnp.float32).astype(
        jnp.bfloat16
    )
    partials = (
        inner_rows(flat_in, dq_flat),
        inner_rows(flat_in, dk_flat),
        inner_rows(flat_in, dv_flat),
        grad_out_local,
    )
    summed = tree_sum(partials, ("gy", "gx"))
    return (
        layer_out.reshape(tile_rows, tile_cols, model_width),
        grad_patches.reshape(tile_rows, tile_cols, model_width),
        summed[0],
        summed[1],
        summed[2],
        summed[3],
    )


def solution(mesh):
    return jax.shard_map(
        on_device,
        mesh=mesh,
        in_specs=(
            P("gx", "gy", None),
            P(),
            P(),
            P(),
            P(),
            P("gx", "gy", None, None, None),
            P("gx", "gy", None, None),
            P("gx", "gy", None, None),
            P("gx", "gy", None),
        ),
        out_specs=(P("gx", "gy", None), P("gx", "gy", None), P(), P(), P(), P()),
        check_vma=False,
    )
```

```python
import math

import jax
import jax.numpy as jnp
from jax import lax
from jax.sharding import PartitionSpec as P

D = 256
HEADS = 2
HEAD_DIM = 128
BSIDE = 8
BT = 64
CAP = 2


masked_score = -1000000000.0


def padded(block, sides, width):
    for axis, dim in sides:
        count = lax.axis_size(axis)
        forward = [(i, i + 1) for i in range(count - 1)]
        backward = [(target, source) for source, target in forward]
        low = lax.ppermute(
            lax.slice_in_dim(block, block.shape[dim] - width, None, axis=dim), axis, forward
        )
        high = lax.ppermute(lax.slice_in_dim(block, 0, width, axis=dim), axis, backward)
        block = jnp.concatenate([low, block, high], axis=dim)
    return block


def to_blocks(grid_array):
    grid_rows, grid_cols, feature_width = grid_array.shape
    shaped = grid_array.reshape(grid_rows // BSIDE, BSIDE, grid_cols // BSIDE, BSIDE, feature_width)
    return shaped.transpose(0, 2, 1, 3, 4).reshape(
        grid_rows // BSIDE, grid_cols // BSIDE, BSIDE * BSIDE, feature_width
    )


def from_blocks(block_array):
    block_rows, block_cols, block_tokens, feature_width = block_array.shape
    shaped = block_array.reshape(block_rows, block_cols, BSIDE, BSIDE, feature_width)
    return shaped.transpose(0, 2, 1, 3, 4).reshape(
        block_rows * BSIDE, block_cols * BSIDE, feature_width
    )


def split_heads(source):
    return source.reshape(source.shape[:-1] + (HEADS, source.shape[-1] // HEADS))


def neighbour_set(padded_blocks, valid_blocks, block_rows, block_cols, axis):
    parts = []
    valid = []
    for row_off in range(3):
        for col_off in range(3):
            part = padded_blocks[row_off : row_off + block_rows, col_off : col_off + block_cols]
            parts.append(part)
            mask = valid_blocks[row_off : row_off + block_rows, col_off : col_off + block_cols]
            valid.append(jnp.broadcast_to(mask[:, :, None], (block_rows, block_cols, BT)))
    return jnp.concatenate(parts, axis), jnp.concatenate(valid, 2)


def key_set(keyval_pad, key_valid, region_keyval):
    block_rows, block_cols = (region_keyval.shape[0], region_keyval.shape[1])
    keyvals, valid = neighbour_set(keyval_pad, key_valid, block_rows, block_cols, 2)
    merged = region_keyval.reshape(block_rows, block_cols, 2 * BT, 2 * D)
    keyvals = jnp.concatenate([keyvals, merged], 2)
    valid = jnp.concatenate([valid, jnp.ones((block_rows, block_cols, 2 * BT), jnp.bool_)], 2)
    return keyvals[..., :D], keyvals[..., D:], valid


def set_scores(query_heads, key_part, valid):
    scores = jnp.einsum(
        "abqhe,abkhe->abhqk", query_heads, split_heads(key_part), preferred_element_type=jnp.float32
    )
    scores = scores * (1.0 / math.sqrt(HEAD_DIM))
    return jnp.where(valid[:, :, None, None, :], scores, masked_score)


def attend_forward(query_blocks, keyval_pad, key_valid, region_keyval):
    query_heads = split_heads(query_blocks)
    key_part, value_part, valid = key_set(keyval_pad, key_valid, region_keyval)
    scores = set_scores(query_heads, key_part, valid)
    row_top = jnp.max(scores, -1, keepdims=True)
    row_total = jnp.sum(jnp.exp(scores - row_top), -1, keepdims=True)
    log_total = row_top + jnp.log(row_total)
    weights = jnp.exp(scores - log_total).astype(jnp.bfloat16)
    mixed_sum = jnp.einsum(
        "abhqk,abkhe->abqhe", weights, split_heads(value_part), preferred_element_type=jnp.float32
    )
    output = mixed_sum.reshape(query_blocks.shape).astype(jnp.bfloat16)
    return (output, log_total[..., 0])


def query_grads(
    query_blocks, keyval_pad, key_valid, region_keyval, log_total, dout_blocks, delta_rows
):
    query_heads = split_heads(query_blocks)
    dout_heads = split_heads(dout_blocks)
    key_part, value_part, valid = key_set(keyval_pad, key_valid, region_keyval)
    scores = set_scores(query_heads, key_part, valid)
    prob = jnp.exp(scores - log_total[..., None])
    grad_prob = jnp.einsum(
        "abqhe,abkhe->abhqk", dout_heads, split_heads(value_part), preferred_element_type=jnp.float32
    )
    grad_score = (prob * (grad_prob - delta_rows[..., None])).astype(jnp.bfloat16)
    accum_sum = jnp.einsum(
        "abhqk,abkhe->abqhe", grad_score, split_heads(key_part), preferred_element_type=jnp.float32
    )
    return (
        (accum_sum * (1.0 / math.sqrt(HEAD_DIM))).reshape(query_blocks.shape).astype(jnp.bfloat16)
    )


def key_grads(keyval_center, query_pad, dout_pad, log_pad, delta_pad, query_valid):
    block_rows, block_cols = (keyval_center.shape[0], keyval_center.shape[1])
    key_heads = split_heads(keyval_center[..., :D])
    value_heads = split_heads(keyval_center[..., D:])
    queries, valid = neighbour_set(query_pad, query_valid, block_rows, block_cols, 2)
    douts, _ = neighbour_set(dout_pad, query_valid, block_rows, block_cols, 2)
    logs, _ = neighbour_set(log_pad, query_valid, block_rows, block_cols, 3)
    deltas, _ = neighbour_set(delta_pad, query_valid, block_rows, block_cols, 3)
    query_heads = split_heads(queries)
    dout_heads = split_heads(douts)
    scores = jnp.einsum(
        "abqhe,abkhe->abhqk", query_heads, key_heads, preferred_element_type=jnp.float32
    )
    scores = scores * (1.0 / math.sqrt(HEAD_DIM))
    prob = jnp.where(valid[:, :, None, :, None], jnp.exp(scores - logs[..., None]), 0.0)
    grad_prob = jnp.einsum(
        "abqhe,abkhe->abhqk", dout_heads, value_heads, preferred_element_type=jnp.float32
    )
    grad_score = (prob * (grad_prob - deltas[..., None])).astype(jnp.bfloat16)
    grad_key = jnp.einsum(
        "abhqk,abqhe->abkhe", grad_score, query_heads, preferred_element_type=jnp.float32
    )
    grad_value = jnp.einsum(
        "abhqk,abqhe->abkhe", prob.astype(jnp.bfloat16), dout_heads, preferred_element_type=jnp.float32
    )
    out_shape = (block_rows, block_cols, BT, D)
    grad_key = (grad_key * (1.0 / math.sqrt(HEAD_DIM))).reshape(out_shape).astype(jnp.bfloat16)
    return (grad_key, grad_value.reshape(out_shape).astype(jnp.bfloat16))


def inner_rows(left_rows, right_rows):
    return lax.dot_general(
        left_rows, right_rows, (((0,), (0,)), ((), ())), preferred_element_type=jnp.float32
    )


def halving_steps(axes):
    steps = []
    for axis in axes:
        count = lax.axis_size(axis)
        stride = 1
        while stride < count:
            steps.append((axis, stride))
            stride *= 2
    return steps


def doubling_gather(joined, steps):
    for axis, stride in reversed(steps):
        pairs = [(i, i ^ stride) for i in range(lax.axis_size(axis))]
        bit = (lax.axis_index(axis) // stride) % 2
        got = lax.ppermute(joined, axis, pairs)
        low = jnp.where(bit == 0, joined, got)
        high = jnp.where(bit == 0, got, joined)
        joined = jnp.concatenate([low, high], 0)
    return joined


def tree_gather(block, axis):
    count = lax.axis_size(axis)
    if count & (count - 1):
        return lax.all_gather(block, axis, axis=0, tiled=True), lambda index: index
    width = count.bit_length() - 1

    def slot_of(index):
        return sum(((index >> bit) & 1) << (width - 1 - bit) for bit in range(width))

    return doubling_gather(block, halving_steps((axis,))), slot_of


def tree_sum(parts, axes):
    sizes = [lax.axis_size(axis) for axis in axes]
    rows = sum(part.shape[0] for part in parts)
    if any(size & (size - 1) for size in sizes) or rows % math.prod(sizes):
        return lax.psum(parts, axes)
    steps = halving_steps(axes)
    last = [step for step in steps if step[0] == axes[-1]]
    halving = steps[: len(steps) - len(last) + 1]
    doubling = steps[len(halving) :]
    joined = jnp.concatenate(parts, 0)
    for axis, stride in halving:
        pairs = [(i, i ^ stride) for i in range(lax.axis_size(axis))]
        bit = (lax.axis_index(axis) // stride) % 2
        half = joined.shape[0] // 2
        keep = lax.dynamic_slice_in_dim(joined, bit * half, half, 0)
        send = lax.dynamic_slice_in_dim(joined, (1 - bit) * half, half, 0)
        joined = keep + lax.ppermute(send, axis, pairs)
    for axis, stride in doubling:
        pairs = [(i, i ^ stride) for i in range(lax.axis_size(axis))]
        joined = joined + lax.ppermute(joined, axis, pairs)
    joined = doubling_gather(joined, halving)
    out = []
    start = 0
    for part in parts:
        out.append(joined[start : start + part.shape[0]])
        start += part.shape[0]
    return tuple(out)


def fetch_regions(memory_local, owners, local_ids, axis):
    count = lax.axis_size(axis)
    entries = owners.shape[0]
    me = lax.axis_index(axis)
    order = jnp.arange(entries)
    earlier = order[None, :] < order[:, None]
    tables, slot_of = tree_gather(jnp.stack([owners, local_ids])[None], axis)
    tables = tables[jnp.array([slot_of(device) for device in range(count)])]
    mine = tables[:, 0] == me
    rank_here = jnp.sum(mine[:, None, :] & earlier[None], axis=2)
    wanted = mine[:, :, None] & (rank_here[:, :, None] == jnp.arange(CAP)[None, None, :])
    asked = jnp.sum(jnp.where(wanted, tables[:, 1][:, :, None], 0), axis=1)
    sent = jnp.take(memory_local, asked.reshape(-1), axis=0)
    sent = sent.reshape((count, CAP) + memory_local.shape[1:])
    received = lax.all_to_all(sent, axis, 0, 0, tiled=True)
    received = received.reshape((count * CAP,) + memory_local.shape[1:])
    same = owners[:, None] == owners[None, :]
    rank = jnp.sum(same & earlier, axis=1)
    return jnp.take(received, owners * CAP + rank, axis=0)


def on_device(
    patches, w_query, w_key, w_value, w_out, region_memory, region_owner, region_local, grad_out
):
    tile_rows, tile_cols, model_width = patches.shape
    block_rows, block_cols = (tile_rows // BSIDE, tile_cols // BSIDE)
    block_count = block_rows * block_cols
    flat_in = patches.reshape(-1, model_width)
    w_pair = jnp.concatenate([w_key, w_value], 1)
    queries = jnp.dot(flat_in, w_query, preferred_element_type=jnp.float32).astype(jnp.bfloat16)
    keyvals = jnp.dot(flat_in, w_pair, preferred_element_type=jnp.float32).astype(jnp.bfloat16)
    keyvals = keyvals.reshape(tile_rows, tile_cols, 2 * model_width)
    keyval_grid = padded(keyvals, (("gy", 1), ("gx", 0)), BSIDE)
    keyval_pad = to_blocks(keyval_grid)
    gx_count = lax.axis_size("gx")
    gy_count = lax.axis_size("gy")
    row_ids = lax.axis_index("gx") * block_rows - 1 + jnp.arange(block_rows + 2, dtype=jnp.int32)
    col_ids = lax.axis_index("gy") * block_cols - 1 + jnp.arange(block_cols + 2, dtype=jnp.int32)
    row_valid = (row_ids >= 0) & (row_ids < block_rows * gx_count)
    col_valid = (col_ids >= 0) & (col_ids < block_cols * gy_count)
    key_valid = row_valid[:, None] & col_valid[None, :]
    owners = region_owner.reshape(2 * block_count)
    local_ids = region_local.reshape(2 * block_count)
    memory_local = region_memory.reshape(
        region_memory.shape[2], region_memory.shape[3], region_memory.shape[4]
    )
    fetched = fetch_regions(memory_local, owners, local_ids, "gx")
    region_keyval = fetched.reshape(
        block_rows, block_cols, 2, memory_local.shape[1], memory_local.shape[2]
    )
    query_blocks = to_blocks(queries.reshape(tile_rows, tile_cols, model_width))
    outputs, log_totals = attend_forward(query_blocks, keyval_pad, key_valid, region_keyval)
    attended = from_blocks(outputs).reshape(-1, model_width)
    layer_out = jnp.dot(attended, w_out, preferred_element_type=jnp.float32).astype(jnp.bfloat16)
    grad_flat = grad_out.reshape(-1, model_width)
    d_attended = jnp.dot(grad_flat, w_out.T, preferred_element_type=jnp.float32).astype(
        jnp.bfloat16
    )
    grad_out_local = inner_rows(attended, grad_flat)
    dout_blocks = to_blocks(d_attended.reshape(tile_rows, tile_cols, model_width))
    delta_rows = jnp.sum(
        split_heads(dout_blocks).astype(jnp.float32) * split_heads(outputs).astype(jnp.float32), -1
    )
    delta_rows = delta_rows.transpose(0, 1, 3, 2)
    d_queries = query_grads(
        query_blocks, keyval_pad, key_valid, region_keyval, log_totals, dout_blocks, delta_rows
    )
    query_grid = jnp.concatenate(
        [
            queries.reshape(tile_rows, tile_cols, model_width),
            d_attended.reshape(tile_rows, tile_cols, model_width),
        ],
        -1,
    )
    query_halo = padded(query_grid, (("gy", 1), ("gx", 0)), BSIDE)
    stat_grid = from_blocks(jnp.concatenate([log_totals, delta_rows], 2).transpose(0, 1, 3, 2))
    stat_halo = padded(stat_grid, (("gy", 1), ("gx", 0)), BSIDE)
    query_all = to_blocks(query_halo)
    stat_pad = to_blocks(stat_halo).transpose(0, 1, 3, 2)
    d_keys, d_values = key_grads(
        keyval_pad[1:-1, 1:-1],
        query_all[..., :model_width],
        query_all[..., model_width:],
        stat_pad[:, :, :HEADS],
        stat_pad[:, :, HEADS:],
        key_valid,
    )
    dq_flat = from_blocks(d_queries).reshape(-1, model_width)
    dk_flat = from_blocks(d_keys).reshape(-1, model_width)
    dv_flat = from_blocks(d_values).reshape(-1, model_width)
    grads_joined = jnp.concatenate([dq_flat, dk_flat, dv_flat], 1)
    w_stacked = jnp.concatenate([w_query.T, w_key.T, w_value.T], 0)
    grad_patches = jnp.dot(grads_joined, w_stacked, preferred_element_type=jnp.float32).astype(
        jnp.bfloat16
    )
    partials = (
        inner_rows(flat_in, dq_flat),
        inner_rows(flat_in, dk_flat),
        inner_rows(flat_in, dv_flat),
        grad_out_local,
    )
    summed = tree_sum(partials, ("gy", "gx"))
    return (
        layer_out.reshape(tile_rows, tile_cols, model_width),
        grad_patches.reshape(tile_rows, tile_cols, model_width),
        summed[0],
        summed[1],
        summed[2],
        summed[3],
    )


def solution(mesh):
    return jax.shard_map(
        on_device,
        mesh=mesh,
        in_specs=(
            P("gx", "gy", None),
            P(),
            P(),
            P(),
            P(),
            P("gx", "gy", None, None, None),
            P("gx", "gy", None, None),
            P("gx", "gy", None, None),
            P("gx", "gy", None),
        ),
        out_specs=(P("gx", "gy", None), P("gx", "gy", None), P(), P(), P(), P()),
        check_vma=False,
    )
```

```python
import math

import jax
import jax.numpy as jnp
from jax import lax
from jax.sharding import PartitionSpec as P

D = 256
HEADS = 2
HEAD_DIM = 128
BSIDE = 8
BT = 64
CAP = 2


masked_score = -1000000000.0


def padded(block, sides, width):
    for axis, dim in sides:
        count = lax.axis_size(axis)
        forward = [(i, i + 1) for i in range(count - 1)]
        backward = [(target, source) for source, target in forward]
        low = lax.ppermute(
            lax.slice_in_dim(block, block.shape[dim] - width, None, axis=dim), axis, forward
        )
        high = lax.ppermute(lax.slice_in_dim(block, 0, width, axis=dim), axis, backward)
        block = jnp.concatenate([low, block, high], axis=dim)
    return block


def to_blocks(grid_array):
    grid_rows, grid_cols, feature_width = grid_array.shape
    shaped = grid_array.reshape(grid_rows // BSIDE, BSIDE, grid_cols // BSIDE, BSIDE, feature_width)
    return shaped.transpose(0, 2, 1, 3, 4).reshape(
        grid_rows // BSIDE, grid_cols // BSIDE, BSIDE * BSIDE, feature_width
    )


def from_blocks(block_array):
    block_rows, block_cols, block_tokens, feature_width = block_array.shape
    shaped = block_array.reshape(block_rows, block_cols, BSIDE, BSIDE, feature_width)
    return shaped.transpose(0, 2, 1, 3, 4).reshape(
        block_rows * BSIDE, block_cols * BSIDE, feature_width
    )


def split_heads(source):
    return source.reshape(source.shape[:-1] + (HEADS, source.shape[-1] // HEADS))


def neighbour_set(padded_blocks, valid_blocks, block_rows, block_cols, axis):
    parts = []
    valid = []
    for row_off in range(3):
        for col_off in range(3):
            part = padded_blocks[row_off : row_off + block_rows, col_off : col_off + block_cols]
            parts.append(part)
            mask = valid_blocks[row_off : row_off + block_rows, col_off : col_off + block_cols]
            valid.append(jnp.broadcast_to(mask[:, :, None], (block_rows, block_cols, BT)))
    return jnp.concatenate(parts, axis), jnp.concatenate(valid, 2)


def key_set(keyval_pad, key_valid, region_keyval):
    block_rows, block_cols = (region_keyval.shape[0], region_keyval.shape[1])
    keyvals, valid = neighbour_set(keyval_pad, key_valid, block_rows, block_cols, 2)
    merged = region_keyval.reshape(block_rows, block_cols, 2 * BT, 2 * D)
    keyvals = jnp.concatenate([keyvals, merged], 2)
    valid = jnp.concatenate([valid, jnp.ones((block_rows, block_cols, 2 * BT), jnp.bool_)], 2)
    return keyvals[..., :D], keyvals[..., D:], valid


def set_scores(query_heads, key_part, valid):
    scores = jnp.einsum(
        "abqhe,abkhe->abhqk", query_heads, split_heads(key_part), preferred_element_type=jnp.float32
    )
    scores = scores * (1.0 / math.sqrt(HEAD_DIM))
    return jnp.where(valid[:, :, None, None, :], scores, masked_score)


def attend_forward(query_blocks, keyval_pad, key_valid, region_keyval):
    query_heads = split_heads(query_blocks)
    key_part, value_part, valid = key_set(keyval_pad, key_valid, region_keyval)
    scores = set_scores(query_heads, key_part, valid)
    row_top = jnp.max(scores, -1, keepdims=True)
    row_total = jnp.sum(jnp.exp(scores - row_top), -1, keepdims=True)
    log_total = row_top + jnp.log(row_total)
    weights = jnp.exp(scores - log_total).astype(jnp.bfloat16)
    mixed_sum = jnp.einsum(
        "abhqk,abkhe->abqhe", weights, split_heads(value_part), preferred_element_type=jnp.float32
    )
    output = mixed_sum.reshape(query_blocks.shape).astype(jnp.bfloat16)
    return (output, log_total[..., 0])


def query_grads(
    query_blocks, keyval_pad, key_valid, region_keyval, log_total, dout_blocks, delta_rows
):
    query_heads = split_heads(query_blocks)
    dout_heads = split_heads(dout_blocks)
    key_part, value_part, valid = key_set(keyval_pad, key_valid, region_keyval)
    scores = set_scores(query_heads, key_part, valid)
    prob = jnp.exp(scores - log_total[..., None])
    grad_prob = jnp.einsum(
        "abqhe,abkhe->abhqk", dout_heads, split_heads(value_part), preferred_element_type=jnp.float32
    )
    grad_score = (prob * (grad_prob - delta_rows[..., None])).astype(jnp.bfloat16)
    accum_sum = jnp.einsum(
        "abhqk,abkhe->abqhe", grad_score, split_heads(key_part), preferred_element_type=jnp.float32
    )
    return (
        (accum_sum * (1.0 / math.sqrt(HEAD_DIM))).reshape(query_blocks.shape).astype(jnp.bfloat16)
    )


def key_grads(keyval_center, query_pad, dout_pad, log_pad, delta_pad, query_valid):
    block_rows, block_cols = (keyval_center.shape[0], keyval_center.shape[1])
    key_heads = split_heads(keyval_center[..., :D])
    value_heads = split_heads(keyval_center[..., D:])
    queries, valid = neighbour_set(query_pad, query_valid, block_rows, block_cols, 2)
    douts, _ = neighbour_set(dout_pad, query_valid, block_rows, block_cols, 2)
    logs, _ = neighbour_set(log_pad, query_valid, block_rows, block_cols, 3)
    deltas, _ = neighbour_set(delta_pad, query_valid, block_rows, block_cols, 3)
    query_heads = split_heads(queries)
    dout_heads = split_heads(douts)
    scores = jnp.einsum(
        "abqhe,abkhe->abhqk", query_heads, key_heads, preferred_element_type=jnp.float32
    )
    scores = scores * (1.0 / math.sqrt(HEAD_DIM))
    prob = jnp.where(valid[:, :, None, :, None], jnp.exp(scores - logs[..., None]), 0.0)
    grad_prob = jnp.einsum(
        "abqhe,abkhe->abhqk", dout_heads, value_heads, preferred_element_type=jnp.float32
    )
    grad_score = (prob * (grad_prob - deltas[..., None])).astype(jnp.bfloat16)
    grad_key = jnp.einsum(
        "abhqk,abqhe->abkhe", grad_score, query_heads, preferred_element_type=jnp.float32
    )
    grad_value = jnp.einsum(
        "abhqk,abqhe->abkhe", prob.astype(jnp.bfloat16), dout_heads, preferred_element_type=jnp.float32
    )
    out_shape = (block_rows, block_cols, BT, D)
    grad_key = (grad_key * (1.0 / math.sqrt(HEAD_DIM))).reshape(out_shape).astype(jnp.bfloat16)
    return (grad_key, grad_value.reshape(out_shape).astype(jnp.bfloat16))


def inner_rows(left_rows, right_rows):
    return lax.dot_general(
        left_rows, right_rows, (((0,), (0,)), ((), ())), preferred_element_type=jnp.float32
    )


def halving_steps(axes):
    steps = []
    for axis in axes:
        count = lax.axis_size(axis)
        stride = 1
        while stride < count:
            steps.append((axis, stride))
            stride *= 2
    return steps


def doubling_gather(joined, steps):
    for axis, stride in reversed(steps):
        pairs = [(i, i ^ stride) for i in range(lax.axis_size(axis))]
        bit = (lax.axis_index(axis) // stride) % 2
        got = lax.ppermute(joined, axis, pairs)
        low = jnp.where(bit == 0, joined, got)
        high = jnp.where(bit == 0, got, joined)
        joined = jnp.concatenate([low, high], 0)
    return joined


def tree_gather(block, axis):
    count = lax.axis_size(axis)
    if count & (count - 1):
        return lax.all_gather(block, axis, axis=0, tiled=True), lambda index: index
    width = count.bit_length() - 1

    def slot_of(index):
        return sum(((index >> bit) & 1) << (width - 1 - bit) for bit in range(width))

    return doubling_gather(block, halving_steps((axis,))), slot_of


def tree_sum(parts, axes):
    sizes = [lax.axis_size(axis) for axis in axes]
    rows = sum(part.shape[0] for part in parts)
    if any(size & (size - 1) for size in sizes) or rows % math.prod(sizes):
        return lax.psum(parts, axes)
    steps = halving_steps(axes)
    last = [step for step in steps if step[0] == axes[-1]]
    halving = steps[: len(steps) - len(last) + 1]
    doubling = steps[len(halving) :]
    joined = jnp.concatenate(parts, 0)
    for axis, stride in halving:
        pairs = [(i, i ^ stride) for i in range(lax.axis_size(axis))]
        bit = (lax.axis_index(axis) // stride) % 2
        half = joined.shape[0] // 2
        keep = lax.dynamic_slice_in_dim(joined, bit * half, half, 0)
        send = lax.dynamic_slice_in_dim(joined, (1 - bit) * half, half, 0)
        joined = keep + lax.ppermute(send, axis, pairs)
    for axis, stride in doubling:
        pairs = [(i, i ^ stride) for i in range(lax.axis_size(axis))]
        joined = joined + lax.ppermute(joined, axis, pairs)
    joined = doubling_gather(joined, halving)
    out = []
    start = 0
    for part in parts:
        out.append(joined[start : start + part.shape[0]])
        start += part.shape[0]
    return tuple(out)


def fetch_regions(memory_local, owners, local_ids, axis):
    count = lax.axis_size(axis)
    entries = owners.shape[0]
    me = lax.axis_index(axis)
    order = jnp.arange(entries)
    earlier = order[None, :] < order[:, None]
    tables, slot_of = tree_gather(jnp.stack([owners, local_ids])[None], axis)
    tables = tables[jnp.array([slot_of(device) for device in range(count)])]
    mine = tables[:, 0] == me
    rank_here = jnp.sum(mine[:, None, :] & earlier[None], axis=2)
    wanted = mine[:, :, None] & (rank_here[:, :, None] == jnp.arange(CAP)[None, None, :])
    asked = jnp.sum(jnp.where(wanted, tables[:, 1][:, :, None], 0), axis=1)
    sent = jnp.take(memory_local, asked.reshape(-1), axis=0)
    sent = sent.reshape((count, CAP) + memory_local.shape[1:])
    received = lax.all_to_all(sent, axis, 0, 0, tiled=True)
    received = received.reshape((count * CAP,) + memory_local.shape[1:])
    same = owners[:, None] == owners[None, :]
    rank = jnp.sum(same & earlier, axis=1)
    return jnp.take(received, owners * CAP + rank, axis=0)


def on_device(
    patches, w_query, w_key, w_value, w_out, region_memory, region_owner, region_local, grad_out
):
    tile_rows, tile_cols, model_width = patches.shape
    block_rows, block_cols = (tile_rows // BSIDE, tile_cols // BSIDE)
    block_count = block_rows * block_cols
    flat_in = patches.reshape(-1, model_width)
    w_pair = jnp.concatenate([w_key, w_value], 1)
    queries = jnp.dot(flat_in, w_query, preferred_element_type=jnp.float32).astype(jnp.bfloat16)
    keyvals = jnp.dot(flat_in, w_pair, preferred_element_type=jnp.float32).astype(jnp.bfloat16)
    keyvals = keyvals.reshape(tile_rows, tile_cols, 2 * model_width)
    keyval_grid = padded(keyvals, (("gx", 0), ("gy", 1)), BSIDE)
    keyval_pad = to_blocks(keyval_grid)
    gx_count = lax.axis_size("gx")
    gy_count = lax.axis_size("gy")
    row_ids = lax.axis_index("gx") * block_rows - 1 + jnp.arange(block_rows + 2, dtype=jnp.int32)
    col_ids = lax.axis_index("gy") * block_cols - 1 + jnp.arange(block_cols + 2, dtype=jnp.int32)
    row_valid = (row_ids >= 0) & (row_ids < block_rows * gx_count)
    col_valid = (col_ids >= 0) & (col_ids < block_cols * gy_count)
    key_valid = row_valid[:, None] & col_valid[None, :]
    owners = region_owner.reshape(2 * block_count)
    local_ids = region_local.reshape(2 * block_count)
    memory_local = region_memory.reshape(
        region_memory.shape[2], region_memory.shape[3], region_memory.shape[4]
    )
    fetched = fetch_regions(memory_local, owners, local_ids, "gx")
    region_keyval = fetched.reshape(
        block_rows, block_cols, 2, memory_local.shape[1], memory_local.shape[2]
    )
    query_blocks = to_blocks(queries.reshape(tile_rows, tile_cols, model_width))
    outputs, log_totals = attend_forward(query_blocks, keyval_pad, key_valid, region_keyval)
    attended = from_blocks(outputs).reshape(-1, model_width)
    layer_out = jnp.dot(attended, w_out, preferred_element_type=jnp.float32).astype(jnp.bfloat16)
    grad_flat = grad_out.reshape(-1, model_width)
    d_attended = jnp.dot(grad_flat, w_out.T, preferred_element_type=jnp.float32).astype(
        jnp.bfloat16
    )
    grad_out_local = inner_rows(attended, grad_flat)
    dout_blocks = to_blocks(d_attended.reshape(tile_rows, tile_cols, model_width))
    delta_rows = jnp.sum(
        split_heads(dout_blocks).astype(jnp.float32) * split_heads(outputs).astype(jnp.float32), -1
    )
    delta_rows = delta_rows.transpose(0, 1, 3, 2)
    d_queries = query_grads(
        query_blocks, keyval_pad, key_valid, region_keyval, log_totals, dout_blocks, delta_rows
    )
    query_grid = jnp.concatenate(
        [
            queries.reshape(tile_rows, tile_cols, model_width),
            d_attended.reshape(tile_rows, tile_cols, model_width),
        ],
        -1,
    )
    query_halo = padded(query_grid, (("gy", 1), ("gx", 0)), BSIDE)
    stat_grid = from_blocks(jnp.concatenate([log_totals, delta_rows], 2).transpose(0, 1, 3, 2))
    stat_halo = padded(stat_grid, (("gy", 1), ("gx", 0)), BSIDE)
    query_all = to_blocks(query_halo)
    stat_pad = to_blocks(stat_halo).transpose(0, 1, 3, 2)
    d_keys, d_values = key_grads(
        keyval_pad[1:-1, 1:-1],
        query_all[..., :model_width],
        query_all[..., model_width:],
        stat_pad[:, :, :HEADS],
        stat_pad[:, :, HEADS:],
        key_valid,
    )
    dq_flat = from_blocks(d_queries).reshape(-1, model_width)
    dk_flat = from_blocks(d_keys).reshape(-1, model_width)
    dv_flat = from_blocks(d_values).reshape(-1, model_width)
    grads_joined = jnp.concatenate([dq_flat, dk_flat, dv_flat], 1)
    w_stacked = jnp.concatenate([w_query.T, w_key.T, w_value.T], 0)
    grad_patches = jnp.dot(grads_joined, w_stacked, preferred_element_type=jnp.float32).astype(
        jnp.bfloat16
    )
    partials = (
        inner_rows(flat_in, dq_flat),
        inner_rows(flat_in, dk_flat),
        inner_rows(flat_in, dv_flat),
        grad_out_local,
    )
    summed = tree_sum(partials, ("gy", "gx"))
    return (
        layer_out.reshape(tile_rows, tile_cols, model_width),
        grad_patches.reshape(tile_rows, tile_cols, model_width),
        summed[0],
        summed[1],
        summed[2],
        summed[3],
    )


def solution(mesh):
    return jax.shard_map(
        on_device,
        mesh=mesh,
        in_specs=(
            P("gx", "gy", None),
            P(),
            P(),
            P(),
            P(),
            P("gx", "gy", None, None, None),
            P("gx", "gy", None, None),
            P("gx", "gy", None, None),
            P("gx", "gy", None),
        ),
        out_specs=(P("gx", "gy", None), P("gx", "gy", None), P(), P(), P(), P()),
        check_vma=False,
    )
```

```python
import math

import jax
import jax.numpy as jnp
from jax import lax
from jax.sharding import PartitionSpec as P

D = 256
HEADS = 2
HEAD_DIM = 128
BSIDE = 8
BT = 64
CAP = 2


masked_score = -1000000000.0


def padded(block, sides, width):
    for axis, dim in sides:
        count = lax.axis_size(axis)
        forward = [(i, i + 1) for i in range(count - 1)]
        backward = [(target, source) for source, target in forward]
        low = lax.ppermute(
            lax.slice_in_dim(block, block.shape[dim] - width, None, axis=dim), axis, forward
        )
        high = lax.ppermute(lax.slice_in_dim(block, 0, width, axis=dim), axis, backward)
        block = jnp.concatenate([low, block, high], axis=dim)
    return block


def to_blocks(grid_array):
    grid_rows, grid_cols, feature_width = grid_array.shape
    shaped = grid_array.reshape(grid_rows // BSIDE, BSIDE, grid_cols // BSIDE, BSIDE, feature_width)
    return shaped.transpose(0, 2, 1, 3, 4).reshape(
        grid_rows // BSIDE, grid_cols // BSIDE, BSIDE * BSIDE, feature_width
    )


def from_blocks(block_array):
    block_rows, block_cols, block_tokens, feature_width = block_array.shape
    shaped = block_array.reshape(block_rows, block_cols, BSIDE, BSIDE, feature_width)
    return shaped.transpose(0, 2, 1, 3, 4).reshape(
        block_rows * BSIDE, block_cols * BSIDE, feature_width
    )


def split_heads(source):
    return source.reshape(source.shape[:-1] + (HEADS, source.shape[-1] // HEADS))


def neighbour_set(padded_blocks, valid_blocks, block_rows, block_cols, axis):
    parts = []
    valid = []
    for row_off in range(3):
        for col_off in range(3):
            part = padded_blocks[row_off : row_off + block_rows, col_off : col_off + block_cols]
            parts.append(part)
            mask = valid_blocks[row_off : row_off + block_rows, col_off : col_off + block_cols]
            valid.append(jnp.broadcast_to(mask[:, :, None], (block_rows, block_cols, BT)))
    return jnp.concatenate(parts, axis), jnp.concatenate(valid, 2)


def key_set(keyval_pad, key_valid, region_keyval):
    block_rows, block_cols = (region_keyval.shape[0], region_keyval.shape[1])
    keyvals, valid = neighbour_set(keyval_pad, key_valid, block_rows, block_cols, 2)
    merged = region_keyval.reshape(block_rows, block_cols, 2 * BT, 2 * D)
    keyvals = jnp.concatenate([keyvals, merged], 2)
    valid = jnp.concatenate([valid, jnp.ones((block_rows, block_cols, 2 * BT), jnp.bool_)], 2)
    return keyvals[..., :D], keyvals[..., D:], valid


def set_scores(query_heads, key_part, valid):
    scores = jnp.einsum(
        "abqhe,abkhe->abhqk", query_heads, split_heads(key_part), preferred_element_type=jnp.float32
    )
    scores = scores * (1.0 / math.sqrt(HEAD_DIM))
    return jnp.where(valid[:, :, None, None, :], scores, masked_score)


def attend_forward(query_blocks, keyval_pad, key_valid, region_keyval):
    query_heads = split_heads(query_blocks)
    key_part, value_part, valid = key_set(keyval_pad, key_valid, region_keyval)
    scores = set_scores(query_heads, key_part, valid)
    row_top = jnp.max(scores, -1, keepdims=True)
    row_total = jnp.sum(jnp.exp(scores - row_top), -1, keepdims=True)
    log_total = row_top + jnp.log(row_total)
    weights = jnp.exp(scores - log_total).astype(jnp.bfloat16)
    mixed_sum = jnp.einsum(
        "abhqk,abkhe->abqhe", weights, split_heads(value_part), preferred_element_type=jnp.float32
    )
    output = mixed_sum.reshape(query_blocks.shape).astype(jnp.bfloat16)
    return (output, log_total[..., 0])


def query_grads(
    query_blocks, keyval_pad, key_valid, region_keyval, log_total, dout_blocks, delta_rows
):
    query_heads = split_heads(query_blocks)
    dout_heads = split_heads(dout_blocks)
    key_part, value_part, valid = key_set(keyval_pad, key_valid, region_keyval)
    scores = set_scores(query_heads, key_part, valid)
    prob = jnp.exp(scores - log_total[..., None])
    grad_prob = jnp.einsum(
        "abqhe,abkhe->abhqk", dout_heads, split_heads(value_part), preferred_element_type=jnp.float32
    )
    grad_score = (prob * (grad_prob - delta_rows[..., None])).astype(jnp.bfloat16)
    accum_sum = jnp.einsum(
        "abhqk,abkhe->abqhe", grad_score, split_heads(key_part), preferred_element_type=jnp.float32
    )
    return (
        (accum_sum * (1.0 / math.sqrt(HEAD_DIM))).reshape(query_blocks.shape).astype(jnp.bfloat16)
    )


def key_grads(keyval_center, query_pad, dout_pad, log_pad, delta_pad, query_valid):
    block_rows, block_cols = (keyval_center.shape[0], keyval_center.shape[1])
    key_heads = split_heads(keyval_center[..., :D])
    value_heads = split_heads(keyval_center[..., D:])
    queries, valid = neighbour_set(query_pad, query_valid, block_rows, block_cols, 2)
    douts, _ = neighbour_set(dout_pad, query_valid, block_rows, block_cols, 2)
    logs, _ = neighbour_set(log_pad, query_valid, block_rows, block_cols, 3)
    deltas, _ = neighbour_set(delta_pad, query_valid, block_rows, block_cols, 3)
    query_heads = split_heads(queries)
    dout_heads = split_heads(douts)
    scores = jnp.einsum(
        "abqhe,abkhe->abhqk", query_heads, key_heads, preferred_element_type=jnp.float32
    )
    scores = scores * (1.0 / math.sqrt(HEAD_DIM))
    prob = jnp.where(valid[:, :, None, :, None], jnp.exp(scores - logs[..., None]), 0.0)
    grad_prob = jnp.einsum(
        "abqhe,abkhe->abhqk", dout_heads, value_heads, preferred_element_type=jnp.float32
    )
    grad_score = (prob * (grad_prob - deltas[..., None])).astype(jnp.bfloat16)
    grad_key = jnp.einsum(
        "abhqk,abqhe->abkhe", grad_score, query_heads, preferred_element_type=jnp.float32
    )
    grad_value = jnp.einsum(
        "abhqk,abqhe->abkhe", prob.astype(jnp.bfloat16), dout_heads, preferred_element_type=jnp.float32
    )
    out_shape = (block_rows, block_cols, BT, D)
    grad_key = (grad_key * (1.0 / math.sqrt(HEAD_DIM))).reshape(out_shape).astype(jnp.bfloat16)
    return (grad_key, grad_value.reshape(out_shape).astype(jnp.bfloat16))


def inner_rows(left_rows, right_rows):
    return lax.dot_general(
        left_rows, right_rows, (((0,), (0,)), ((), ())), preferred_element_type=jnp.float32
    )


def halving_steps(axes):
    steps = []
    for axis in axes:
        count = lax.axis_size(axis)
        stride = 1
        while stride < count:
            steps.append((axis, stride))
            stride *= 2
    return steps


def doubling_gather(joined, steps):
    for axis, stride in reversed(steps):
        pairs = [(i, i ^ stride) for i in range(lax.axis_size(axis))]
        bit = (lax.axis_index(axis) // stride) % 2
        got = lax.ppermute(joined, axis, pairs)
        low = jnp.where(bit == 0, joined, got)
        high = jnp.where(bit == 0, got, joined)
        joined = jnp.concatenate([low, high], 0)
    return joined


def tree_gather(block, axis):
    count = lax.axis_size(axis)
    if count & (count - 1):
        return lax.all_gather(block, axis, axis=0, tiled=True), lambda index: index
    width = count.bit_length() - 1

    def slot_of(index):
        return sum(((index >> bit) & 1) << (width - 1 - bit) for bit in range(width))

    return doubling_gather(block, halving_steps((axis,))), slot_of


def tree_sum(parts, axes):
    sizes = [lax.axis_size(axis) for axis in axes]
    rows = sum(part.shape[0] for part in parts)
    if any(size & (size - 1) for size in sizes) or rows % math.prod(sizes):
        return lax.psum(parts, axes)
    steps = halving_steps(axes)
    last = [step for step in steps if step[0] == axes[-1]]
    halving = steps[: len(steps) - len(last) + 1]
    doubling = steps[len(halving) :]
    joined = jnp.concatenate(parts, 0)
    for axis, stride in halving:
        pairs = [(i, i ^ stride) for i in range(lax.axis_size(axis))]
        bit = (lax.axis_index(axis) // stride) % 2
        half = joined.shape[0] // 2
        keep = lax.dynamic_slice_in_dim(joined, bit * half, half, 0)
        send = lax.dynamic_slice_in_dim(joined, (1 - bit) * half, half, 0)
        joined = keep + lax.ppermute(send, axis, pairs)
    for axis, stride in doubling:
        pairs = [(i, i ^ stride) for i in range(lax.axis_size(axis))]
        joined = joined + lax.ppermute(joined, axis, pairs)
    joined = doubling_gather(joined, halving)
    out = []
    start = 0
    for part in parts:
        out.append(joined[start : start + part.shape[0]])
        start += part.shape[0]
    return tuple(out)


def fetch_regions(memory_local, owners, local_ids, axis):
    count = lax.axis_size(axis)
    entries = owners.shape[0]
    me = lax.axis_index(axis)
    order = jnp.arange(entries)
    earlier = order[None, :] < order[:, None]
    tables, slot_of = tree_gather(jnp.stack([owners, local_ids])[None], axis)
    tables = tables[jnp.array([slot_of(device) for device in range(count)])]
    mine = tables[:, 0] == me
    rank_here = jnp.sum(mine[:, None, :] & earlier[None], axis=2)
    wanted = mine[:, :, None] & (rank_here[:, :, None] == jnp.arange(CAP)[None, None, :])
    asked = jnp.sum(jnp.where(wanted, tables[:, 1][:, :, None], 0), axis=1)
    sent = jnp.take(memory_local, asked.reshape(-1), axis=0)
    sent = sent.reshape((count, CAP) + memory_local.shape[1:])
    received = lax.all_to_all(sent, axis, 0, 0, tiled=True)
    received = received.reshape((count * CAP,) + memory_local.shape[1:])
    same = owners[:, None] == owners[None, :]
    rank = jnp.sum(same & earlier, axis=1)
    return jnp.take(received, owners * CAP + rank, axis=0)


def on_device(
    patches, w_query, w_key, w_value, w_out, region_memory, region_owner, region_local, grad_out
):
    tile_rows, tile_cols, model_width = patches.shape
    block_rows, block_cols = (tile_rows // BSIDE, tile_cols // BSIDE)
    block_count = block_rows * block_cols
    flat_in = patches.reshape(-1, model_width)
    w_pair = jnp.concatenate([w_key, w_value], 1)
    queries = jnp.dot(flat_in, w_query, preferred_element_type=jnp.float32).astype(jnp.bfloat16)
    keyvals = jnp.dot(flat_in, w_pair, preferred_element_type=jnp.float32).astype(jnp.bfloat16)
    keyvals = keyvals.reshape(tile_rows, tile_cols, 2 * model_width)
    keyval_grid = padded(keyvals, (("gy", 1), ("gx", 0)), BSIDE)
    keyval_pad = to_blocks(keyval_grid)
    gx_count = lax.axis_size("gx")
    gy_count = lax.axis_size("gy")
    row_ids = lax.axis_index("gx") * block_rows - 1 + jnp.arange(block_rows + 2, dtype=jnp.int32)
    col_ids = lax.axis_index("gy") * block_cols - 1 + jnp.arange(block_cols + 2, dtype=jnp.int32)
    row_valid = (row_ids >= 0) & (row_ids < block_rows * gx_count)
    col_valid = (col_ids >= 0) & (col_ids < block_cols * gy_count)
    key_valid = row_valid[:, None] & col_valid[None, :]
    owners = region_owner.reshape(2 * block_count)
    local_ids = region_local.reshape(2 * block_count)
    memory_local = region_memory.reshape(
        region_memory.shape[2], region_memory.shape[3], region_memory.shape[4]
    )
    fetched = fetch_regions(memory_local, owners, local_ids, "gx")
    region_keyval = fetched.reshape(
        block_rows, block_cols, 2, memory_local.shape[1], memory_local.shape[2]
    )
    query_blocks = to_blocks(queries.reshape(tile_rows, tile_cols, model_width))
    outputs, log_totals = attend_forward(query_blocks, keyval_pad, key_valid, region_keyval)
    attended = from_blocks(outputs).reshape(-1, model_width)
    layer_out = jnp.dot(attended, w_out, preferred_element_type=jnp.float32).astype(jnp.bfloat16)
    grad_flat = grad_out.reshape(-1, model_width)
    d_attended = jnp.dot(grad_flat, w_out.T, preferred_element_type=jnp.float32).astype(
        jnp.bfloat16
    )
    grad_out_local = inner_rows(attended, grad_flat)
    dout_blocks = to_blocks(d_attended.reshape(tile_rows, tile_cols, model_width))
    delta_rows = jnp.sum(
        split_heads(dout_blocks).astype(jnp.float32) * split_heads(outputs).astype(jnp.float32), -1
    )
    delta_rows = delta_rows.transpose(0, 1, 3, 2)
    d_queries = query_grads(
        query_blocks, keyval_pad, key_valid, region_keyval, log_totals, dout_blocks, delta_rows
    )
    query_grid = jnp.concatenate(
        [
            queries.reshape(tile_rows, tile_cols, model_width),
            d_attended.reshape(tile_rows, tile_cols, model_width),
        ],
        -1,
    )
    query_halo = padded(query_grid, (("gx", 0), ("gy", 1)), BSIDE)
    stat_grid = from_blocks(jnp.concatenate([log_totals, delta_rows], 2).transpose(0, 1, 3, 2))
    stat_halo = padded(stat_grid, (("gy", 1), ("gx", 0)), BSIDE)
    query_all = to_blocks(query_halo)
    stat_pad = to_blocks(stat_halo).transpose(0, 1, 3, 2)
    d_keys, d_values = key_grads(
        keyval_pad[1:-1, 1:-1],
        query_all[..., :model_width],
        query_all[..., model_width:],
        stat_pad[:, :, :HEADS],
        stat_pad[:, :, HEADS:],
        key_valid,
    )
    dq_flat = from_blocks(d_queries).reshape(-1, model_width)
    dk_flat = from_blocks(d_keys).reshape(-1, model_width)
    dv_flat = from_blocks(d_values).reshape(-1, model_width)
    grads_joined = jnp.concatenate([dq_flat, dk_flat, dv_flat], 1)
    w_stacked = jnp.concatenate([w_query.T, w_key.T, w_value.T], 0)
    grad_patches = jnp.dot(grads_joined, w_stacked, preferred_element_type=jnp.float32).astype(
        jnp.bfloat16
    )
    partials = (
        inner_rows(flat_in, dq_flat),
        inner_rows(flat_in, dk_flat),
        inner_rows(flat_in, dv_flat),
        grad_out_local,
    )
    summed = tree_sum(partials, ("gy", "gx"))
    return (
        layer_out.reshape(tile_rows, tile_cols, model_width),
        grad_patches.reshape(tile_rows, tile_cols, model_width),
        summed[0],
        summed[1],
        summed[2],
        summed[3],
    )


def solution(mesh):
    return jax.shard_map(
        on_device,
        mesh=mesh,
        in_specs=(
            P("gx", "gy", None),
            P(),
            P(),
            P(),
            P(),
            P("gx", "gy", None, None, None),
            P("gx", "gy", None, None),
            P("gx", "gy", None, None),
            P("gx", "gy", None),
        ),
        out_specs=(P("gx", "gy", None), P("gx", "gy", None), P(), P(), P(), P()),
        check_vma=False,
    )
```

```python
import math

import jax
import jax.numpy as jnp
from jax import lax
from jax.sharding import PartitionSpec as P

D = 256
HEADS = 2
HEAD_DIM = 128
BSIDE = 8
BT = 64
CAP = 2


masked_score = -1000000000.0


def padded(block, sides, width):
    for axis, dim in sides:
        count = lax.axis_size(axis)
        forward = [(i, i + 1) for i in range(count - 1)]
        backward = [(target, source) for source, target in forward]
        low = lax.ppermute(
            lax.slice_in_dim(block, block.shape[dim] - width, None, axis=dim), axis, forward
        )
        high = lax.ppermute(lax.slice_in_dim(block, 0, width, axis=dim), axis, backward)
        block = jnp.concatenate([low, block, high], axis=dim)
    return block


def to_blocks(grid_array):
    grid_rows, grid_cols, feature_width = grid_array.shape
    shaped = grid_array.reshape(grid_rows // BSIDE, BSIDE, grid_cols // BSIDE, BSIDE, feature_width)
    return shaped.transpose(0, 2, 1, 3, 4).reshape(
        grid_rows // BSIDE, grid_cols // BSIDE, BSIDE * BSIDE, feature_width
    )


def from_blocks(block_array):
    block_rows, block_cols, block_tokens, feature_width = block_array.shape
    shaped = block_array.reshape(block_rows, block_cols, BSIDE, BSIDE, feature_width)
    return shaped.transpose(0, 2, 1, 3, 4).reshape(
        block_rows * BSIDE, block_cols * BSIDE, feature_width
    )


def split_heads(source):
    return source.reshape(source.shape[:-1] + (HEADS, source.shape[-1] // HEADS))


def neighbour_set(padded_blocks, valid_blocks, block_rows, block_cols, axis):
    parts = []
    valid = []
    for row_off in range(3):
        for col_off in range(3):
            part = padded_blocks[row_off : row_off + block_rows, col_off : col_off + block_cols]
            parts.append(part)
            mask = valid_blocks[row_off : row_off + block_rows, col_off : col_off + block_cols]
            valid.append(jnp.broadcast_to(mask[:, :, None], (block_rows, block_cols, BT)))
    return jnp.concatenate(parts, axis), jnp.concatenate(valid, 2)


def key_set(keyval_pad, key_valid, region_keyval):
    block_rows, block_cols = (region_keyval.shape[0], region_keyval.shape[1])
    keyvals, valid = neighbour_set(keyval_pad, key_valid, block_rows, block_cols, 2)
    merged = region_keyval.reshape(block_rows, block_cols, 2 * BT, 2 * D)
    keyvals = jnp.concatenate([keyvals, merged], 2)
    valid = jnp.concatenate([valid, jnp.ones((block_rows, block_cols, 2 * BT), jnp.bool_)], 2)
    return keyvals[..., :D], keyvals[..., D:], valid


def set_scores(query_heads, key_part, valid):
    scores = jnp.einsum(
        "abqhe,abkhe->abhqk", query_heads, split_heads(key_part), preferred_element_type=jnp.float32
    )
    scores = scores * (1.0 / math.sqrt(HEAD_DIM))
    return jnp.where(valid[:, :, None, None, :], scores, masked_score)


def attend_forward(query_blocks, keyval_pad, key_valid, region_keyval):
    query_heads = split_heads(query_blocks)
    key_part, value_part, valid = key_set(keyval_pad, key_valid, region_keyval)
    scores = set_scores(query_heads, key_part, valid)
    row_top = jnp.max(scores, -1, keepdims=True)
    row_total = jnp.sum(jnp.exp(scores - row_top), -1, keepdims=True)
    log_total = row_top + jnp.log(row_total)
    weights = jnp.exp(scores - log_total).astype(jnp.bfloat16)
    mixed_sum = jnp.einsum(
        "abhqk,abkhe->abqhe", weights, split_heads(value_part), preferred_element_type=jnp.float32
    )
    output = mixed_sum.reshape(query_blocks.shape).astype(jnp.bfloat16)
    return (output, log_total[..., 0])


def query_grads(
    query_blocks, keyval_pad, key_valid, region_keyval, log_total, dout_blocks, delta_rows
):
    query_heads = split_heads(query_blocks)
    dout_heads = split_heads(dout_blocks)
    key_part, value_part, valid = key_set(keyval_pad, key_valid, region_keyval)
    scores = set_scores(query_heads, key_part, valid)
    prob = jnp.exp(scores - log_total[..., None])
    grad_prob = jnp.einsum(
        "abqhe,abkhe->abhqk", dout_heads, split_heads(value_part), preferred_element_type=jnp.float32
    )
    grad_score = (prob * (grad_prob - delta_rows[..., None])).astype(jnp.bfloat16)
    accum_sum = jnp.einsum(
        "abhqk,abkhe->abqhe", grad_score, split_heads(key_part), preferred_element_type=jnp.float32
    )
    return (
        (accum_sum * (1.0 / math.sqrt(HEAD_DIM))).reshape(query_blocks.shape).astype(jnp.bfloat16)
    )


def key_grads(keyval_center, query_pad, dout_pad, log_pad, delta_pad, query_valid):
    block_rows, block_cols = (keyval_center.shape[0], keyval_center.shape[1])
    key_heads = split_heads(keyval_center[..., :D])
    value_heads = split_heads(keyval_center[..., D:])
    queries, valid = neighbour_set(query_pad, query_valid, block_rows, block_cols, 2)
    douts, _ = neighbour_set(dout_pad, query_valid, block_rows, block_cols, 2)
    logs, _ = neighbour_set(log_pad, query_valid, block_rows, block_cols, 3)
    deltas, _ = neighbour_set(delta_pad, query_valid, block_rows, block_cols, 3)
    query_heads = split_heads(queries)
    dout_heads = split_heads(douts)
    scores = jnp.einsum(
        "abqhe,abkhe->abhqk", query_heads, key_heads, preferred_element_type=jnp.float32
    )
    scores = scores * (1.0 / math.sqrt(HEAD_DIM))
    prob = jnp.where(valid[:, :, None, :, None], jnp.exp(scores - logs[..., None]), 0.0)
    grad_prob = jnp.einsum(
        "abqhe,abkhe->abhqk", dout_heads, value_heads, preferred_element_type=jnp.float32
    )
    grad_score = (prob * (grad_prob - deltas[..., None])).astype(jnp.bfloat16)
    grad_key = jnp.einsum(
        "abhqk,abqhe->abkhe", grad_score, query_heads, preferred_element_type=jnp.float32
    )
    grad_value = jnp.einsum(
        "abhqk,abqhe->abkhe", prob.astype(jnp.bfloat16), dout_heads, preferred_element_type=jnp.float32
    )
    out_shape = (block_rows, block_cols, BT, D)
    grad_key = (grad_key * (1.0 / math.sqrt(HEAD_DIM))).reshape(out_shape).astype(jnp.bfloat16)
    return (grad_key, grad_value.reshape(out_shape).astype(jnp.bfloat16))


def inner_rows(left_rows, right_rows):
    return lax.dot_general(
        left_rows, right_rows, (((0,), (0,)), ((), ())), preferred_element_type=jnp.float32
    )


def halving_steps(axes):
    steps = []
    for axis in axes:
        count = lax.axis_size(axis)
        stride = 1
        while stride < count:
            steps.append((axis, stride))
            stride *= 2
    return steps


def doubling_gather(joined, steps):
    for axis, stride in reversed(steps):
        pairs = [(i, i ^ stride) for i in range(lax.axis_size(axis))]
        bit = (lax.axis_index(axis) // stride) % 2
        got = lax.ppermute(joined, axis, pairs)
        low = jnp.where(bit == 0, joined, got)
        high = jnp.where(bit == 0, got, joined)
        joined = jnp.concatenate([low, high], 0)
    return joined


def tree_gather(block, axis):
    count = lax.axis_size(axis)
    if count & (count - 1):
        return lax.all_gather(block, axis, axis=0, tiled=True), lambda index: index
    return doubling_gather(block, halving_steps((axis,))[::-1]), lambda index: index


def tree_sum(parts, axes):
    sizes = [lax.axis_size(axis) for axis in axes]
    rows = sum(part.shape[0] for part in parts)
    if any(size & (size - 1) for size in sizes) or rows % math.prod(sizes):
        return lax.psum(parts, axes)
    steps = halving_steps(axes)
    last = [step for step in steps if step[0] == axes[-1]]
    halving = steps[: len(steps) - len(last) + 1]
    doubling = steps[len(halving) :]
    joined = jnp.concatenate(parts, 0)
    for axis, stride in halving:
        pairs = [(i, i ^ stride) for i in range(lax.axis_size(axis))]
        bit = (lax.axis_index(axis) // stride) % 2
        half = joined.shape[0] // 2
        keep = lax.dynamic_slice_in_dim(joined, bit * half, half, 0)
        send = lax.dynamic_slice_in_dim(joined, (1 - bit) * half, half, 0)
        joined = keep + lax.ppermute(send, axis, pairs)
    for axis, stride in doubling:
        pairs = [(i, i ^ stride) for i in range(lax.axis_size(axis))]
        joined = joined + lax.ppermute(joined, axis, pairs)
    joined = doubling_gather(joined, halving)
    out = []
    start = 0
    for part in parts:
        out.append(joined[start : start + part.shape[0]])
        start += part.shape[0]
    return tuple(out)


def fetch_regions(memory_local, owners, local_ids, axis):
    count = lax.axis_size(axis)
    entries = owners.shape[0]
    me = lax.axis_index(axis)
    order = jnp.arange(entries)
    earlier = order[None, :] < order[:, None]
    tables, slot_of = tree_gather(jnp.stack([owners, local_ids])[None], axis)
    tables = tables[jnp.array([slot_of(device) for device in range(count)])]
    mine = tables[:, 0] == me
    rank_here = jnp.sum(mine[:, None, :] & earlier[None], axis=2)
    wanted = mine[:, :, None] & (rank_here[:, :, None] == jnp.arange(CAP)[None, None, :])
    asked = jnp.sum(jnp.where(wanted, tables[:, 1][:, :, None], 0), axis=1)
    sent = jnp.take(memory_local, asked.reshape(-1), axis=0)
    sent = sent.reshape((count, CAP) + memory_local.shape[1:])
    received = lax.all_to_all(sent, axis, 0, 0, tiled=True)
    received = received.reshape((count * CAP,) + memory_local.shape[1:])
    same = owners[:, None] == owners[None, :]
    rank = jnp.sum(same & earlier, axis=1)
    return jnp.take(received, owners * CAP + rank, axis=0)


def on_device(
    patches, w_query, w_key, w_value, w_out, region_memory, region_owner, region_local, grad_out
):
    tile_rows, tile_cols, model_width = patches.shape
    block_rows, block_cols = (tile_rows // BSIDE, tile_cols // BSIDE)
    block_count = block_rows * block_cols
    flat_in = patches.reshape(-1, model_width)
    w_pair = jnp.concatenate([w_key, w_value], 1)
    queries = jnp.dot(flat_in, w_query, preferred_element_type=jnp.float32).astype(jnp.bfloat16)
    keyvals = jnp.dot(flat_in, w_pair, preferred_element_type=jnp.float32).astype(jnp.bfloat16)
    keyvals = keyvals.reshape(tile_rows, tile_cols, 2 * model_width)
    keyval_grid = padded(keyvals, (("gx", 0), ("gy", 1)), BSIDE)
    keyval_pad = to_blocks(keyval_grid)
    gx_count = lax.axis_size("gx")
    gy_count = lax.axis_size("gy")
    row_ids = lax.axis_index("gx") * block_rows - 1 + jnp.arange(block_rows + 2, dtype=jnp.int32)
    col_ids = lax.axis_index("gy") * block_cols - 1 + jnp.arange(block_cols + 2, dtype=jnp.int32)
    row_valid = (row_ids >= 0) & (row_ids < block_rows * gx_count)
    col_valid = (col_ids >= 0) & (col_ids < block_cols * gy_count)
    key_valid = row_valid[:, None] & col_valid[None, :]
    owners = region_owner.reshape(2 * block_count)
    local_ids = region_local.reshape(2 * block_count)
    memory_local = region_memory.reshape(
        region_memory.shape[2], region_memory.shape[3], region_memory.shape[4]
    )
    fetched = fetch_regions(memory_local, owners, local_ids, "gx")
    region_keyval = fetched.reshape(
        block_rows, block_cols, 2, memory_local.shape[1], memory_local.shape[2]
    )
    query_blocks = to_blocks(queries.reshape(tile_rows, tile_cols, model_width))
    outputs, log_totals = attend_forward(query_blocks, keyval_pad, key_valid, region_keyval)
    attended = from_blocks(outputs).reshape(-1, model_width)
    layer_out = jnp.dot(attended, w_out, preferred_element_type=jnp.float32).astype(jnp.bfloat16)
    grad_flat = grad_out.reshape(-1, model_width)
    d_attended = jnp.dot(grad_flat, w_out.T, preferred_element_type=jnp.float32).astype(
        jnp.bfloat16
    )
    grad_out_local = inner_rows(attended, grad_flat)
    dout_blocks = to_blocks(d_attended.reshape(tile_rows, tile_cols, model_width))
    delta_rows = jnp.sum(
        split_heads(dout_blocks).astype(jnp.float32) * split_heads(outputs).astype(jnp.float32), -1
    )
    delta_rows = delta_rows.transpose(0, 1, 3, 2)
    d_queries = query_grads(
        query_blocks, keyval_pad, key_valid, region_keyval, log_totals, dout_blocks, delta_rows
    )
    query_grid = jnp.concatenate(
        [
            queries.reshape(tile_rows, tile_cols, model_width),
            d_attended.reshape(tile_rows, tile_cols, model_width),
        ],
        -1,
    )
    query_halo = padded(query_grid, (("gx", 0), ("gy", 1)), BSIDE)
    stat_grid = from_blocks(jnp.concatenate([log_totals, delta_rows], 2).transpose(0, 1, 3, 2))
    stat_halo = padded(stat_grid, (("gy", 1), ("gx", 0)), BSIDE)
    query_all = to_blocks(query_halo)
    stat_pad = to_blocks(stat_halo).transpose(0, 1, 3, 2)
    d_keys, d_values = key_grads(
        keyval_pad[1:-1, 1:-1],
        query_all[..., :model_width],
        query_all[..., model_width:],
        stat_pad[:, :, :HEADS],
        stat_pad[:, :, HEADS:],
        key_valid,
    )
    dq_flat = from_blocks(d_queries).reshape(-1, model_width)
    dk_flat = from_blocks(d_keys).reshape(-1, model_width)
    dv_flat = from_blocks(d_values).reshape(-1, model_width)
    grads_joined = jnp.concatenate([dq_flat, dk_flat, dv_flat], 1)
    w_stacked = jnp.concatenate([w_query.T, w_key.T, w_value.T], 0)
    grad_patches = jnp.dot(grads_joined, w_stacked, preferred_element_type=jnp.float32).astype(
        jnp.bfloat16
    )
    partials = (
        inner_rows(flat_in, dq_flat),
        inner_rows(flat_in, dk_flat),
        inner_rows(flat_in, dv_flat),
        grad_out_local,
    )
    summed = tree_sum(partials, ("gy", "gx"))
    return (
        layer_out.reshape(tile_rows, tile_cols, model_width),
        grad_patches.reshape(tile_rows, tile_cols, model_width),
        summed[0],
        summed[1],
        summed[2],
        summed[3],
    )


def solution(mesh):
    return jax.shard_map(
        on_device,
        mesh=mesh,
        in_specs=(
            P("gx", "gy", None),
            P(),
            P(),
            P(),
            P(),
            P("gx", "gy", None, None, None),
            P("gx", "gy", None, None),
            P("gx", "gy", None, None),
            P("gx", "gy", None),
        ),
        out_specs=(P("gx", "gy", None), P("gx", "gy", None), P(), P(), P(), P()),
        check_vma=False,
    )
```
